32 devices in a mesh: seq: 8 (over z, y), mp: 4 (over x, core).
Axes of the slice: x: 2, y: 2, z: 4, core: 2. Of those that a mesh axis runs over, the one named last changes fastest.
Arguments:
- queries: bfloat16 [64, 64, 4096], P('seq', None, 'mp'), may hold values from -5 to 5
- out_grad: bfloat16 [64, 64, 4096], P('seq', None, 'mp'), may hold values from -6 to 6
- row_keys: bfloat16 [64, 128, 4096], P('seq', None, 'mp'), may hold values from -5 to 5
- row_values: bfloat16 [64, 128, 4096], P('seq', None, 'mp'), may hold values from -6 to 6
- neighbours: int32 [64, 2], P(('seq', 'mp')), may hold values from 0 to 63, as said below
Outputs:
- query_grad: bfloat16 [64, 64, 4096], P('seq', None, 'mp')
- key_grad: bfloat16 [64, 128, 4096], P('seq', None, 'mp')
- value_grad: bfloat16 [64, 128, 4096], P('seq', None, 'mp')
The draws below stay inside these ranges and needn't reach their ends.
Inputs may be any that keep to these rules, and one draw needn't show every extreme that they name: Row r lies with seq index r // 8. The 2 neighbours of a span are different rows. The spans of one seq index retrieve at most 2 rows lying with any one seq index, and some seq indices are retrieved from that often by every seq index.
All inputs are finite; a program needn't handle non-finite values.
Results may differ from the reference program's by a relative error of at most 0.008.
Values may be sent and summed in bfloat16 or wider, within the bound.
No kernel may reach another device: no remote copies, remote signals or barrier semaphores. Data moves between devices by JAX's collectives and lax.ppermute only.
A program may use at most 320 MiB of HBM per device.

```python
import jax
import jax.numpy as jnp
from jax import lax

HEADS = 32
HEAD = 128
SPAN = 64
NLEN = 128
NBR = 2
CH_DEV = 8
ROWS_DEV = 8
OWNERS = 8
SLOT = 2
HOT = 2
SPANS = 64
ROWS = 64
WIDTH = 4096


def draw_queries(key, part):
    own_key = jax.random.fold_in(key, 11)
    return jax.random.truncated_normal(own_key, -5.0, 5.0, (SPANS, SPAN, HEADS * HEAD), jnp.float32).astype(jnp.bfloat16)


def draw_row_keys(key, part):
    own_key = jax.random.fold_in(key, 23)
    return jax.random.truncated_normal(own_key, -5.0, 5.0, (ROWS, NLEN, HEADS * HEAD), jnp.float32).astype(jnp.bfloat16)


def draw_neighbours(key, part):
    item_count = NBR * CH_DEV
    candidate_rows = OWNERS * SLOT
    own_key = jax.random.fold_in(key, 37)
    first_key, second_key, third_key, fourth_key = jax.random.split(own_key, 4)
    hot_order = jax.random.permutation(first_key, OWNERS)
    owner_rank = jnp.argsort(hot_order)
    popular_flag = owner_rank < HOT
    owning_holder = jnp.arange(candidate_rows) // SLOT
    baseline_level = jax.random.randint(second_key, (OWNERS, candidate_rows), 0, 2 ** 20)
    extra_reward = jnp.where(popular_flag[owning_holder], 2 ** 21, 0)
    ranking_score = (baseline_level + extra_reward[None, :]) * candidate_rows + jnp.arange(candidate_rows)[None, :]
    _, picked = lax.top_k(ranking_score, item_count)
    orders = jax.vmap(lambda sub_key: jax.random.permutation(sub_key, item_count))(jax.random.split(third_key, OWNERS))
    picked = jnp.take_along_axis(picked, orders, axis=1)
    owner_dev = picked // SLOT
    copy_index = picked % SLOT
    offsets = jax.random.randint(fourth_key, (OWNERS, OWNERS), 0, ROWS_DEV)
    local_row = (jnp.take_along_axis(offsets, owner_dev, axis=1) + copy_index) % ROWS_DEV
    chosen = owner_dev * ROWS_DEV + local_row
    return chosen.reshape(SPANS, NBR).astype(jnp.int32)


def levels(key, shape, pieces, smallest, top_value):
    level, own = 1.0, jax.random.fold_in(key, 6)
    for dim, parts in pieces:
        steps = jnp.exp(jax.random.uniform(jax.random.fold_in(own, dim), (parts,), jnp.float32, smallest / len(pieces), top_value / len(pieces)))
        level = level * jnp.repeat(steps, shape[dim] // parts).reshape([-1 if axis == dim else 1 for axis in range(len(shape))])
    return level


def gaussian(rng, dims, deviation, limit, cuts=(), held_as=jnp.bfloat16):
    factor_of = levels(rng, dims, cuts, -0.22, 0.18) if cuts else 1.0
    values = jax.random.normal(rng, dims, jnp.float32) * deviation * factor_of
    return jnp.minimum(jnp.maximum(values, -limit), limit).astype(held_as)


def setup_inputs(seed: int = 0) -> dict:
    keys = jax.random.split(jax.random.key(seed), 6)
    return {
        "queries": draw_queries(jax.random.fold_in(keys[5], 71), 0),
        "out_grad": gaussian(keys[1], (SPANS, SPAN, WIDTH), 1.0, 6.0, ((0, 8), (2, 4))),
        "row_keys": draw_row_keys(jax.random.fold_in(keys[5], 71), 0),
        "row_values": gaussian(keys[3], (ROWS, NLEN, WIDTH), 1.0, 6.0, ((0, 8), (2, 4))),
        "neighbours": draw_neighbours(jax.random.fold_in(keys[5], 71), 0),
    }


def span_terms(query_rows, gradient_rows, key_rows, value_rows):
    score_scale = HEAD ** -0.5
    query_f = query_rows.astype(jnp.float32).reshape(SPAN, HEADS, HEAD)
    grad_f = gradient_rows.astype(jnp.float32).reshape(SPAN, HEADS, HEAD)
    key_f = key_rows.astype(jnp.float32).reshape(NBR * NLEN, HEADS, HEAD)
    value_f = value_rows.astype(jnp.float32).reshape(NBR * NLEN, HEADS, HEAD)
    scores = jnp.einsum("ihd,jhd->hij", query_f, key_f) * score_scale
    highest = jnp.max(scores, axis=2, keepdims=True)
    log_total = highest + jnp.log(jnp.sum(jnp.exp(scores - highest), axis=2, keepdims=True))
    softmax_p = jnp.exp(scores - log_total)
    grad_p = jnp.einsum("ihd,jhd->hij", grad_f, value_f)
    row_delta = jnp.sum(softmax_p * grad_p, axis=2, keepdims=True)
    grad_low = (softmax_p * (grad_p - row_delta) * score_scale).astype(jnp.bfloat16)
    grad_s = lax.optimization_barrier(grad_low).astype(jnp.float32)
    probs_low = lax.optimization_barrier(softmax_p.astype(jnp.bfloat16)).astype(jnp.float32)
    value_part = jnp.einsum("hij,ihd->jhd", probs_low, grad_f).reshape(NBR, NLEN, HEADS * HEAD)
    key_part = jnp.einsum("hij,ihd->jhd", grad_s, query_f).reshape(NBR, NLEN, HEADS * HEAD)
    split_s = grad_s.reshape(HEADS, SPAN, NBR, NLEN)
    query_parts = jnp.einsum("hinj,njhd->nihd", split_s, key_f.reshape(NBR, NLEN, HEADS, HEAD))
    query_parts = lax.optimization_barrier(query_parts.astype(jnp.bfloat16)).astype(jnp.float32)
    query_part = jnp.sum(query_parts, axis=0).astype(jnp.bfloat16).reshape(SPAN, HEADS * HEAD)
    return query_part, key_part, value_part


def reference(queries, out_grad, row_keys, row_values, neighbours):
    def step(carry, inputs):
        key_acc, value_acc = carry
        query_rows, gradient_rows, picked = inputs
        picked = picked.astype(jnp.int32)
        key_rows = row_keys[picked].reshape(NBR * NLEN, HEADS * HEAD)
        value_rows = row_values[picked].reshape(NBR * NLEN, HEADS * HEAD)
        query_part, key_part, value_part = span_terms(query_rows, gradient_rows, key_rows, value_rows)
        key_acc = key_acc.at[picked].add(key_part)
        value_acc = value_acc.at[picked].add(value_part)
        return (key_acc, value_acc), query_part

    start = (jnp.zeros((ROWS, NLEN, HEADS * HEAD), jnp.float32), jnp.zeros((ROWS, NLEN, HEADS * HEAD), jnp.float32))
    (key_acc, value_acc), query_grad = lax.scan(step, start, (queries, out_grad, neighbours))
    return query_grad, key_acc.astype(jnp.bfloat16), value_acc.astype(jnp.bfloat16)
```

```python
import jax
import jax.numpy as jnp
from jax import lax
from jax.sharding import PartitionSpec as P

HEAD = 128
SPAN = 64
NLEN = 128
NBR = 2


def split_heads(tensor):
    return tensor.reshape(tensor.shape[:-1] + (tensor.shape[-1] // HEAD, HEAD))


def per_device(queries, out_grad, row_keys, row_values, neighbours):
    seq_count = lax.axis_size("seq")
    own_lists = lax.all_gather(neighbours, "mp", axis=0, tiled=True)
    span_count = queries.shape[0]
    rows_here = row_keys.shape[0]
    width_here = queries.shape[2]
    heads_here = width_here // HEAD
    flat_rows = own_lists.reshape(-1)
    item_count = flat_rows.shape[0]
    owner_dev = flat_rows // rows_here
    local_row = flat_rows % rows_here
    slot_depth = (item_count + seq_count - 1) // seq_count
    slot_total = seq_count * slot_depth
    position = jnp.arange(item_count)
    same_before = (owner_dev[:, None] == owner_dev[None, :]) & (
        position[None, :] < position[:, None]
    )
    earlier = jnp.sum(same_before.astype(jnp.int32), axis=1)
    target = owner_dev * slot_depth + earlier
    item_span = position // NBR
    score_scale = HEAD ** (-0.5)

    match = target[None, :] == jnp.arange(slot_total)[:, None]
    slot_valid = jnp.any(match, axis=1)
    slot_item = jnp.sum(jnp.where(match, position[None, :], 0), axis=1)
    slot_span = item_span[slot_item]

    both = jnp.stack([queries, out_grad], axis=1)
    pair_send = jnp.where(
        slot_valid[:, None, None, None], both[slot_span], jnp.zeros((), both.dtype)
    )
    row_send = jnp.where(slot_valid, local_row[slot_item], -1)
    pair_recv = lax.all_to_all(pair_send, "seq", split_axis=0, concat_axis=0, tiled=True)
    row_recv = lax.all_to_all(row_send, "seq", split_axis=0, concat_axis=0, tiled=True)

    recv_valid = row_recv >= 0
    row_index = jnp.clip(row_recv, 0, rows_here - 1)
    query_heads = split_heads(pair_recv[:, 0])
    grad_heads = split_heads(pair_recv[:, 1])
    key_heads = split_heads(row_keys[row_index])
    value_heads = split_heads(row_values[row_index])

    scores = (
        jnp.einsum("bihd,bjhd->bhij", query_heads, key_heads, preferred_element_type=jnp.float32)
        * score_scale
    )
    grad_p = jnp.einsum(
        "bihd,bjhd->bhij", grad_heads, value_heads, preferred_element_type=jnp.float32
    )
    highest = jnp.max(scores, axis=3)
    expons = jnp.exp(scores - highest[..., None])
    part = jnp.stack(
        [highest, jnp.sum(expons, axis=3), jnp.sum(expons * grad_p, axis=3)], axis=1
    ).reshape(slot_total, 3, heads_here * SPAN)
    back = lax.all_to_all(part, "seq", split_axis=0, concat_axis=0, tiled=True)

    item_part = back[target].reshape(span_count, NBR, 3, heads_here * SPAN)
    item_max = item_part[:, :, 0]
    item_sum = item_part[:, :, 1]
    item_cross = item_part[:, :, 2]
    span_max = jnp.max(item_max, axis=1, keepdims=True)
    factor = jnp.exp(item_max - span_max)
    span_sum = jnp.sum(item_sum * factor, axis=1)
    log_total = span_max[:, 0] + jnp.log(span_sum)
    row_delta = jnp.sum(item_cross * factor, axis=1) / span_sum
    span_stats = jnp.stack([log_total, row_delta], axis=1)
    stats_send = jnp.where(slot_valid[:, None, None], span_stats[slot_span], 0.0)
    stats_recv = lax.all_to_all(stats_send, "seq", split_axis=0, concat_axis=0, tiled=True)

    norm_here = stats_recv[:, 0].reshape(slot_total, heads_here, SPAN)
    delta_here = stats_recv[:, 1].reshape(slot_total, heads_here, SPAN)
    softmax_p = jnp.exp(scores - norm_here[..., None])
    grad_s = (softmax_p * (grad_p - delta_here[..., None]) * score_scale).astype(jnp.bfloat16)
    probs_low = softmax_p.astype(jnp.bfloat16)
    value_part = jnp.einsum(
        "bhij,bihd->bjhd", probs_low, grad_heads, preferred_element_type=jnp.float32
    ).reshape(slot_total, NLEN * width_here)
    key_part = jnp.einsum(
        "bhij,bihd->bjhd", grad_s, query_heads, preferred_element_type=jnp.float32
    ).reshape(slot_total, NLEN * width_here)
    query_part = jnp.einsum(
        "bhij,bjhd->bihd", grad_s, key_heads, preferred_element_type=jnp.float32
    ).astype(jnp.bfloat16).reshape(slot_total, SPAN, width_here)

    pick = (
        (row_recv[None, :] == jnp.arange(rows_here)[:, None]) & recv_valid[None, :]
    ).astype(jnp.float32)
    key_acc = jnp.dot(pick, key_part, precision=lax.Precision.HIGHEST)
    value_acc = jnp.dot(pick, value_part, precision=lax.Precision.HIGHEST)
    key_grad = key_acc.astype(jnp.bfloat16).reshape(rows_here, NLEN, width_here)
    value_grad = value_acc.astype(jnp.bfloat16).reshape(rows_here, NLEN, width_here)

    query_back = lax.all_to_all(query_part, "seq", split_axis=0, concat_axis=0, tiled=True)
    returned = query_back[target].reshape(span_count, NBR, SPAN, width_here).astype(jnp.float32)
    query_grad = jnp.sum(returned, axis=1).astype(jnp.bfloat16)
    return (query_grad, key_grad, value_grad)


def solution(mesh):
    in_specs = (
        P("seq", None, "mp"),
        P("seq", None, "mp"),
        P("seq", None, "mp"),
        P("seq", None, "mp"),
        P(("seq", "mp"), None),
    )
    out_specs = (P("seq", None, "mp"), P("seq", None, "mp"), P("seq", None, "mp"))
    return jax.shard_map(
        per_device, mesh=mesh, in_specs=in_specs, out_specs=out_specs, check_vma=False
    )
```

```python
import jax
import jax.numpy as jnp
from jax import lax
from jax.sharding import PartitionSpec as P

HEAD = 128
SPAN = 64
NLEN = 128
NBR = 2


def split_heads(tensor):
    return tensor.reshape(tensor.shape[:-1] + (tensor.shape[-1] // HEAD, HEAD))


def send_stage(queries, out_grad, slot_valid, slot_span):
    both = jnp.stack([queries, out_grad], axis=1)
    pair_send = jnp.where(
        slot_valid[:, None, None, None], both[slot_span], jnp.zeros((), both.dtype)
    )
    return lax.all_to_all(pair_send, "seq", split_axis=0, concat_axis=0, tiled=True)


def first_stage(pair_recv, row_keys, row_values, row_index):
    slot_total = pair_recv.shape[0]
    heads_chunk = pair_recv.shape[-1] // HEAD
    score_scale = HEAD ** (-0.5)
    query_heads = split_heads(pair_recv[:, 0])
    grad_heads = split_heads(pair_recv[:, 1])
    key_heads = split_heads(row_keys[row_index])
    value_heads = split_heads(row_values[row_index])
    scores = (
        jnp.einsum("bihd,bjhd->bhij", query_heads, key_heads, preferred_element_type=jnp.float32)
        * score_scale
    )
    grad_p = jnp.einsum(
        "bihd,bjhd->bhij", grad_heads, value_heads, preferred_element_type=jnp.float32
    )
    highest = jnp.max(scores, axis=3)
    expons = jnp.exp(scores - highest[..., None])
    part = jnp.stack(
        [highest, jnp.sum(expons, axis=3), jnp.sum(expons * grad_p, axis=3)], axis=1
    ).reshape(slot_total, 3, heads_chunk * SPAN)
    return part, (query_heads, grad_heads, key_heads, scores, grad_p)


def stats_stage(part, target, slot_valid, slot_span, span_count):
    back = lax.all_to_all(part, "seq", split_axis=0, concat_axis=0, tiled=True)
    item_part = back[target].reshape((span_count, NBR) + part.shape[1:])
    item_max = item_part[:, :, 0]
    item_sum = item_part[:, :, 1]
    item_cross = item_part[:, :, 2]
    span_max = jnp.max(item_max, axis=1, keepdims=True)
    factor = jnp.exp(item_max - span_max)
    span_sum = jnp.sum(item_sum * factor, axis=1)
    log_total = span_max[:, 0] + jnp.log(span_sum)
    row_delta = jnp.sum(item_cross * factor, axis=1) / span_sum
    span_stats = jnp.stack([log_total, row_delta], axis=1)
    stats_send = jnp.where(slot_valid[:, None, None], span_stats[slot_span], 0.0)
    return lax.all_to_all(stats_send, "seq", split_axis=0, concat_axis=0, tiled=True)


def second_stage(kept, stats_recv, pick):
    query_heads, grad_heads, key_heads, scores, grad_p = kept
    slot_total, heads_chunk, span_len = scores.shape[:3]
    width_chunk = heads_chunk * HEAD
    score_scale = HEAD ** (-0.5)
    norm_here = stats_recv[:, 0].reshape(slot_total, heads_chunk, span_len)
    delta_here = stats_recv[:, 1].reshape(slot_total, heads_chunk, span_len)
    softmax_p = jnp.exp(scores - norm_here[..., None])
    grad_s = (softmax_p * (grad_p - delta_here[..., None]) * score_scale).astype(jnp.bfloat16)
    probs_low = softmax_p.astype(jnp.bfloat16)
    value_part = jnp.einsum(
        "bhij,bihd->bjhd", probs_low, grad_heads, preferred_element_type=jnp.float32
    ).reshape(slot_total, NLEN * width_chunk)
    key_part = jnp.einsum(
        "bhij,bihd->bjhd", grad_s, query_heads, preferred_element_type=jnp.float32
    ).reshape(slot_total, NLEN * width_chunk)
    query_part = jnp.einsum(
        "bhij,bjhd->bihd", grad_s, key_heads, preferred_element_type=jnp.float32
    ).astype(jnp.bfloat16).reshape(slot_total, span_len, width_chunk)
    query_back = lax.all_to_all(query_part, "seq", split_axis=0, concat_axis=0, tiled=True)
    key_acc = jnp.dot(pick, key_part, precision=lax.Precision.HIGHEST)
    value_acc = jnp.dot(pick, value_part, precision=lax.Precision.HIGHEST)
    rows_here = pick.shape[0]
    key_grad = key_acc.astype(jnp.bfloat16).reshape(rows_here, NLEN, width_chunk)
    value_grad = value_acc.astype(jnp.bfloat16).reshape(rows_here, NLEN, width_chunk)
    return query_back, key_grad, value_grad


def per_device(queries, out_grad, row_keys, row_values, neighbours):
    seq_count = lax.axis_size("seq")
    own_lists = lax.all_gather(neighbours, "mp", axis=0, tiled=True)
    span_count = queries.shape[0]
    rows_here = row_keys.shape[0]
    width_here = queries.shape[2]
    heads_here = width_here // HEAD
    flat_rows = own_lists.reshape(-1)
    item_count = flat_rows.shape[0]
    owner_dev = flat_rows // rows_here
    local_row = flat_rows % rows_here
    slot_depth = (item_count + seq_count - 1) // seq_count
    slot_total = seq_count * slot_depth
    position = jnp.arange(item_count)
    same_before = (owner_dev[:, None] == owner_dev[None, :]) & (
        position[None, :] < position[:, None]
    )
    earlier = jnp.sum(same_before.astype(jnp.int32), axis=1)
    target = owner_dev * slot_depth + earlier
    item_span = position // NBR

    match = target[None, :] == jnp.arange(slot_total)[:, None]
    slot_valid = jnp.any(match, axis=1)
    slot_item = jnp.sum(jnp.where(match, position[None, :], 0), axis=1)
    slot_span = item_span[slot_item]

    row_send = jnp.where(slot_valid, local_row[slot_item], -1)
    row_recv = lax.all_to_all(row_send, "seq", split_axis=0, concat_axis=0, tiled=True)
    recv_valid = row_recv >= 0
    row_index = jnp.clip(row_recv, 0, rows_here - 1)
    pick = (
        (row_recv[None, :] == jnp.arange(rows_here)[:, None]) & recv_valid[None, :]
    ).astype(jnp.float32)

    chunk_count = 2 if heads_here % 2 == 0 else 1
    chunk_width = width_here // chunk_count
    col_sets = [slice(k * chunk_width, (k + 1) * chunk_width) for k in range(chunk_count)]
    received = [
        send_stage(queries[..., cols], out_grad[..., cols], slot_valid, slot_span)
        for cols in col_sets
    ]
    parts, kept = [], []
    for k, cols in enumerate(col_sets):
        part, held = first_stage(
            received[k], row_keys[..., cols], row_values[..., cols], row_index
        )
        if k + 1 < chunk_count:
            part, received[k + 1] = lax.optimization_barrier((part, received[k + 1]))
        parts.append(part)
        kept.append(held)
    stats = [stats_stage(p, target, slot_valid, slot_span, span_count) for p in parts]
    outs = [second_stage(kept[k], stats[k], pick) for k in range(chunk_count)]
    query_grads = []
    for query_back, _, _ in outs:
        returned = query_back[target].reshape((span_count, NBR) + query_back.shape[1:])
        query_grads.append(jnp.sum(returned.astype(jnp.float32), axis=1).astype(jnp.bfloat16))
    query_grad = jnp.concatenate(query_grads, axis=-1)
    key_grad = jnp.concatenate([o[1] for o in outs], axis=-1)
    value_grad = jnp.concatenate([o[2] for o in outs], axis=-1)
    return (query_grad, key_grad, value_grad)


def solution(mesh):
    in_specs = (
        P("seq", None, "mp"),
        P("seq", None, "mp"),
        P("seq", None, "mp"),
        P("seq", None, "mp"),
        P(("seq", "mp"), None),
    )
    out_specs = (P("seq", None, "mp"), P("seq", None, "mp"), P("seq", None, "mp"))
    return jax.shard_map(
        per_device, mesh=mesh, in_specs=in_specs, out_specs=out_specs, check_vma=False
    )
```

```python
import jax
import jax.numpy as jnp
from jax import lax
from jax.experimental import pallas as pl
from jax.experimental.pallas import tpu as pltpu
from jax.sharding import PartitionSpec as P

HEAD = 128
SPAN = 64
NLEN = 128
NBR = 2

TRANS_A = (((0,), (0,)), ((), ()))


def split_heads(tensor):
    return tensor.reshape(tensor.shape[:-1] + (tensor.shape[-1] // HEAD, HEAD))


def kv_kernel(rows_ref, probs_ref, grads_ref, pair_ref, key_out, value_out, key_acc, value_acc):
    slot = pl.program_id(0)
    heads = probs_ref.shape[1]

    @pl.when(slot == 0)
    def _():
        key_acc[...] = jnp.zeros_like(key_acc)
        value_acc[...] = jnp.zeros_like(value_acc)

    row = rows_ref[slot]

    @pl.when(row >= 0)
    def _():
        here = jnp.maximum(row, 0)
        for h in range(heads):
            cols = pl.ds(h * HEAD, HEAD)
            value_part = lax.dot_general(
                probs_ref[0, h], pair_ref[0, 1, :, cols], TRANS_A,
                preferred_element_type=jnp.float32,
            )
            key_part = lax.dot_general(
                grads_ref[0, h], pair_ref[0, 0, :, cols], TRANS_A,
                preferred_element_type=jnp.float32,
            )
            value_acc[here, :, cols] += value_part
            key_acc[here, :, cols] += key_part

    @pl.when(slot == pl.num_programs(0) - 1)
    def _():
        key_out[...] = key_acc[...].astype(key_out.dtype)
        value_out[...] = value_acc[...].astype(value_out.dtype)


def kv_grads(row_recv, probs_low, grad_s, pair_recv, rows_here):
    slot_total, heads, span_len, nlen = probs_low.shape
    width = pair_recv.shape[-1]
    out_shape = jax.ShapeDtypeStruct((rows_here, nlen, width), jnp.bfloat16)
    grid_spec = pltpu.PrefetchScalarGridSpec(
        num_scalar_prefetch=1,
        grid=(slot_total,),
        in_specs=[
            pl.BlockSpec((1, heads, span_len, nlen), lambda t, rows: (t, 0, 0, 0)),
            pl.BlockSpec((1, heads, span_len, nlen), lambda t, rows: (t, 0, 0, 0)),
            pl.BlockSpec((1, 2, span_len, width), lambda t, rows: (t, 0, 0, 0)),
        ],
        out_specs=[
            pl.BlockSpec((rows_here, nlen, width), lambda t, rows: (0, 0, 0)),
            pl.BlockSpec((rows_here, nlen, width), lambda t, rows: (0, 0, 0)),
        ],
        scratch_shapes=[
            pltpu.VMEM((rows_here, nlen, width), jnp.float32),
            pltpu.VMEM((rows_here, nlen, width), jnp.float32),
        ],
    )
    return pl.pallas_call(
        kv_kernel,
        grid_spec=grid_spec,
        out_shape=[out_shape, out_shape],
        compiler_params=pltpu.CompilerParams(
            dimension_semantics=("arbitrary",), vmem_limit_bytes=48 * 1024 * 1024
        ),
    )(row_recv, probs_low, grad_s, pair_recv)


def per_device(queries, out_grad, row_keys, row_values, neighbours):
    seq_count = lax.axis_size("seq")
    own_lists = lax.all_gather(neighbours, "mp", axis=0, tiled=True)
    span_count = queries.shape[0]
    rows_here = row_keys.shape[0]
    width_here = queries.shape[2]
    heads_here = width_here // HEAD
    flat_rows = own_lists.reshape(-1)
    item_count = flat_rows.shape[0]
    owner_dev = flat_rows // rows_here
    local_row = flat_rows % rows_here
    slot_depth = (item_count + seq_count - 1) // seq_count
    slot_total = seq_count * slot_depth
    position = jnp.arange(item_count)
    same_before = (owner_dev[:, None] == owner_dev[None, :]) & (
        position[None, :] < position[:, None]
    )
    earlier = jnp.sum(same_before.astype(jnp.int32), axis=1)
    target = owner_dev * slot_depth + earlier
    item_span = position // NBR
    score_scale = HEAD ** (-0.5)

    match = target[None, :] == jnp.arange(slot_total)[:, None]
    slot_valid = jnp.any(match, axis=1)
    slot_item = jnp.sum(jnp.where(match, position[None, :], 0), axis=1)
    slot_span = item_span[slot_item]

    pair_send = jnp.stack([queries[slot_span], out_grad[slot_span]], axis=1)
    row_send = jnp.where(slot_valid, local_row[slot_item], -1)
    pair_recv = lax.all_to_all(pair_send, "seq", split_axis=0, concat_axis=0, tiled=True)
    row_recv = lax.all_to_all(row_send, "seq", split_axis=0, concat_axis=0, tiled=True)

    row_index = jnp.clip(row_recv, 0, rows_here - 1)
    query_heads = split_heads(pair_recv[:, 0])
    grad_heads = split_heads(pair_recv[:, 1])
    key_heads = split_heads(row_keys[row_index])
    value_heads = split_heads(row_values[row_index])

    scores = (
        jnp.einsum("bihd,bjhd->bhij", query_heads, key_heads, preferred_element_type=jnp.float32)
        * score_scale
    )
    grad_p = jnp.einsum(
        "bihd,bjhd->bhij", grad_heads, value_heads, preferred_element_type=jnp.float32
    )
    highest = jnp.max(scores, axis=3)
    expons = jnp.exp(scores - highest[..., None])
    part = jnp.stack(
        [highest, jnp.sum(expons, axis=3), jnp.sum(expons * grad_p, axis=3)], axis=1
    ).reshape(slot_total, 3, heads_here * SPAN)
    back = lax.all_to_all(part, "seq", split_axis=0, concat_axis=0, tiled=True)

    item_part = back[target].reshape(span_count, NBR, 3, heads_here * SPAN)
    item_max = item_part[:, :, 0]
    item_sum = item_part[:, :, 1]
    item_cross = item_part[:, :, 2]
    span_max = jnp.max(item_max, axis=1, keepdims=True)
    factor = jnp.exp(item_max - span_max)
    span_sum = jnp.sum(item_sum * factor, axis=1)
    log_total = span_max[:, 0] + jnp.log(span_sum)
    row_delta = jnp.sum(item_cross * factor, axis=1) / span_sum
    span_stats = jnp.stack([log_total, row_delta], axis=1)
    stats_recv = lax.all_to_all(
        span_stats[slot_span], "seq", split_axis=0, concat_axis=0, tiled=True
    )

    norm_here = stats_recv[:, 0].reshape(slot_total, heads_here, SPAN)
    delta_here = stats_recv[:, 1].reshape(slot_total, heads_here, SPAN)
    softmax_p = jnp.exp(scores - norm_here[..., None])
    grad_s = (softmax_p * (grad_p - delta_here[..., None]) * score_scale).astype(jnp.bfloat16)
    probs_low = softmax_p.astype(jnp.bfloat16)
    query_part = jnp.einsum(
        "bhij,bjhd->bihd", grad_s, key_heads, preferred_element_type=jnp.float32
    ).astype(jnp.bfloat16).reshape(slot_total, SPAN, width_here)
    query_back = lax.all_to_all(query_part, "seq", split_axis=0, concat_axis=0, tiled=True)

    key_grad, value_grad = kv_grads(row_recv, probs_low, grad_s, pair_recv, rows_here)

    returned = query_back[target].reshape(span_count, NBR, SPAN, width_here).astype(jnp.float32)
    query_grad = jnp.sum(returned, axis=1).astype(jnp.bfloat16)
    return (query_grad, key_grad, value_grad)


def solution(mesh):
    in_specs = (
        P("seq", None, "mp"),
        P("seq", None, "mp"),
        P("seq", None, "mp"),
        P("seq", None, "mp"),
        P(("seq", "mp"), None),
    )
    out_specs = (P("seq", None, "mp"), P("seq", None, "mp"), P("seq", None, "mp"))
    return jax.shard_map(
        per_device, mesh=mesh, in_specs=in_specs, out_specs=out_specs, check_vma=False
    )
```

```python
import jax
import jax.numpy as jnp
from jax import lax
from jax.experimental import pallas as pl
from jax.experimental.pallas import tpu as pltpu
from jax.sharding import PartitionSpec as P

HEAD = 128
SPAN = 64
NLEN = 128
NBR = 2

TRANS_A = (((0,), (0,)), ((), ()))


def split_heads(tensor):
    return tensor.reshape(tensor.shape[:-1] + (tensor.shape[-1] // HEAD, HEAD))


def kv_kernel(rows_ref, probs_ref, grads_ref, pair_ref, key_out, value_out, key_acc, value_acc):
    slot = pl.program_id(0)
    heads = probs_ref.shape[1]

    @pl.when(slot == 0)
    def _():
        key_acc[...] = jnp.zeros_like(key_acc)
        value_acc[...] = jnp.zeros_like(value_acc)

    row = rows_ref[slot]

    @pl.when(row >= 0)
    def _():
        here = jnp.maximum(row, 0)
        for h in range(heads):
            cols = pl.ds(h * HEAD, HEAD)
            value_part = lax.dot_general(
                probs_ref[0, h], pair_ref[0, 1, :, cols], TRANS_A,
                preferred_element_type=jnp.float32,
            )
            key_part = lax.dot_general(
                grads_ref[0, h], pair_ref[0, 0, :, cols], TRANS_A,
                preferred_element_type=jnp.float32,
            )
            value_acc[here, :, cols] += value_part
            key_acc[here, :, cols] += key_part

    @pl.when(slot == pl.num_programs(0) - 1)
    def _():
        key_out[...] = key_acc[...].astype(key_out.dtype)
        value_out[...] = value_acc[...].astype(value_out.dtype)


def kv_grads(row_recv, probs_low, grad_s, pair_recv, rows_here):
    slot_total, heads, span_len, nlen = probs_low.shape
    width = pair_recv.shape[-1]
    out_shape = jax.ShapeDtypeStruct((rows_here, nlen, width), jnp.bfloat16)
    grid_spec = pltpu.PrefetchScalarGridSpec(
        num_scalar_prefetch=1,
        grid=(slot_total,),
        in_specs=[
            pl.BlockSpec((1, heads, span_len, nlen), lambda t, rows: (t, 0, 0, 0)),
            pl.BlockSpec((1, heads, span_len, nlen), lambda t, rows: (t, 0, 0, 0)),
            pl.BlockSpec((1, 2, span_len, width), lambda t, rows: (t, 0, 0, 0)),
        ],
        out_specs=[
            pl.BlockSpec((rows_here, nlen, width), lambda t, rows: (0, 0, 0)),
            pl.BlockSpec((rows_here, nlen, width), lambda t, rows: (0, 0, 0)),
        ],
        scratch_shapes=[
            pltpu.VMEM((rows_here, nlen, width), jnp.float32),
            pltpu.VMEM((rows_here, nlen, width), jnp.float32),
        ],
    )
    return pl.pallas_call(
        kv_kernel,
        grid_spec=grid_spec,
        out_shape=[out_shape, out_shape],
        compiler_params=pltpu.CompilerParams(
            dimension_semantics=("arbitrary",), vmem_limit_bytes=48 * 1024 * 1024
        ),
    )(row_recv, probs_low, grad_s, pair_recv)


def per_device(queries, out_grad, row_keys, row_values, neighbours):
    seq_count = lax.axis_size("seq")
    my_seq = lax.axis_index("seq")
    span_count = queries.shape[0]
    rows_here = row_keys.shape[0]
    width_here = queries.shape[2]
    heads_here = width_here // HEAD
    all_lists = lax.all_gather(neighbours, ("seq", "mp"), axis=0, tiled=True)
    lists = all_lists.reshape(seq_count, span_count * NBR)
    item_count = lists.shape[1]
    owner_all = lists // rows_here
    local_all = lists % rows_here
    slot_depth = (item_count + seq_count - 1) // seq_count
    slot_total = seq_count * slot_depth
    position = jnp.arange(item_count)
    same_before = (owner_all[:, :, None] == owner_all[:, None, :]) & (
        position[None, None, :] < position[None, :, None]
    )
    earlier_all = jnp.sum(same_before.astype(jnp.int32), axis=2)
    target_all = owner_all * slot_depth + earlier_all
    target = lax.dynamic_index_in_dim(target_all, my_seq, axis=0, keepdims=False)
    item_span = position // NBR
    score_scale = HEAD ** (-0.5)

    match = target[None, :] == jnp.arange(slot_total)[:, None]
    slot_item = jnp.sum(jnp.where(match, position[None, :], 0), axis=1)
    slot_span = item_span[slot_item]

    wanted = my_seq * slot_depth + jnp.arange(slot_depth)
    hit = target_all[:, None, :] == wanted[None, :, None]
    row_recv = jnp.where(
        jnp.any(hit, axis=2), jnp.sum(jnp.where(hit, local_all[:, None, :], 0), axis=2), -1
    ).reshape(slot_total)

    joined = jnp.concatenate([queries, out_grad], axis=1)
    pair_send = joined[slot_span].reshape(slot_total, 2, SPAN, width_here)
    pair_recv = lax.all_to_all(pair_send, "seq", split_axis=0, concat_axis=0, tiled=True)

    row_index = jnp.clip(row_recv, 0, rows_here - 1)
    query_heads = split_heads(pair_recv[:, 0])
    grad_heads = split_heads(pair_recv[:, 1])
    key_heads = split_heads(row_keys[row_index])
    value_heads = split_heads(row_values[row_index])

    scores = (
        jnp.einsum("bihd,bjhd->bhij", query_heads, key_heads, preferred_element_type=jnp.float32)
        * score_scale
    )
    grad_p = jnp.einsum(
        "bihd,bjhd->bhij", grad_heads, value_heads, preferred_element_type=jnp.float32
    )
    highest = jnp.max(scores, axis=3)
    expons = jnp.exp(scores - highest[..., None])
    part = jnp.stack(
        [highest, jnp.sum(expons, axis=3), jnp.sum(expons * grad_p, axis=3)], axis=1
    ).reshape(slot_total, 3, heads_here * SPAN)
    back = lax.all_to_all(part, "seq", split_axis=0, concat_axis=0, tiled=True)

    item_part = back[target].reshape(span_count, NBR, 3, heads_here * SPAN)
    item_max = item_part[:, :, 0]
    item_sum = item_part[:, :, 1]
    item_cross = item_part[:, :, 2]
    span_max = jnp.max(item_max, axis=1, keepdims=True)
    factor = jnp.exp(item_max - span_max)
    span_sum = jnp.sum(item_sum * factor, axis=1)
    log_total = span_max[:, 0] + jnp.log(span_sum)
    row_delta = jnp.sum(item_cross * factor, axis=1) / span_sum
    span_stats = jnp.stack([log_total, row_delta], axis=1)
    stats_recv = lax.all_to_all(
        span_stats[slot_span], "seq", split_axis=0, concat_axis=0, tiled=True
    )

    norm_here = stats_recv[:, 0].reshape(slot_total, heads_here, SPAN)
    delta_here = stats_recv[:, 1].reshape(slot_total, heads_here, SPAN)
    softmax_p = jnp.exp(scores - norm_here[..., None])
    grad_s = (softmax_p * (grad_p - delta_here[..., None]) * score_scale).astype(jnp.bfloat16)
    probs_low = softmax_p.astype(jnp.bfloat16)
    query_part = jnp.einsum(
        "bhij,bjhd->bihd", grad_s, key_heads, preferred_element_type=jnp.float32
    ).astype(jnp.bfloat16).reshape(slot_total, SPAN, width_here)
    query_back = lax.all_to_all(query_part, "seq", split_axis=0, concat_axis=0, tiled=True)

    key_grad, value_grad = kv_grads(row_recv, probs_low, grad_s, pair_recv, rows_here)

    returned = query_back[target].reshape(span_count, NBR, SPAN, width_here).astype(jnp.float32)
    query_grad = jnp.sum(returned, axis=1).astype(jnp.bfloat16)
    return (query_grad, key_grad, value_grad)


def solution(mesh):
    in_specs = (
        P("seq", None, "mp"),
        P("seq", None, "mp"),
        P("seq", None, "mp"),
        P("seq", None, "mp"),
        P(("seq", "mp"), None),
    )
    out_specs = (P("seq", None, "mp"), P("seq", None, "mp"), P("seq", None, "mp"))
    return jax.shard_map(
        per_device, mesh=mesh, in_specs=in_specs, out_specs=out_specs, check_vma=False
    )
```

```python
import jax
import jax.numpy as jnp
from jax import lax
from jax.experimental import pallas as pl
from jax.experimental.pallas import tpu as pltpu
from jax.sharding import PartitionSpec as P

HEAD = 128
SPAN = 64
NLEN = 128
NBR = 2

TRANS_A = (((0,), (0,)), ((), ()))


def split_heads(tensor):
    return tensor.reshape(tensor.shape[:-1] + (tensor.shape[-1] // HEAD, HEAD))


def kv_kernel(rows_ref, probs_ref, grads_ref, pair_ref, key_out, value_out, key_acc, value_acc):
    slot = pl.program_id(0)
    heads = probs_ref.shape[1]

    @pl.when(slot == 0)
    def _():
        key_acc[...] = jnp.zeros_like(key_acc)
        value_acc[...] = jnp.zeros_like(value_acc)

    row = rows_ref[slot]

    @pl.when(row >= 0)
    def _():
        here = jnp.maximum(row, 0)
        for h in range(heads):
            cols = pl.ds(h * HEAD, HEAD)
            value_part = lax.dot_general(
                probs_ref[0, h], pair_ref[0, 1, :, cols], TRANS_A,
                preferred_element_type=jnp.float32,
            )
            key_part = lax.dot_general(
                grads_ref[0, h], pair_ref[0, 0, :, cols], TRANS_A,
                preferred_element_type=jnp.float32,
            )
            value_acc[here, :, cols] += value_part
            key_acc[here, :, cols] += key_part

    @pl.when(slot == pl.num_programs(0) - 1)
    def _():
        key_out[...] = key_acc[...].astype(key_out.dtype)
        value_out[...] = value_acc[...].astype(value_out.dtype)


def kv_grads(row_recv, probs_low, grad_s, pair_recv, rows_here):
    slot_total, heads, span_len, nlen = probs_low.shape
    width = pair_recv.shape[-1]
    out_shape = jax.ShapeDtypeStruct((rows_here, nlen, width), jnp.bfloat16)
    grid_spec = pltpu.PrefetchScalarGridSpec(
        num_scalar_prefetch=1,
        grid=(slot_total,),
        in_specs=[
            pl.BlockSpec((1, heads, span_len, nlen), lambda t, rows: (t, 0, 0, 0)),
            pl.BlockSpec((1, heads, span_len, nlen), lambda t, rows: (t, 0, 0, 0)),
            pl.BlockSpec((1, 2, span_len, width), lambda t, rows: (t, 0, 0, 0)),
        ],
        out_specs=[
            pl.BlockSpec((rows_here, nlen, width), lambda t, rows: (0, 0, 0)),
            pl.BlockSpec((rows_here, nlen, width), lambda t, rows: (0, 0, 0)),
        ],
        scratch_shapes=[
            pltpu.VMEM((rows_here, nlen, width), jnp.float32),
            pltpu.VMEM((rows_here, nlen, width), jnp.float32),
        ],
    )
    return pl.pallas_call(
        kv_kernel,
        grid_spec=grid_spec,
        out_shape=[out_shape, out_shape],
        compiler_params=pltpu.CompilerParams(
            dimension_semantics=("arbitrary",), vmem_limit_bytes=48 * 1024 * 1024
        ),
    )(row_recv, probs_low, grad_s, pair_recv)


def per_device(queries, out_grad, row_keys, row_values, neighbours):
    seq_count = lax.axis_size("seq")
    own_lists = lax.all_gather(neighbours, "mp", axis=0, tiled=True)
    span_count = queries.shape[0]
    rows_here = row_keys.shape[0]
    width_here = queries.shape[2]
    heads_here = width_here // HEAD
    flat_rows = own_lists.reshape(-1)
    item_count = flat_rows.shape[0]
    owner_dev = flat_rows // rows_here
    local_row = flat_rows % rows_here
    slot_depth = (item_count + seq_count - 1) // seq_count
    slot_total = seq_count * slot_depth
    position = jnp.arange(item_count)
    same_before = (owner_dev[:, None] == owner_dev[None, :]) & (
        position[None, :] < position[:, None]
    )
    earlier = jnp.sum(same_before.astype(jnp.int32), axis=1)
    target = owner_dev * slot_depth + earlier
    item_span = position // NBR
    score_scale = HEAD ** (-0.5)

    match = target[None, :] == jnp.arange(slot_total)[:, None]
    slot_item = jnp.sum(jnp.where(match, position[None, :], 0), axis=1)
    slot_span = item_span[slot_item]

    joined = jnp.concatenate([queries, out_grad], axis=1)
    pair_send = joined[slot_span].reshape(slot_total, 2, SPAN, width_here)
    pair_recv = lax.all_to_all(pair_send, "seq", split_axis=0, concat_axis=0, tiled=True)

    my_seq = lax.axis_index("seq")
    lists = lax.all_gather(flat_rows, "seq", axis=0, tiled=False)
    owner_all = lists // rows_here
    local_all = lists % rows_here
    before_all = (owner_all[:, :, None] == owner_all[:, None, :]) & (
        position[None, None, :] < position[None, :, None]
    )
    target_all = owner_all * slot_depth + jnp.sum(before_all.astype(jnp.int32), axis=2)
    wanted = my_seq * slot_depth + jnp.arange(slot_depth)
    hit = target_all[:, None, :] == wanted[None, :, None]
    row_recv = jnp.where(
        jnp.any(hit, axis=2), jnp.sum(jnp.where(hit, local_all[:, None, :], 0), axis=2), -1
    ).reshape(slot_total)

    row_index = jnp.clip(row_recv, 0, rows_here - 1)
    query_heads = split_heads(pair_recv[:, 0])
    grad_heads = split_heads(pair_recv[:, 1])
    key_heads = split_heads(row_keys[row_index])
    value_heads = split_heads(row_values[row_index])

    scores = (
        jnp.einsum("bihd,bjhd->bhij", query_heads, key_heads, preferred_element_type=jnp.float32)
        * score_scale
    )
    grad_p = jnp.einsum(
        "bihd,bjhd->bhij", grad_heads, value_heads, preferred_element_type=jnp.float32
    )
    highest = jnp.max(scores, axis=3)
    expons = jnp.exp(scores - highest[..., None])
    part = jnp.stack(
        [highest, jnp.sum(expons, axis=3), jnp.sum(expons * grad_p, axis=3)], axis=1
    ).reshape(slot_total, 3, heads_here * SPAN)
    back = lax.all_to_all(part, "seq", split_axis=0, concat_axis=0, tiled=True)

    item_part = back[target].reshape(span_count, NBR, 3, heads_here * SPAN)
    item_max = item_part[:, :, 0]
    item_sum = item_part[:, :, 1]
    item_cross = item_part[:, :, 2]
    span_max = jnp.max(item_max, axis=1, keepdims=True)
    factor = jnp.exp(item_max - span_max)
    span_sum = jnp.sum(item_sum * factor, axis=1)
    log_total = span_max[:, 0] + jnp.log(span_sum)
    row_delta = jnp.sum(item_cross * factor, axis=1) / span_sum
    span_stats = jnp.stack([log_total, row_delta], axis=1)
    stats_recv = lax.all_to_all(
        span_stats[slot_span], "seq", split_axis=0, concat_axis=0, tiled=True
    )

    norm_here = stats_recv[:, 0].reshape(slot_total, heads_here, SPAN)
    delta_here = stats_recv[:, 1].reshape(slot_total, heads_here, SPAN)
    softmax_p = jnp.exp(scores - norm_here[..., None])
    grad_s = (softmax_p * (grad_p - delta_here[..., None]) * score_scale).astype(jnp.bfloat16)
    probs_low = softmax_p.astype(jnp.bfloat16)
    query_part = jnp.einsum(
        "bhij,bjhd->bihd", grad_s, key_heads, preferred_element_type=jnp.float32
    ).astype(jnp.bfloat16).reshape(slot_total, SPAN, width_here)
    query_back = lax.all_to_all(query_part, "seq", split_axis=0, concat_axis=0, tiled=True)

    key_grad, value_grad = kv_grads(row_recv, probs_low, grad_s, pair_recv, rows_here)

    returned = query_back[target].reshape(span_count, NBR, SPAN, width_here).astype(jnp.float32)
    query_grad = jnp.sum(returned, axis=1).astype(jnp.bfloat16)
    return (query_grad, key_grad, value_grad)


def solution(mesh):
    in_specs = (
        P("seq", None, "mp"),
        P("seq", None, "mp"),
        P("seq", None, "mp"),
        P("seq", None, "mp"),
        P(("seq", "mp"), None),
    )
    out_specs = (P("seq", None, "mp"), P("seq", None, "mp"), P("seq", None, "mp"))
    return jax.shard_map(
        per_device, mesh=mesh, in_specs=in_specs, out_specs=out_specs, check_vma=False
    )
```

```python
import jax
import jax.numpy as jnp
from jax import lax
from jax.experimental import pallas as pl
from jax.experimental.pallas import tpu as pltpu
from jax.sharding import PartitionSpec as P

HEAD = 128
SPAN = 64
NLEN = 128
NBR = 2

TRANS_A = (((0,), (0,)), ((), ()))


def split_heads(tensor):
    return tensor.reshape(tensor.shape[:-1] + (tensor.shape[-1] // HEAD, HEAD))


TRANS_B = (((1,), (1,)), ((), ()))


def stats_kernel(rows_ref, pair_ref, key_ref, value_ref, part_ref):
    heads = part_ref.shape[2]
    score_scale = HEAD ** (-0.5)
    for h in range(heads):
        cols = pl.ds(h * HEAD, HEAD)
        scores = lax.dot_general(
            key_ref[0, :, cols], pair_ref[0, 0, :, cols], TRANS_B,
            preferred_element_type=jnp.float32,
        ) * score_scale
        grad_p = lax.dot_general(
            value_ref[0, :, cols], pair_ref[0, 1, :, cols], TRANS_B,
            preferred_element_type=jnp.float32,
        )
        highest = jnp.max(scores, axis=0, keepdims=True)
        expons = jnp.exp(scores - highest)
        part_ref[0, 0, pl.ds(h, 1), :] = highest
        part_ref[0, 1, pl.ds(h, 1), :] = jnp.sum(expons, axis=0, keepdims=True)
        part_ref[0, 2, pl.ds(h, 1), :] = jnp.sum(expons * grad_p, axis=0, keepdims=True)


def grad_kernel(rows_ref, pair_ref, key_ref, value_ref, stats_ref, query_out, probs_out, grads_out):
    heads = stats_ref.shape[2]
    score_scale = HEAD ** (-0.5)
    for h in range(heads):
        cols = pl.ds(h * HEAD, HEAD)
        keys = key_ref[0, :, cols]
        scores = lax.dot_general(
            keys, pair_ref[0, 0, :, cols], TRANS_B, preferred_element_type=jnp.float32
        ) * score_scale
        grad_p = lax.dot_general(
            value_ref[0, :, cols], pair_ref[0, 1, :, cols], TRANS_B,
            preferred_element_type=jnp.float32,
        )
        softmax_p = jnp.exp(scores - stats_ref[0, 0, pl.ds(h, 1), :])
        grad_s = (softmax_p * (grad_p - stats_ref[0, 1, pl.ds(h, 1), :]) * score_scale).astype(
            jnp.bfloat16
        )
        probs_out[0, h] = softmax_p.astype(jnp.bfloat16)
        grads_out[0, h] = grad_s
        query_out[0, :, cols] = lax.dot_general(
            grad_s, keys, TRANS_A, preferred_element_type=jnp.float32
        ).astype(query_out.dtype)


def slot_specs(span_len, nlen, width):
    return [
        pl.BlockSpec((1, 2, span_len, width), lambda t, rows: (t, 0, 0, 0)),
        pl.BlockSpec((1, nlen, width), lambda t, rows: (rows[t], 0, 0)),
        pl.BlockSpec((1, nlen, width), lambda t, rows: (rows[t], 0, 0)),
    ]


def slot_stats(row_index, pair_recv, row_keys, row_values):
    slot_total, _, span_len, width = pair_recv.shape
    nlen = row_keys.shape[1]
    heads = width // HEAD
    grid_spec = pltpu.PrefetchScalarGridSpec(
        num_scalar_prefetch=1,
        grid=(slot_total,),
        in_specs=slot_specs(span_len, nlen, width),
        out_specs=pl.BlockSpec((1, 3, heads, span_len), lambda t, rows: (t, 0, 0, 0)),
    )
    return pl.pallas_call(
        stats_kernel,
        grid_spec=grid_spec,
        out_shape=jax.ShapeDtypeStruct((slot_total, 3, heads, span_len), jnp.float32),
        compiler_params=pltpu.CompilerParams(dimension_semantics=("arbitrary",)),
    )(row_index, pair_recv, row_keys, row_values)


def slot_grads(row_index, pair_recv, row_keys, row_values, stats_recv):
    slot_total, _, span_len, width = pair_recv.shape
    nlen = row_keys.shape[1]
    heads = width // HEAD
    grid_spec = pltpu.PrefetchScalarGridSpec(
        num_scalar_prefetch=1,
        grid=(slot_total,),
        in_specs=slot_specs(span_len, nlen, width)
        + [pl.BlockSpec((1, 2, heads, span_len), lambda t, rows: (t, 0, 0, 0))],
        out_specs=[
            pl.BlockSpec((1, span_len, width), lambda t, rows: (t, 0, 0)),
            pl.BlockSpec((1, heads, nlen, span_len), lambda t, rows: (t, 0, 0, 0)),
            pl.BlockSpec((1, heads, nlen, span_len), lambda t, rows: (t, 0, 0, 0)),
        ],
    )
    return pl.pallas_call(
        grad_kernel,
        grid_spec=grid_spec,
        out_shape=[
            jax.ShapeDtypeStruct((slot_total, span_len, width), jnp.bfloat16),
            jax.ShapeDtypeStruct((slot_total, heads, nlen, span_len), jnp.bfloat16),
            jax.ShapeDtypeStruct((slot_total, heads, nlen, span_len), jnp.bfloat16),
        ],
        compiler_params=pltpu.CompilerParams(dimension_semantics=("arbitrary",)),
    )(row_index, pair_recv, row_keys, row_values, stats_recv)


def kv_kernel(rows_ref, probs_ref, grads_ref, pair_ref, key_out, value_out, key_acc, value_acc):
    slot = pl.program_id(0)
    heads = probs_ref.shape[1]

    @pl.when(slot == 0)
    def _():
        key_acc[...] = jnp.zeros_like(key_acc)
        value_acc[...] = jnp.zeros_like(value_acc)

    row = rows_ref[slot]

    @pl.when(row >= 0)
    def _():
        here = jnp.maximum(row, 0)
        for h in range(heads):
            cols = pl.ds(h * HEAD, HEAD)
            value_part = jnp.dot(
                probs_ref[0, h], pair_ref[0, 1, :, cols], preferred_element_type=jnp.float32
            )
            key_part = jnp.dot(
                grads_ref[0, h], pair_ref[0, 0, :, cols], preferred_element_type=jnp.float32
            )
            value_acc[here, :, cols] += value_part
            key_acc[here, :, cols] += key_part

    @pl.when(slot == pl.num_programs(0) - 1)
    def _():
        key_out[...] = key_acc[...].astype(key_out.dtype)
        value_out[...] = value_acc[...].astype(value_out.dtype)


def kv_grads(row_recv, probs_low, grad_s, pair_recv, rows_here):
    slot_total, heads, nlen, span_len = probs_low.shape
    width = pair_recv.shape[-1]
    out_shape = jax.ShapeDtypeStruct((rows_here, nlen, width), jnp.bfloat16)
    grid_spec = pltpu.PrefetchScalarGridSpec(
        num_scalar_prefetch=1,
        grid=(slot_total,),
        in_specs=[
            pl.BlockSpec((1, heads, nlen, span_len), lambda t, rows: (t, 0, 0, 0)),
            pl.BlockSpec((1, heads, nlen, span_len), lambda t, rows: (t, 0, 0, 0)),
            pl.BlockSpec((1, 2, span_len, width), lambda t, rows: (t, 0, 0, 0)),
        ],
        out_specs=[
            pl.BlockSpec((rows_here, nlen, width), lambda t, rows: (0, 0, 0)),
            pl.BlockSpec((rows_here, nlen, width), lambda t, rows: (0, 0, 0)),
        ],
        scratch_shapes=[
            pltpu.VMEM((rows_here, nlen, width), jnp.float32),
            pltpu.VMEM((rows_here, nlen, width), jnp.float32),
        ],
    )
    return pl.pallas_call(
        kv_kernel,
        grid_spec=grid_spec,
        out_shape=[out_shape, out_shape],
        compiler_params=pltpu.CompilerParams(
            dimension_semantics=("arbitrary",), vmem_limit_bytes=48 * 1024 * 1024
        ),
    )(row_recv, probs_low, grad_s, pair_recv)


def per_device(queries, out_grad, row_keys, row_values, neighbours):
    seq_count = lax.axis_size("seq")
    own_lists = lax.all_gather(neighbours, "mp", axis=0, tiled=True)
    span_count = queries.shape[0]
    rows_here = row_keys.shape[0]
    width_here = queries.shape[2]
    heads_here = width_here // HEAD
    flat_rows = own_lists.reshape(-1)
    item_count = flat_rows.shape[0]
    owner_dev = flat_rows // rows_here
    local_row = flat_rows % rows_here
    slot_depth = (item_count + seq_count - 1) // seq_count
    slot_total = seq_count * slot_depth
    position = jnp.arange(item_count)
    same_before = (owner_dev[:, None] == owner_dev[None, :]) & (
        position[None, :] < position[:, None]
    )
    earlier = jnp.sum(same_before.astype(jnp.int32), axis=1)
    target = owner_dev * slot_depth + earlier
    item_span = position // NBR
    score_scale = HEAD ** (-0.5)

    match = target[None, :] == jnp.arange(slot_total)[:, None]
    slot_item = jnp.sum(jnp.where(match, position[None, :], 0), axis=1)
    slot_span = item_span[slot_item]

    joined = jnp.concatenate([queries, out_grad], axis=1)
    pair_send = joined[slot_span].reshape(slot_total, 2, SPAN, width_here)
    pair_recv = lax.all_to_all(pair_send, "seq", split_axis=0, concat_axis=0, tiled=True)

    my_seq = lax.axis_index("seq")
    lists = lax.all_gather(flat_rows, "seq", axis=0, tiled=False)
    owner_all = lists // rows_here
    local_all = lists % rows_here
    before_all = (owner_all[:, :, None] == owner_all[:, None, :]) & (
        position[None, None, :] < position[None, :, None]
    )
    target_all = owner_all * slot_depth + jnp.sum(before_all.astype(jnp.int32), axis=2)
    wanted = my_seq * slot_depth + jnp.arange(slot_depth)
    hit = target_all[:, None, :] == wanted[None, :, None]
    row_recv = jnp.where(
        jnp.any(hit, axis=2), jnp.sum(jnp.where(hit, local_all[:, None, :], 0), axis=2), -1
    ).reshape(slot_total)

    row_index = jnp.clip(row_recv, 0, rows_here - 1)
    part = slot_stats(row_index, pair_recv, row_keys, row_values).reshape(
        slot_total, 3, heads_here * SPAN
    )
    back = lax.all_to_all(part, "seq", split_axis=0, concat_axis=0, tiled=True)

    item_part = back[target].reshape(span_count, NBR, 3, heads_here * SPAN)
    item_max = item_part[:, :, 0]
    item_sum = item_part[:, :, 1]
    item_cross = item_part[:, :, 2]
    span_max = jnp.max(item_max, axis=1, keepdims=True)
    factor = jnp.exp(item_max - span_max)
    span_sum = jnp.sum(item_sum * factor, axis=1)
    log_total = span_max[:, 0] + jnp.log(span_sum)
    row_delta = jnp.sum(item_cross * factor, axis=1) / span_sum
    span_stats = jnp.stack([log_total, row_delta], axis=1)
    stats_recv = lax.all_to_all(
        span_stats[slot_span], "seq", split_axis=0, concat_axis=0, tiled=True
    )

    query_part, probs_low, grad_s = slot_grads(
        row_index, pair_recv, row_keys, row_values,
        stats_recv.reshape(slot_total, 2, heads_here, SPAN),
    )
    query_back = lax.all_to_all(query_part, "seq", split_axis=0, concat_axis=0, tiled=True)

    key_grad, value_grad = kv_grads(row_recv, probs_low, grad_s, pair_recv, rows_here)

    returned = query_back[target].reshape(span_count, NBR, SPAN, width_here).astype(jnp.float32)
    query_grad = jnp.sum(returned, axis=1).astype(jnp.bfloat16)
    return (query_grad, key_grad, value_grad)


def solution(mesh):
    in_specs = (
        P("seq", None, "mp"),
        P("seq", None, "mp"),
        P("seq", None, "mp"),
        P("seq", None, "mp"),
        P(("seq", "mp"), None),
    )
    out_specs = (P("seq", None, "mp"), P("seq", None, "mp"), P("seq", None, "mp"))
    return jax.shard_map(
        per_device, mesh=mesh, in_specs=in_specs, out_specs=out_specs, check_vma=False
    )
```

```python
import jax
import jax.numpy as jnp
from jax import lax
from jax.experimental import pallas as pl
from jax.experimental.pallas import tpu as pltpu
from jax.sharding import PartitionSpec as P

HEAD = 128
SPAN = 64
NLEN = 128
NBR = 2

TRANS_A = (((0,), (0,)), ((), ()))


def split_heads(tensor):
    return tensor.reshape(tensor.shape[:-1] + (tensor.shape[-1] // HEAD, HEAD))


TRANS_B = (((1,), (1,)), ((), ()))


def stats_kernel(rows_ref, pair_ref, key_ref, value_ref, part_ref):
    heads = part_ref.shape[2]
    score_scale = HEAD ** (-0.5)
    for h in range(heads):
        cols = pl.ds(h * HEAD, HEAD)
        scores = lax.dot_general(
            key_ref[0, :, cols], pair_ref[0, 0, :, cols], TRANS_B,
            preferred_element_type=jnp.float32,
        ) * score_scale
        grad_p = lax.dot_general(
            value_ref[0, :, cols], pair_ref[0, 1, :, cols], TRANS_B,
            preferred_element_type=jnp.float32,
        )
        highest = jnp.max(scores, axis=0, keepdims=True)
        expons = jnp.exp(scores - highest)
        total = jnp.sum(expons, axis=0, keepdims=True)
        part_ref[0, 0, pl.ds(h, 1), :] = highest + jnp.log(total)
        part_ref[0, 1, pl.ds(h, 1), :] = jnp.sum(expons * grad_p, axis=0, keepdims=True) / total


def grad_kernel(rows_ref, pair_ref, key_ref, value_ref, stats_ref, query_out, probs_out, grads_out):
    heads = stats_ref.shape[2]
    score_scale = HEAD ** (-0.5)
    for h in range(heads):
        cols = pl.ds(h * HEAD, HEAD)
        keys = key_ref[0, :, cols]
        scores = lax.dot_general(
            keys, pair_ref[0, 0, :, cols], TRANS_B, preferred_element_type=jnp.float32
        ) * score_scale
        grad_p = lax.dot_general(
            value_ref[0, :, cols], pair_ref[0, 1, :, cols], TRANS_B,
            preferred_element_type=jnp.float32,
        )
        softmax_p = jnp.exp(scores - stats_ref[0, 0, pl.ds(h, 1), :])
        grad_s = (softmax_p * (grad_p - stats_ref[0, 1, pl.ds(h, 1), :]) * score_scale).astype(
            jnp.bfloat16
        )
        probs_out[0, h] = softmax_p.astype(jnp.bfloat16)
        grads_out[0, h] = grad_s
        query_out[0, :, cols] = lax.dot_general(
            grad_s, keys, TRANS_A, preferred_element_type=jnp.float32
        ).astype(query_out.dtype)


def slot_specs(span_len, nlen, width):
    return [
        pl.BlockSpec((1, 2, span_len, width), lambda t, rows: (t, 0, 0, 0)),
        pl.BlockSpec((1, nlen, width), lambda t, rows: (rows[t], 0, 0)),
        pl.BlockSpec((1, nlen, width), lambda t, rows: (rows[t], 0, 0)),
    ]


def slot_stats(row_index, pair_recv, row_keys, row_values):
    slot_total, _, span_len, width = pair_recv.shape
    nlen = row_keys.shape[1]
    heads = width // HEAD
    grid_spec = pltpu.PrefetchScalarGridSpec(
        num_scalar_prefetch=1,
        grid=(slot_total,),
        in_specs=slot_specs(span_len, nlen, width),
        out_specs=pl.BlockSpec((1, 2, heads, span_len), lambda t, rows: (t, 0, 0, 0)),
    )
    return pl.pallas_call(
        stats_kernel,
        grid_spec=grid_spec,
        out_shape=jax.ShapeDtypeStruct((slot_total, 2, heads, span_len), jnp.float32),
        compiler_params=pltpu.CompilerParams(dimension_semantics=("arbitrary",)),
    )(row_index, pair_recv, row_keys, row_values)


def slot_grads(row_index, pair_recv, row_keys, row_values, stats_recv):
    slot_total, _, span_len, width = pair_recv.shape
    nlen = row_keys.shape[1]
    heads = width // HEAD
    grid_spec = pltpu.PrefetchScalarGridSpec(
        num_scalar_prefetch=1,
        grid=(slot_total,),
        in_specs=slot_specs(span_len, nlen, width)
        + [pl.BlockSpec((1, 2, heads, span_len), lambda t, rows: (t, 0, 0, 0))],
        out_specs=[
            pl.BlockSpec((1, span_len, width), lambda t, rows: (t, 0, 0)),
            pl.BlockSpec((1, heads, nlen, span_len), lambda t, rows: (t, 0, 0, 0)),
            pl.BlockSpec((1, heads, nlen, span_len), lambda t, rows: (t, 0, 0, 0)),
        ],
    )
    return pl.pallas_call(
        grad_kernel,
        grid_spec=grid_spec,
        out_shape=[
            jax.ShapeDtypeStruct((slot_total, span_len, width), jnp.bfloat16),
            jax.ShapeDtypeStruct((slot_total, heads, nlen, span_len), jnp.bfloat16),
            jax.ShapeDtypeStruct((slot_total, heads, nlen, span_len), jnp.bfloat16),
        ],
        compiler_params=pltpu.CompilerParams(dimension_semantics=("arbitrary",)),
    )(row_index, pair_recv, row_keys, row_values, stats_recv)


def kv_kernel(rows_ref, probs_ref, grads_ref, pair_ref, key_out, value_out, key_acc, value_acc):
    slot = pl.program_id(0)
    heads = probs_ref.shape[1]

    @pl.when(slot == 0)
    def _():
        key_acc[...] = jnp.zeros_like(key_acc)
        value_acc[...] = jnp.zeros_like(value_acc)

    row = rows_ref[slot]

    @pl.when(row >= 0)
    def _():
        here = jnp.maximum(row, 0)
        for h in range(heads):
            cols = pl.ds(h * HEAD, HEAD)
            value_part = jnp.dot(
                probs_ref[0, h], pair_ref[0, 1, :, cols], preferred_element_type=jnp.float32
            )
            key_part = jnp.dot(
                grads_ref[0, h], pair_ref[0, 0, :, cols], preferred_element_type=jnp.float32
            )
            value_acc[here, :, cols] += value_part
            key_acc[here, :, cols] += key_part

    @pl.when(slot == pl.num_programs(0) - 1)
    def _():
        key_out[...] = key_acc[...].astype(key_out.dtype)
        value_out[...] = value_acc[...].astype(value_out.dtype)


def kv_grads(row_recv, probs_low, grad_s, pair_recv, rows_here):
    slot_total, heads, nlen, span_len = probs_low.shape
    width = pair_recv.shape[-1]
    out_shape = jax.ShapeDtypeStruct((rows_here, nlen, width), jnp.bfloat16)
    grid_spec = pltpu.PrefetchScalarGridSpec(
        num_scalar_prefetch=1,
        grid=(slot_total,),
        in_specs=[
            pl.BlockSpec((1, heads, nlen, span_len), lambda t, rows: (t, 0, 0, 0)),
            pl.BlockSpec((1, heads, nlen, span_len), lambda t, rows: (t, 0, 0, 0)),
            pl.BlockSpec((1, 2, span_len, width), lambda t, rows: (t, 0, 0, 0)),
        ],
        out_specs=[
            pl.BlockSpec((rows_here, nlen, width), lambda t, rows: (0, 0, 0)),
            pl.BlockSpec((rows_here, nlen, width), lambda t, rows: (0, 0, 0)),
        ],
        scratch_shapes=[
            pltpu.VMEM((rows_here, nlen, width), jnp.float32),
            pltpu.VMEM((rows_here, nlen, width), jnp.float32),
        ],
    )
    return pl.pallas_call(
        kv_kernel,
        grid_spec=grid_spec,
        out_shape=[out_shape, out_shape],
        compiler_params=pltpu.CompilerParams(
            dimension_semantics=("arbitrary",), vmem_limit_bytes=48 * 1024 * 1024
        ),
    )(row_recv, probs_low, grad_s, pair_recv)


def per_device(queries, out_grad, row_keys, row_values, neighbours):
    seq_count = lax.axis_size("seq")
    own_lists = lax.all_gather(neighbours, "mp", axis=0, tiled=True)
    span_count = queries.shape[0]
    rows_here = row_keys.shape[0]
    width_here = queries.shape[2]
    heads_here = width_here // HEAD
    flat_rows = own_lists.reshape(-1)
    item_count = flat_rows.shape[0]
    owner_dev = flat_rows // rows_here
    local_row = flat_rows % rows_here
    slot_depth = (item_count + seq_count - 1) // seq_count
    slot_total = seq_count * slot_depth
    position = jnp.arange(item_count)
    same_before = (owner_dev[:, None] == owner_dev[None, :]) & (
        position[None, :] < position[:, None]
    )
    earlier = jnp.sum(same_before.astype(jnp.int32), axis=1)
    target = owner_dev * slot_depth + earlier
    item_span = position // NBR
    score_scale = HEAD ** (-0.5)

    match = target[None, :] == jnp.arange(slot_total)[:, None]
    slot_item = jnp.sum(jnp.where(match, position[None, :], 0), axis=1)
    slot_span = item_span[slot_item]

    joined = jnp.concatenate([queries, out_grad], axis=1)
    pair_send = joined[slot_span].reshape(slot_total, 2, SPAN, width_here)
    pair_recv = lax.all_to_all(pair_send, "seq", split_axis=0, concat_axis=0, tiled=True)

    my_seq = lax.axis_index("seq")
    lists = lax.all_gather(flat_rows, "seq", axis=0, tiled=False)
    owner_all = lists // rows_here
    local_all = lists % rows_here
    before_all = (owner_all[:, :, None] == owner_all[:, None, :]) & (
        position[None, None, :] < position[None, :, None]
    )
    target_all = owner_all * slot_depth + jnp.sum(before_all.astype(jnp.int32), axis=2)
    wanted = my_seq * slot_depth + jnp.arange(slot_depth)
    hit = target_all[:, None, :] == wanted[None, :, None]
    row_recv = jnp.where(
        jnp.any(hit, axis=2), jnp.sum(jnp.where(hit, local_all[:, None, :], 0), axis=2), -1
    ).reshape(slot_total)

    row_index = jnp.clip(row_recv, 0, rows_here - 1)
    part = slot_stats(row_index, pair_recv, row_keys, row_values)
    every_part = lax.all_gather(part, "seq", axis=0, tiled=True)

    sender = jnp.arange(slot_total) // slot_depth
    item_here = jnp.sum(jnp.where(hit, position[None, None, :], 0), axis=2).reshape(slot_total)
    partner = item_here + 1 - 2 * (item_here % NBR)
    partner_owner = owner_all[sender, partner]
    partner_slot = sender * slot_depth + target_all[sender, partner] - partner_owner * slot_depth
    other = every_part[partner_owner * slot_total + partner_slot]
    own_total, other_total = part[:, 0], other[:, 0]
    top = jnp.maximum(own_total, other_total)
    log_total = top + jnp.log(jnp.exp(own_total - top) + jnp.exp(other_total - top))
    row_delta = (
        jnp.exp(own_total - log_total) * part[:, 1] + jnp.exp(other_total - log_total) * other[:, 1]
    )
    stats_recv = jnp.stack([log_total, row_delta], axis=1)

    query_part, probs_low, grad_s = slot_grads(
        row_index, pair_recv, row_keys, row_values,
        stats_recv,
    )
    query_back = lax.all_to_all(query_part, "seq", split_axis=0, concat_axis=0, tiled=True)

    key_grad, value_grad = kv_grads(row_recv, probs_low, grad_s, pair_recv, rows_here)

    returned = query_back[target].reshape(span_count, NBR, SPAN, width_here).astype(jnp.float32)
    query_grad = jnp.sum(returned, axis=1).astype(jnp.bfloat16)
    return (query_grad, key_grad, value_grad)


def solution(mesh):
    in_specs = (
        P("seq", None, "mp"),
        P("seq", None, "mp"),
        P("seq", None, "mp"),
        P("seq", None, "mp"),
        P(("seq", "mp"), None),
    )
    out_specs = (P("seq", None, "mp"), P("seq", None, "mp"), P("seq", None, "mp"))
    return jax.shard_map(
        per_device, mesh=mesh, in_specs=in_specs, out_specs=out_specs, check_vma=False
    )
```

```python
import jax
import jax.numpy as jnp
from jax import lax
from jax.experimental import pallas as pl
from jax.experimental.pallas import tpu as pltpu
from jax.sharding import PartitionSpec as P

HEAD = 128
SPAN = 64
NLEN = 128
NBR = 2

TRANS_A = (((0,), (0,)), ((), ()))


def split_heads(tensor):
    return tensor.reshape(tensor.shape[:-1] + (tensor.shape[-1] // HEAD, HEAD))


TRANS_B = (((1,), (1,)), ((), ()))


def stats_kernel(rows_ref, pair_ref, key_ref, value_ref, part_ref):
    heads = part_ref.shape[2]
    score_scale = HEAD ** (-0.5)
    for h in range(heads):
        cols = pl.ds(h * HEAD, HEAD)
        scores = lax.dot_general(
            key_ref[0, :, cols], pair_ref[0, 0, :, cols], TRANS_B,
            preferred_element_type=jnp.float32,
        ) * score_scale
        grad_p = lax.dot_general(
            value_ref[0, :, cols], pair_ref[0, 1, :, cols], TRANS_B,
            preferred_element_type=jnp.float32,
        )
        highest = jnp.max(scores, axis=0, keepdims=True)
        expons = jnp.exp(scores - highest)
        part_ref[0, 0, pl.ds(h, 1), :] = highest
        part_ref[0, 1, pl.ds(h, 1), :] = jnp.sum(expons, axis=0, keepdims=True)
        part_ref[0, 2, pl.ds(h, 1), :] = jnp.sum(expons * grad_p, axis=0, keepdims=True)


def grad_kernel(rows_ref, pair_ref, key_ref, value_ref, stats_ref, query_out):
    heads = stats_ref.shape[2]
    score_scale = HEAD ** (-0.5)
    for h in range(heads):
        cols = pl.ds(h * HEAD, HEAD)
        keys = key_ref[0, :, cols]
        scores = lax.dot_general(
            keys, pair_ref[0, 0, :, cols], TRANS_B, preferred_element_type=jnp.float32
        ) * score_scale
        grad_p = lax.dot_general(
            value_ref[0, :, cols], pair_ref[0, 1, :, cols], TRANS_B,
            preferred_element_type=jnp.float32,
        )
        softmax_p = jnp.exp(scores - stats_ref[0, 0, pl.ds(h, 1), :])
        grad_s = (softmax_p * (grad_p - stats_ref[0, 1, pl.ds(h, 1), :]) * score_scale).astype(
            jnp.bfloat16
        )
        query_out[0, :, cols] = lax.dot_general(
            grad_s, keys, TRANS_A, preferred_element_type=jnp.float32
        ).astype(query_out.dtype)


def slot_specs(span_len, nlen, width):
    return [
        pl.BlockSpec((1, 2, span_len, width), lambda t, rows: (t, 0, 0, 0)),
        pl.BlockSpec((1, nlen, width), lambda t, rows: (rows[t], 0, 0)),
        pl.BlockSpec((1, nlen, width), lambda t, rows: (rows[t], 0, 0)),
    ]


def slot_stats(row_index, pair_recv, row_keys, row_values):
    slot_total, _, span_len, width = pair_recv.shape
    nlen = row_keys.shape[1]
    heads = width // HEAD
    grid_spec = pltpu.PrefetchScalarGridSpec(
        num_scalar_prefetch=1,
        grid=(slot_total,),
        in_specs=slot_specs(span_len, nlen, width),
        out_specs=pl.BlockSpec((1, 3, heads, span_len), lambda t, rows: (t, 0, 0, 0)),
    )
    return pl.pallas_call(
        stats_kernel,
        grid_spec=grid_spec,
        out_shape=jax.ShapeDtypeStruct((slot_total, 3, heads, span_len), jnp.float32),
        compiler_params=pltpu.CompilerParams(dimension_semantics=("arbitrary",)),
    )(row_index, pair_recv, row_keys, row_values)


def slot_grads(row_index, pair_recv, row_keys, row_values, stats_recv):
    slot_total, _, span_len, width = pair_recv.shape
    nlen = row_keys.shape[1]
    heads = width // HEAD
    grid_spec = pltpu.PrefetchScalarGridSpec(
        num_scalar_prefetch=1,
        grid=(slot_total,),
        in_specs=slot_specs(span_len, nlen, width)
        + [pl.BlockSpec((1, 2, heads, span_len), lambda t, rows: (t, 0, 0, 0))],
        out_specs=pl.BlockSpec((1, span_len, width), lambda t, rows: (t, 0, 0)),
    )
    return pl.pallas_call(
        grad_kernel,
        grid_spec=grid_spec,
        out_shape=jax.ShapeDtypeStruct((slot_total, span_len, width), jnp.bfloat16),
        compiler_params=pltpu.CompilerParams(dimension_semantics=("arbitrary",)),
    )(row_index, pair_recv, row_keys, row_values, stats_recv)


def kv_kernel(rows_ref, pair_ref, key_ref, value_ref, stats_ref, key_out, value_out, key_acc, value_acc):
    slot = pl.program_id(0)
    heads = stats_ref.shape[2]
    score_scale = HEAD ** (-0.5)

    @pl.when(slot == 0)
    def _():
        key_acc[...] = jnp.zeros_like(key_acc)
        value_acc[...] = jnp.zeros_like(value_acc)

    row = rows_ref[slot]

    @pl.when(row >= 0)
    def _():
        here = jnp.maximum(row, 0)
        for h in range(heads):
            cols = pl.ds(h * HEAD, HEAD)
            query_rows = pair_ref[0, 0, :, cols]
            grad_rows = pair_ref[0, 1, :, cols]
            scores = lax.dot_general(
                key_ref[0, :, cols], query_rows, TRANS_B, preferred_element_type=jnp.float32
            ) * score_scale
            grad_p = lax.dot_general(
                value_ref[0, :, cols], grad_rows, TRANS_B, preferred_element_type=jnp.float32
            )
            softmax_p = jnp.exp(scores - stats_ref[0, 0, pl.ds(h, 1), :])
            grad_s = (
                softmax_p * (grad_p - stats_ref[0, 1, pl.ds(h, 1), :]) * score_scale
            ).astype(jnp.bfloat16)
            value_acc[here, :, cols] += jnp.dot(
                softmax_p.astype(jnp.bfloat16), grad_rows, preferred_element_type=jnp.float32
            )
            key_acc[here, :, cols] += jnp.dot(
                grad_s, query_rows, preferred_element_type=jnp.float32
            )

    @pl.when(slot == pl.num_programs(0) - 1)
    def _():
        key_out[...] = key_acc[...].astype(key_out.dtype)
        value_out[...] = value_acc[...].astype(value_out.dtype)


def kv_grads(rows, pair_recv, row_keys, row_values, stats_recv):
    slot_total, _, span_len, width = pair_recv.shape
    rows_here, nlen = row_keys.shape[:2]
    heads = width // HEAD
    out_shape = jax.ShapeDtypeStruct((rows_here, nlen, width), jnp.bfloat16)
    grid_spec = pltpu.PrefetchScalarGridSpec(
        num_scalar_prefetch=1,
        grid=(slot_total,),
        in_specs=[
            pl.BlockSpec((1, 2, span_len, width), lambda t, rows: (t, 0, 0, 0)),
            pl.BlockSpec((1, nlen, width), lambda t, rows: (jnp.maximum(rows[t], 0), 0, 0)),
            pl.BlockSpec((1, nlen, width), lambda t, rows: (jnp.maximum(rows[t], 0), 0, 0)),
            pl.BlockSpec((1, 2, heads, span_len), lambda t, rows: (t, 0, 0, 0)),
        ],
        out_specs=[
            pl.BlockSpec((rows_here, nlen, width), lambda t, rows: (0, 0, 0)),
            pl.BlockSpec((rows_here, nlen, width), lambda t, rows: (0, 0, 0)),
        ],
        scratch_shapes=[
            pltpu.VMEM((rows_here, nlen, width), jnp.float32),
            pltpu.VMEM((rows_here, nlen, width), jnp.float32),
        ],
    )
    return pl.pallas_call(
        kv_kernel,
        grid_spec=grid_spec,
        out_shape=[out_shape, out_shape],
        compiler_params=pltpu.CompilerParams(
            dimension_semantics=("arbitrary",), vmem_limit_bytes=48 * 1024 * 1024
        ),
    )(rows, pair_recv, row_keys, row_values, stats_recv)


def per_device(queries, out_grad, row_keys, row_values, neighbours):
    seq_count = lax.axis_size("seq")
    own_lists = lax.all_gather(neighbours, "mp", axis=0, tiled=True)
    span_count = queries.shape[0]
    rows_here = row_keys.shape[0]
    width_here = queries.shape[2]
    heads_here = width_here // HEAD
    flat_rows = own_lists.reshape(-1)
    item_count = flat_rows.shape[0]
    owner_dev = flat_rows // rows_here
    local_row = flat_rows % rows_here
    slot_depth = (item_count + seq_count - 1) // seq_count
    slot_total = seq_count * slot_depth
    position = jnp.arange(item_count)
    same_before = (owner_dev[:, None] == owner_dev[None, :]) & (
        position[None, :] < position[:, None]
    )
    earlier = jnp.sum(same_before.astype(jnp.int32), axis=1)
    target = owner_dev * slot_depth + earlier
    item_span = position // NBR
    score_scale = HEAD ** (-0.5)

    match = target[None, :] == jnp.arange(slot_total)[:, None]
    slot_item = jnp.sum(jnp.where(match, position[None, :], 0), axis=1)
    slot_span = item_span[slot_item]

    joined = jnp.concatenate([queries, out_grad], axis=1)
    pair_send = joined[slot_span].reshape(slot_total, 2, SPAN, width_here)
    pair_recv = lax.all_to_all(pair_send, "seq", split_axis=0, concat_axis=0, tiled=True)

    my_seq = lax.axis_index("seq")
    lists = lax.all_gather(flat_rows, "seq", axis=0, tiled=False)
    owner_all = lists // rows_here
    local_all = lists % rows_here
    before_all = (owner_all[:, :, None] == owner_all[:, None, :]) & (
        position[None, None, :] < position[None, :, None]
    )
    target_all = owner_all * slot_depth + jnp.sum(before_all.astype(jnp.int32), axis=2)
    wanted = my_seq * slot_depth + jnp.arange(slot_depth)
    hit = target_all[:, None, :] == wanted[None, :, None]
    row_recv = jnp.where(
        jnp.any(hit, axis=2), jnp.sum(jnp.where(hit, local_all[:, None, :], 0), axis=2), -1
    ).reshape(slot_total)

    row_index = jnp.clip(row_recv, 0, rows_here - 1)
    part = slot_stats(row_index, pair_recv, row_keys, row_values).reshape(
        slot_total, 3, heads_here * SPAN
    )
    back = lax.all_to_all(part, "seq", split_axis=0, concat_axis=0, tiled=True)

    item_part = back[target].reshape(span_count, NBR, 3, heads_here * SPAN)
    item_max = item_part[:, :, 0]
    item_sum = item_part[:, :, 1]
    item_cross = item_part[:, :, 2]
    span_max = jnp.max(item_max, axis=1, keepdims=True)
    factor = jnp.exp(item_max - span_max)
    span_sum = jnp.sum(item_sum * factor, axis=1)
    log_total = span_max[:, 0] + jnp.log(span_sum)
    row_delta = jnp.sum(item_cross * factor, axis=1) / span_sum
    span_stats = jnp.stack([log_total, row_delta], axis=1)
    stats_recv = lax.all_to_all(
        span_stats[slot_span], "seq", split_axis=0, concat_axis=0, tiled=True
    )

    stats_here = stats_recv.reshape(slot_total, 2, heads_here, SPAN)
    query_part = slot_grads(row_index, pair_recv, row_keys, row_values, stats_here)
    query_back = lax.all_to_all(query_part, "seq", split_axis=0, concat_axis=0, tiled=True)

    key_grad, value_grad = kv_grads(row_recv, pair_recv, row_keys, row_values, stats_here)

    returned = query_back[target].reshape(span_count, NBR, SPAN, width_here).astype(jnp.float32)
    query_grad = jnp.sum(returned, axis=1).astype(jnp.bfloat16)
    return (query_grad, key_grad, value_grad)


def solution(mesh):
    in_specs = (
        P("seq", None, "mp"),
        P("seq", None, "mp"),
        P("seq", None, "mp"),
        P("seq", None, "mp"),
        P(("seq", "mp"), None),
    )
    out_specs = (P("seq", None, "mp"), P("seq", None, "mp"), P("seq", None, "mp"))
    return jax.shard_map(
        per_device, mesh=mesh, in_specs=in_specs, out_specs=out_specs, check_vma=False
    )
```

```python
import jax
import jax.numpy as jnp
from jax import lax
from jax.experimental import pallas as pl
from jax.experimental.pallas import tpu as pltpu
from jax.sharding import PartitionSpec as P

HEAD = 128
SPAN = 64
NLEN = 128
NBR = 2

TRANS_A = (((0,), (0,)), ((), ()))


def split_heads(tensor):
    return tensor.reshape(tensor.shape[:-1] + (tensor.shape[-1] // HEAD, HEAD))


def kv_kernel(rows_ref, probs_ref, grads_ref, pair_ref, key_out, value_out, key_acc, value_acc):
    slot = pl.program_id(0)
    heads = probs_ref.shape[1]

    @pl.when(slot == 0)
    def _():
        key_acc[...] = jnp.zeros_like(key_acc)
        value_acc[...] = jnp.zeros_like(value_acc)

    row = rows_ref[slot]

    @pl.when(row >= 0)
    def _():
        here = jnp.maximum(row, 0)
        for h in range(heads):
            cols = pl.ds(h * HEAD, HEAD)
            value_part = lax.dot_general(
                probs_ref[0, h], pair_ref[0, 1, :, cols], TRANS_A,
                preferred_element_type=jnp.float32,
            )
            key_part = lax.dot_general(
                grads_ref[0, h], pair_ref[0, 0, :, cols], TRANS_A,
                preferred_element_type=jnp.float32,
            )
            value_acc[here, :, cols] += value_part
            key_acc[here, :, cols] += key_part

    @pl.when(slot == pl.num_programs(0) - 1)
    def _():
        key_out[...] = key_acc[...].astype(key_out.dtype)
        value_out[...] = value_acc[...].astype(value_out.dtype)


def kv_grads(row_recv, probs_low, grad_s, pair_recv, rows_here):
    slot_total, heads, span_len, nlen = probs_low.shape
    width = pair_recv.shape[-1]
    out_shape = jax.ShapeDtypeStruct((rows_here, nlen, width), jnp.bfloat16)
    grid_spec = pltpu.PrefetchScalarGridSpec(
        num_scalar_prefetch=1,
        grid=(slot_total,),
        in_specs=[
            pl.BlockSpec((1, heads, span_len, nlen), lambda t, rows: (t, 0, 0, 0)),
            pl.BlockSpec((1, heads, span_len, nlen), lambda t, rows: (t, 0, 0, 0)),
            pl.BlockSpec((1, 2, span_len, width), lambda t, rows: (t, 0, 0, 0)),
        ],
        out_specs=[
            pl.BlockSpec((rows_here, nlen, width), lambda t, rows: (0, 0, 0)),
            pl.BlockSpec((rows_here, nlen, width), lambda t, rows: (0, 0, 0)),
        ],
        scratch_shapes=[
            pltpu.VMEM((rows_here, nlen, width), jnp.float32),
            pltpu.VMEM((rows_here, nlen, width), jnp.float32),
        ],
    )
    return pl.pallas_call(
        kv_kernel,
        grid_spec=grid_spec,
        out_shape=[out_shape, out_shape],
        compiler_params=pltpu.CompilerParams(
            dimension_semantics=("arbitrary",), vmem_limit_bytes=48 * 1024 * 1024
        ),
    )(row_recv, probs_low, grad_s, pair_recv)


def per_device(queries, out_grad, row_keys, row_values, neighbours):
    seq_count = lax.axis_size("seq")
    own_lists = lax.all_gather(neighbours, "mp", axis=0, tiled=True)
    span_count = queries.shape[0]
    rows_here = row_keys.shape[0]
    width_here = queries.shape[2]
    heads_here = width_here // HEAD
    flat_rows = own_lists.reshape(-1)
    item_count = flat_rows.shape[0]
    owner_dev = flat_rows // rows_here
    local_row = flat_rows % rows_here
    slot_depth = (item_count + seq_count - 1) // seq_count
    slot_total = seq_count * slot_depth
    position = jnp.arange(item_count)
    same_before = (owner_dev[:, None] == owner_dev[None, :]) & (
        position[None, :] < position[:, None]
    )
    earlier = jnp.sum(same_before.astype(jnp.int32), axis=1)
    target = owner_dev * slot_depth + earlier
    item_span = position // NBR
    score_scale = HEAD ** (-0.5)

    match = target[None, :] == jnp.arange(slot_total)[:, None]
    slot_valid = jnp.any(match, axis=1)
    slot_item = jnp.sum(jnp.where(match, position[None, :], 0), axis=1)
    slot_span = item_span[slot_item]

    joined = jnp.concatenate([queries, out_grad], axis=1)
    pair_send = joined[slot_span].reshape(slot_total, 2, SPAN, width_here)
    row_send = jnp.where(slot_valid, local_row[slot_item], -1)
    pair_recv = lax.all_to_all(pair_send, "seq", split_axis=0, concat_axis=0, tiled=True)
    row_recv = lax.all_to_all(row_send, "seq", split_axis=0, concat_axis=0, tiled=True)

    row_index = jnp.clip(row_recv, 0, rows_here - 1)
    query_heads = split_heads(pair_recv[:, 0])
    grad_heads = split_heads(pair_recv[:, 1])
    key_heads = split_heads(row_keys[row_index])
    value_heads = split_heads(row_values[row_index])

    scores = (
        jnp.einsum("bihd,bjhd->bhij", query_heads, key_heads, preferred_element_type=jnp.float32)
        * score_scale
    )
    grad_p = jnp.einsum(
        "bihd,bjhd->bhij", grad_heads, value_heads, preferred_element_type=jnp.float32
    )
    highest = jnp.max(scores, axis=3)
    expons = jnp.exp(scores - highest[..., None])
    part = jnp.stack(
        [highest, jnp.sum(expons, axis=3), jnp.sum(expons * grad_p, axis=3)], axis=1
    ).reshape(slot_total, 3, heads_here * SPAN)
    back = lax.all_to_all(part, "seq", split_axis=0, concat_axis=0, tiled=True)

    item_part = back[target].reshape(span_count, NBR, 3, heads_here * SPAN)
    item_max = item_part[:, :, 0]
    item_sum = item_part[:, :, 1]
    item_cross = item_part[:, :, 2]
    span_max = jnp.max(item_max, axis=1, keepdims=True)
    factor = jnp.exp(item_max - span_max)
    span_sum = jnp.sum(item_sum * factor, axis=1)
    log_total = span_max[:, 0] + jnp.log(span_sum)
    row_delta = jnp.sum(item_cross * factor, axis=1) / span_sum
    span_stats = jnp.stack([log_total, row_delta], axis=1)
    stats_recv = lax.all_to_all(
        span_stats[slot_span], "seq", split_axis=0, concat_axis=0, tiled=True
    )

    norm_here = stats_recv[:, 0].reshape(slot_total, heads_here, SPAN)
    delta_here = stats_recv[:, 1].reshape(slot_total, heads_here, SPAN)
    softmax_p = jnp.exp(scores - norm_here[..., None])
    grad_s = (softmax_p * (grad_p - delta_here[..., None]) * score_scale).astype(jnp.bfloat16)
    probs_low = softmax_p.astype(jnp.bfloat16)
    query_part = jnp.einsum(
        "bhij,bjhd->bihd", grad_s, key_heads, preferred_element_type=jnp.float32
    ).astype(jnp.bfloat16).reshape(slot_total, SPAN, width_here)
    query_back = lax.all_to_all(query_part, "seq", split_axis=0, concat_axis=0, tiled=True)

    key_grad, value_grad = kv_grads(row_recv, probs_low, grad_s, pair_recv, rows_here)

    pair_target = target.reshape(span_count, NBR)
    query_grad = (
        query_back[pair_target[:, 0]].astype(jnp.float32)
        + query_back[pair_target[:, 1]].astype(jnp.float32)
    ).astype(jnp.bfloat16)
    return (query_grad, key_grad, value_grad)


def solution(mesh):
    in_specs = (
        P("seq", None, "mp"),
        P("seq", None, "mp"),
        P("seq", None, "mp"),
        P("seq", None, "mp"),
        P(("seq", "mp"), None),
    )
    out_specs = (P("seq", None, "mp"), P("seq", None, "mp"), P("seq", None, "mp"))
    return jax.shard_map(
        per_device, mesh=mesh, in_specs=in_specs, out_specs=out_specs, check_vma=False
    )
```

```python
import jax
import jax.numpy as jnp
from jax import lax
from jax.experimental import pallas as pl
from jax.experimental.pallas import tpu as pltpu
from jax.sharding import PartitionSpec as P

HEAD = 128
SPAN = 64
NLEN = 128
NBR = 2

TRANS_A = (((0,), (0,)), ((), ()))


def split_heads(tensor):
    return tensor.reshape(tensor.shape[:-1] + (tensor.shape[-1] // HEAD, HEAD))


def kv_kernel(rows_ref, probs_ref, grads_ref, pair_ref, key_out, value_out, key_acc, value_acc):
    slot = pl.program_id(0)
    heads = probs_ref.shape[1]

    @pl.when(slot == 0)
    def _():
        key_acc[...] = jnp.zeros_like(key_acc)
        value_acc[...] = jnp.zeros_like(value_acc)

    row = rows_ref[slot]

    @pl.when(row >= 0)
    def _():
        here = jnp.maximum(row, 0)
        for h in range(heads):
            cols = pl.ds(h * HEAD, HEAD)
            value_part = lax.dot_general(
                probs_ref[0, h], pair_ref[0, 1, :, cols], TRANS_A,
                preferred_element_type=jnp.float32,
            )
            key_part = lax.dot_general(
                grads_ref[0, h], pair_ref[0, 0, :, cols], TRANS_A,
                preferred_element_type=jnp.float32,
            )
            value_acc[here, :, cols] += value_part
            key_acc[here, :, cols] += key_part

    @pl.when(slot == pl.num_programs(0) - 1)
    def _():
        key_out[...] = key_acc[...].astype(key_out.dtype)
        value_out[...] = value_acc[...].astype(value_out.dtype)


def kv_grads(row_recv, probs_low, grad_s, pair_recv, rows_here):
    slot_total, heads, span_len, nlen = probs_low.shape
    width = pair_recv.shape[-1]
    out_shape = jax.ShapeDtypeStruct((rows_here, nlen, width), jnp.bfloat16)
    grid_spec = pltpu.PrefetchScalarGridSpec(
        num_scalar_prefetch=1,
        grid=(slot_total,),
        in_specs=[
            pl.BlockSpec((1, heads, span_len, nlen), lambda t, rows: (t, 0, 0, 0)),
            pl.BlockSpec((1, heads, span_len, nlen), lambda t, rows: (t, 0, 0, 0)),
            pl.BlockSpec((1, 2, span_len, width), lambda t, rows: (t, 0, 0, 0)),
        ],
        out_specs=[
            pl.BlockSpec((rows_here, nlen, width), lambda t, rows: (0, 0, 0)),
            pl.BlockSpec((rows_here, nlen, width), lambda t, rows: (0, 0, 0)),
        ],
        scratch_shapes=[
            pltpu.VMEM((rows_here, nlen, width), jnp.float32),
            pltpu.VMEM((rows_here, nlen, width), jnp.float32),
        ],
    )
    return pl.pallas_call(
        kv_kernel,
        grid_spec=grid_spec,
        out_shape=[out_shape, out_shape],
        compiler_params=pltpu.CompilerParams(
            dimension_semantics=("arbitrary",), vmem_limit_bytes=48 * 1024 * 1024
        ),
    )(row_recv, probs_low, grad_s, pair_recv)


def pair_kernel(span_ref, query_ref, grad_ref, pair_out):
    pair_out[0, 0] = query_ref[0]
    pair_out[0, 1] = grad_ref[0]


def gather_pairs(slot_span, queries, out_grad):
    span_count, span_len, width = queries.shape
    slot_total = slot_span.shape[0]

    def source(t, spans):
        return (jnp.clip(spans[t], 0, span_count - 1), 0, 0)

    grid_spec = pltpu.PrefetchScalarGridSpec(
        num_scalar_prefetch=1,
        grid=(slot_total,),
        in_specs=[
            pl.BlockSpec((1, span_len, width), source),
            pl.BlockSpec((1, span_len, width), source),
        ],
        out_specs=pl.BlockSpec((1, 2, span_len, width), lambda t, spans: (t, 0, 0, 0)),
    )
    return pl.pallas_call(
        pair_kernel,
        grid_spec=grid_spec,
        out_shape=jax.ShapeDtypeStruct((slot_total, 2, span_len, width), queries.dtype),
        compiler_params=pltpu.CompilerParams(dimension_semantics=("arbitrary",)),
    )(slot_span, queries, out_grad)


def sum_kernel(target_ref, first_ref, second_ref, query_out):
    query_out[0] = (
        first_ref[0].astype(jnp.float32) + second_ref[0].astype(jnp.float32)
    ).astype(query_out.dtype)


def sum_parts(target, query_back):
    slot_total, span_len, width = query_back.shape
    span_count = target.shape[0] // NBR

    def part(n):
        return lambda c, tgt: (jnp.clip(tgt[c * NBR + n], 0, slot_total - 1), 0, 0)

    grid_spec = pltpu.PrefetchScalarGridSpec(
        num_scalar_prefetch=1,
        grid=(span_count,),
        in_specs=[
            pl.BlockSpec((1, span_len, width), part(0)),
            pl.BlockSpec((1, span_len, width), part(1)),
        ],
        out_specs=pl.BlockSpec((1, span_len, width), lambda c, tgt: (c, 0, 0)),
    )
    return pl.pallas_call(
        sum_kernel,
        grid_spec=grid_spec,
        out_shape=jax.ShapeDtypeStruct((span_count, span_len, width), query_back.dtype),
        compiler_params=pltpu.CompilerParams(dimension_semantics=("arbitrary",)),
    )(target, query_back, query_back)


def per_device(queries, out_grad, row_keys, row_values, neighbours):
    seq_count = lax.axis_size("seq")
    own_lists = lax.all_gather(neighbours, "mp", axis=0, tiled=True)
    span_count = queries.shape[0]
    rows_here = row_keys.shape[0]
    width_here = queries.shape[2]
    heads_here = width_here // HEAD
    flat_rows = own_lists.reshape(-1)
    item_count = flat_rows.shape[0]
    owner_dev = flat_rows // rows_here
    local_row = flat_rows % rows_here
    slot_depth = (item_count + seq_count - 1) // seq_count
    slot_total = seq_count * slot_depth
    position = jnp.arange(item_count)
    same_before = (owner_dev[:, None] == owner_dev[None, :]) & (
        position[None, :] < position[:, None]
    )
    earlier = jnp.sum(same_before.astype(jnp.int32), axis=1)
    target = owner_dev * slot_depth + earlier
    item_span = position // NBR
    score_scale = HEAD ** (-0.5)

    match = target[None, :] == jnp.arange(slot_total)[:, None]
    slot_valid = jnp.any(match, axis=1)
    slot_item = jnp.sum(jnp.where(match, position[None, :], 0), axis=1)
    slot_span = item_span[slot_item]

    pair_send = gather_pairs(slot_span, queries, out_grad)
    row_send = jnp.where(slot_valid, local_row[slot_item], -1)
    pair_recv = lax.all_to_all(pair_send, "seq", split_axis=0, concat_axis=0, tiled=True)
    row_recv = lax.all_to_all(row_send, "seq", split_axis=0, concat_axis=0, tiled=True)

    row_index = jnp.clip(row_recv, 0, rows_here - 1)
    query_heads = split_heads(pair_recv[:, 0])
    grad_heads = split_heads(pair_recv[:, 1])
    key_heads = split_heads(row_keys[row_index])
    value_heads = split_heads(row_values[row_index])

    scores = (
        jnp.einsum("bihd,bjhd->bhij", query_heads, key_heads, preferred_element_type=jnp.float32)
        * score_scale
    )
    grad_p = jnp.einsum(
        "bihd,bjhd->bhij", grad_heads, value_heads, preferred_element_type=jnp.float32
    )
    highest = jnp.max(scores, axis=3)
    expons = jnp.exp(scores - highest[..., None])
    part = jnp.stack(
        [highest, jnp.sum(expons, axis=3), jnp.sum(expons * grad_p, axis=3)], axis=1
    ).reshape(slot_total, 3, heads_here * SPAN)
    back = lax.all_to_all(part, "seq", split_axis=0, concat_axis=0, tiled=True)

    item_part = back[target].reshape(span_count, NBR, 3, heads_here * SPAN)
    item_max = item_part[:, :, 0]
    item_sum = item_part[:, :, 1]
    item_cross = item_part[:, :, 2]
    span_max = jnp.max(item_max, axis=1, keepdims=True)
    factor = jnp.exp(item_max - span_max)
    span_sum = jnp.sum(item_sum * factor, axis=1)
    log_total = span_max[:, 0] + jnp.log(span_sum)
    row_delta = jnp.sum(item_cross * factor, axis=1) / span_sum
    span_stats = jnp.stack([log_total, row_delta], axis=1)
    stats_recv = lax.all_to_all(
        span_stats[slot_span], "seq", split_axis=0, concat_axis=0, tiled=True
    )

    norm_here = stats_recv[:, 0].reshape(slot_total, heads_here, SPAN)
    delta_here = stats_recv[:, 1].reshape(slot_total, heads_here, SPAN)
    softmax_p = jnp.exp(scores - norm_here[..., None])
    grad_s = (softmax_p * (grad_p - delta_here[..., None]) * score_scale).astype(jnp.bfloat16)
    probs_low = softmax_p.astype(jnp.bfloat16)
    query_part = jnp.einsum(
        "bhij,bjhd->bihd", grad_s, key_heads, preferred_element_type=jnp.float32
    ).astype(jnp.bfloat16).reshape(slot_total, SPAN, width_here)
    query_back = lax.all_to_all(query_part, "seq", split_axis=0, concat_axis=0, tiled=True)

    key_grad, value_grad = kv_grads(row_recv, probs_low, grad_s, pair_recv, rows_here)

    query_grad = sum_parts(target, query_back)
    return (query_grad, key_grad, value_grad)


def solution(mesh):
    in_specs = (
        P("seq", None, "mp"),
        P("seq", None, "mp"),
        P("seq", None, "mp"),
        P("seq", None, "mp"),
        P(("seq", "mp"), None),
    )
    out_specs = (P("seq", None, "mp"), P("seq", None, "mp"), P("seq", None, "mp"))
    return jax.shard_map(
        per_device, mesh=mesh, in_specs=in_specs, out_specs=out_specs, check_vma=False
    )
```

```python
import jax
import jax.numpy as jnp
from jax import lax
from jax.experimental import pallas as pl
from jax.experimental.pallas import tpu as pltpu
from jax.sharding import PartitionSpec as P

HEAD = 128
SPAN = 64
NLEN = 128
NBR = 2

TRANS_A = (((0,), (0,)), ((), ()))


def split_heads(tensor):
    return tensor.reshape(tensor.shape[:-1] + (tensor.shape[-1] // HEAD, HEAD))


def kv_kernel(rows_ref, probs_ref, grads_ref, pair_ref, key_out, value_out, key_acc, value_acc):
    slot = pl.program_id(0)
    heads = probs_ref.shape[1]

    @pl.when(slot == 0)
    def _():
        key_acc[...] = jnp.zeros_like(key_acc)
        value_acc[...] = jnp.zeros_like(value_acc)

    row = rows_ref[slot]

    @pl.when(row >= 0)
    def _():
        here = jnp.maximum(row, 0)
        for h in range(heads):
            cols = pl.ds(h * HEAD, HEAD)
            value_part = lax.dot_general(
                probs_ref[0, h], pair_ref[0, 1, :, cols], TRANS_A,
                preferred_element_type=jnp.float32,
            )
            key_part = lax.dot_general(
                grads_ref[0, h], pair_ref[0, 0, :, cols], TRANS_A,
                preferred_element_type=jnp.float32,
            )
            value_acc[here, :, cols] += value_part
            key_acc[here, :, cols] += key_part

    @pl.when(slot == pl.num_programs(0) - 1)
    def _():
        key_out[...] = key_acc[...].astype(key_out.dtype)
        value_out[...] = value_acc[...].astype(value_out.dtype)


def kv_grads(row_recv, probs_low, grad_s, pair_recv, rows_here):
    slot_total, heads, span_len, nlen = probs_low.shape
    width = pair_recv.shape[-1]
    out_shape = jax.ShapeDtypeStruct((rows_here, nlen, width), jnp.bfloat16)
    grid_spec = pltpu.PrefetchScalarGridSpec(
        num_scalar_prefetch=1,
        grid=(slot_total,),
        in_specs=[
            pl.BlockSpec((1, heads, span_len, nlen), lambda t, rows: (t, 0, 0, 0)),
            pl.BlockSpec((1, heads, span_len, nlen), lambda t, rows: (t, 0, 0, 0)),
            pl.BlockSpec((1, 2, span_len, width), lambda t, rows: (t, 0, 0, 0)),
        ],
        out_specs=[
            pl.BlockSpec((rows_here, nlen, width), lambda t, rows: (0, 0, 0)),
            pl.BlockSpec((rows_here, nlen, width), lambda t, rows: (0, 0, 0)),
        ],
        scratch_shapes=[
            pltpu.VMEM((rows_here, nlen, width), jnp.float32),
            pltpu.VMEM((rows_here, nlen, width), jnp.float32),
        ],
    )
    return pl.pallas_call(
        kv_kernel,
        grid_spec=grid_spec,
        out_shape=[out_shape, out_shape],
        compiler_params=pltpu.CompilerParams(
            dimension_semantics=("arbitrary",), vmem_limit_bytes=48 * 1024 * 1024
        ),
    )(row_recv, probs_low, grad_s, pair_recv)


def pair_kernel(span_ref, query_ref, grad_ref, pair_out):
    def body(t, carry):
        source = span_ref[t]
        pair_out[t, 0] = query_ref[source]
        pair_out[t, 1] = grad_ref[source]
        return carry

    lax.fori_loop(0, pair_out.shape[0], body, 0)


def gather_pairs(slot_span, queries, out_grad):
    span_count, span_len, width = queries.shape
    slot_total = slot_span.shape[0]
    grid_spec = pltpu.PrefetchScalarGridSpec(
        num_scalar_prefetch=1,
        grid=(1,),
        in_specs=[
            pl.BlockSpec((span_count, span_len, width), lambda i, spans: (0, 0, 0)),
            pl.BlockSpec((span_count, span_len, width), lambda i, spans: (0, 0, 0)),
        ],
        out_specs=pl.BlockSpec((slot_total, 2, span_len, width), lambda i, spans: (0, 0, 0, 0)),
    )
    return pl.pallas_call(
        pair_kernel,
        grid_spec=grid_spec,
        out_shape=jax.ShapeDtypeStruct((slot_total, 2, span_len, width), queries.dtype),
        compiler_params=pltpu.CompilerParams(vmem_limit_bytes=48 * 1024 * 1024),
    )(jnp.clip(slot_span, 0, span_count - 1), queries, out_grad)


def sum_kernel(target_ref, back_ref, query_out):
    def body(c, carry):
        first = back_ref[target_ref[c * NBR]].astype(jnp.float32)
        second = back_ref[target_ref[c * NBR + 1]].astype(jnp.float32)
        query_out[c] = (first + second).astype(query_out.dtype)
        return carry

    lax.fori_loop(0, query_out.shape[0], body, 0)


def sum_parts(target, query_back):
    slot_total, span_len, width = query_back.shape
    span_count = target.shape[0] // NBR
    grid_spec = pltpu.PrefetchScalarGridSpec(
        num_scalar_prefetch=1,
        grid=(1,),
        in_specs=[pl.BlockSpec((slot_total, span_len, width), lambda i, tgt: (0, 0, 0))],
        out_specs=pl.BlockSpec((span_count, span_len, width), lambda i, tgt: (0, 0, 0)),
    )
    return pl.pallas_call(
        sum_kernel,
        grid_spec=grid_spec,
        out_shape=jax.ShapeDtypeStruct((span_count, span_len, width), query_back.dtype),
        compiler_params=pltpu.CompilerParams(vmem_limit_bytes=48 * 1024 * 1024),
    )(jnp.clip(target, 0, slot_total - 1), query_back)


def per_device(queries, out_grad, row_keys, row_values, neighbours):
    seq_count = lax.axis_size("seq")
    own_lists = lax.all_gather(neighbours, "mp", axis=0, tiled=True)
    span_count = queries.shape[0]
    rows_here = row_keys.shape[0]
    width_here = queries.shape[2]
    heads_here = width_here // HEAD
    flat_rows = own_lists.reshape(-1)
    item_count = flat_rows.shape[0]
    owner_dev = flat_rows // rows_here
    local_row = flat_rows % rows_here
    slot_depth = (item_count + seq_count - 1) // seq_count
    slot_total = seq_count * slot_depth
    position = jnp.arange(item_count)
    same_before = (owner_dev[:, None] == owner_dev[None, :]) & (
        position[None, :] < position[:, None]
    )
    earlier = jnp.sum(same_before.astype(jnp.int32), axis=1)
    target = owner_dev * slot_depth + earlier
    item_span = position // NBR
    score_scale = HEAD ** (-0.5)

    match = target[None, :] == jnp.arange(slot_total)[:, None]
    slot_valid = jnp.any(match, axis=1)
    slot_item = jnp.sum(jnp.where(match, position[None, :], 0), axis=1)
    slot_span = item_span[slot_item]

    pair_send = gather_pairs(slot_span, queries, out_grad)
    row_send = jnp.where(slot_valid, local_row[slot_item], -1)
    pair_recv = lax.all_to_all(pair_send, "seq", split_axis=0, concat_axis=0, tiled=True)
    row_recv = lax.all_to_all(row_send, "seq", split_axis=0, concat_axis=0, tiled=True)

    row_index = jnp.clip(row_recv, 0, rows_here - 1)
    query_heads = split_heads(pair_recv[:, 0])
    grad_heads = split_heads(pair_recv[:, 1])
    key_heads = split_heads(row_keys[row_index])
    value_heads = split_heads(row_values[row_index])

    scores = (
        jnp.einsum("bihd,bjhd->bhij", query_heads, key_heads, preferred_element_type=jnp.float32)
        * score_scale
    )
    grad_p = jnp.einsum(
        "bihd,bjhd->bhij", grad_heads, value_heads, preferred_element_type=jnp.float32
    )
    highest = jnp.max(scores, axis=3)
    expons = jnp.exp(scores - highest[..., None])
    part = jnp.stack(
        [highest, jnp.sum(expons, axis=3), jnp.sum(expons * grad_p, axis=3)], axis=1
    ).reshape(slot_total, 3, heads_here * SPAN)
    back = lax.all_to_all(part, "seq", split_axis=0, concat_axis=0, tiled=True)

    item_part = back[target].reshape(span_count, NBR, 3, heads_here * SPAN)
    item_max = item_part[:, :, 0]
    item_sum = item_part[:, :, 1]
    item_cross = item_part[:, :, 2]
    span_max = jnp.max(item_max, axis=1, keepdims=True)
    factor = jnp.exp(item_max - span_max)
    span_sum = jnp.sum(item_sum * factor, axis=1)
    log_total = span_max[:, 0] + jnp.log(span_sum)
    row_delta = jnp.sum(item_cross * factor, axis=1) / span_sum
    span_stats = jnp.stack([log_total, row_delta], axis=1)
    stats_recv = lax.all_to_all(
        span_stats[slot_span], "seq", split_axis=0, concat_axis=0, tiled=True
    )

    norm_here = stats_recv[:, 0].reshape(slot_total, heads_here, SPAN)
    delta_here = stats_recv[:, 1].reshape(slot_total, heads_here, SPAN)
    softmax_p = jnp.exp(scores - norm_here[..., None])
    grad_s = (softmax_p * (grad_p - delta_here[..., None]) * score_scale).astype(jnp.bfloat16)
    probs_low = softmax_p.astype(jnp.bfloat16)
    query_part = jnp.einsum(
        "bhij,bjhd->bihd", grad_s, key_heads, preferred_element_type=jnp.float32
    ).astype(jnp.bfloat16).reshape(slot_total, SPAN, width_here)
    query_back = lax.all_to_all(query_part, "seq", split_axis=0, concat_axis=0, tiled=True)

    key_grad, value_grad = kv_grads(row_recv, probs_low, grad_s, pair_recv, rows_here)

    query_grad = sum_parts(target, query_back)
    return (query_grad, key_grad, value_grad)


def solution(mesh):
    in_specs = (
        P("seq", None, "mp"),
        P("seq", None, "mp"),
        P("seq", None, "mp"),
        P("seq", None, "mp"),
        P(("seq", "mp"), None),
    )
    out_specs = (P("seq", None, "mp"), P("seq", None, "mp"), P("seq", None, "mp"))
    return jax.shard_map(
        per_device, mesh=mesh, in_specs=in_specs, out_specs=out_specs, check_vma=False
    )
```

```python
import jax
import jax.numpy as jnp
from jax import lax
from jax.experimental import pallas as pl
from jax.experimental.pallas import tpu as pltpu
from jax.sharding import PartitionSpec as P

HEAD = 128
SPAN = 64
NLEN = 128
NBR = 2

TRANS_A = (((0,), (0,)), ((), ()))


def split_heads(tensor):
    return tensor.reshape(tensor.shape[:-1] + (tensor.shape[-1] // HEAD, HEAD))


def kv_kernel(rows_ref, probs_ref, grads_ref, pair_ref, key_out, value_out, key_acc, value_acc):
    slot = pl.program_id(0)
    heads = probs_ref.shape[1]

    @pl.when(slot == 0)
    def _():
        key_acc[...] = jnp.zeros_like(key_acc)
        value_acc[...] = jnp.zeros_like(value_acc)

    row = rows_ref[slot]

    @pl.when(row >= 0)
    def _():
        here = jnp.maximum(row, 0)
        for h in range(heads):
            cols = pl.ds(h * HEAD, HEAD)
            value_part = lax.dot_general(
                probs_ref[0, h], pair_ref[0, 1, h], TRANS_A,
                preferred_element_type=jnp.float32,
            )
            key_part = lax.dot_general(
                grads_ref[0, h], pair_ref[0, 0, h], TRANS_A,
                preferred_element_type=jnp.float32,
            )
            value_acc[here, :, cols] += value_part
            key_acc[here, :, cols] += key_part

    @pl.when(slot == pl.num_programs(0) - 1)
    def _():
        key_out[...] = key_acc[...].astype(key_out.dtype)
        value_out[...] = value_acc[...].astype(value_out.dtype)


def kv_grads(row_recv, probs_low, grad_s, pair_recv, rows_here):
    slot_total, heads, span_len, nlen = probs_low.shape
    width = heads * HEAD
    out_shape = jax.ShapeDtypeStruct((rows_here, nlen, width), jnp.bfloat16)
    grid_spec = pltpu.PrefetchScalarGridSpec(
        num_scalar_prefetch=1,
        grid=(slot_total,),
        in_specs=[
            pl.BlockSpec((1, heads, span_len, nlen), lambda t, rows: (t, 0, 0, 0)),
            pl.BlockSpec((1, heads, span_len, nlen), lambda t, rows: (t, 0, 0, 0)),
            pl.BlockSpec((1, 2, heads, span_len, HEAD), lambda t, rows: (t, 0, 0, 0, 0)),
        ],
        out_specs=[
            pl.BlockSpec((rows_here, nlen, width), lambda t, rows: (0, 0, 0)),
            pl.BlockSpec((rows_here, nlen, width), lambda t, rows: (0, 0, 0)),
        ],
        scratch_shapes=[
            pltpu.VMEM((rows_here, nlen, width), jnp.float32),
            pltpu.VMEM((rows_here, nlen, width), jnp.float32),
        ],
    )
    return pl.pallas_call(
        kv_kernel,
        grid_spec=grid_spec,
        out_shape=[out_shape, out_shape],
        compiler_params=pltpu.CompilerParams(
            dimension_semantics=("arbitrary",), vmem_limit_bytes=48 * 1024 * 1024
        ),
    )(row_recv, probs_low, grad_s, pair_recv)


def pair_kernel(span_ref, query_ref, grad_ref, pair_out):
    heads = pair_out.shape[2]

    def body(t, carry):
        source = span_ref[t]
        for h in range(heads):
            cols = pl.ds(h * HEAD, HEAD)
            pair_out[t, 0, h] = query_ref[source, :, cols]
            pair_out[t, 1, h] = grad_ref[source, :, cols]
        return carry

    lax.fori_loop(0, pair_out.shape[0], body, 0)


def gather_pairs(slot_span, queries, out_grad):
    span_count, span_len, width = queries.shape
    slot_total = slot_span.shape[0]
    heads = width // HEAD
    pair_shape = (slot_total, 2, heads, span_len, HEAD)
    grid_spec = pltpu.PrefetchScalarGridSpec(
        num_scalar_prefetch=1,
        grid=(1,),
        in_specs=[
            pl.BlockSpec((span_count, span_len, width), lambda i, spans: (0, 0, 0)),
            pl.BlockSpec((span_count, span_len, width), lambda i, spans: (0, 0, 0)),
        ],
        out_specs=pl.BlockSpec(pair_shape, lambda i, spans: (0, 0, 0, 0, 0)),
    )
    return pl.pallas_call(
        pair_kernel,
        grid_spec=grid_spec,
        out_shape=jax.ShapeDtypeStruct(pair_shape, queries.dtype),
        compiler_params=pltpu.CompilerParams(vmem_limit_bytes=48 * 1024 * 1024),
    )(jnp.clip(slot_span, 0, span_count - 1), queries, out_grad)


def sum_kernel(target_ref, back_ref, query_out):
    heads = back_ref.shape[1]

    def body(c, carry):
        first_slot = target_ref[c * NBR]
        second_slot = target_ref[c * NBR + 1]
        for h in range(heads):
            first = back_ref[first_slot, h].astype(jnp.float32)
            second = back_ref[second_slot, h].astype(jnp.float32)
            query_out[c, :, pl.ds(h * HEAD, HEAD)] = (first + second).astype(query_out.dtype)
        return carry

    lax.fori_loop(0, query_out.shape[0], body, 0)


def sum_parts(target, query_back):
    slot_total, heads, span_len, _ = query_back.shape
    width = heads * HEAD
    span_count = target.shape[0] // NBR
    grid_spec = pltpu.PrefetchScalarGridSpec(
        num_scalar_prefetch=1,
        grid=(1,),
        in_specs=[pl.BlockSpec(query_back.shape, lambda i, tgt: (0, 0, 0, 0))],
        out_specs=pl.BlockSpec((span_count, span_len, width), lambda i, tgt: (0, 0, 0)),
    )
    return pl.pallas_call(
        sum_kernel,
        grid_spec=grid_spec,
        out_shape=jax.ShapeDtypeStruct((span_count, span_len, width), query_back.dtype),
        compiler_params=pltpu.CompilerParams(vmem_limit_bytes=48 * 1024 * 1024),
    )(jnp.clip(target, 0, slot_total - 1), query_back)


def per_device(queries, out_grad, row_keys, row_values, neighbours):
    seq_count = lax.axis_size("seq")
    own_lists = lax.all_gather(neighbours, "mp", axis=0, tiled=True)
    span_count = queries.shape[0]
    rows_here = row_keys.shape[0]
    width_here = queries.shape[2]
    heads_here = width_here // HEAD
    flat_rows = own_lists.reshape(-1)
    item_count = flat_rows.shape[0]
    owner_dev = flat_rows // rows_here
    local_row = flat_rows % rows_here
    slot_depth = (item_count + seq_count - 1) // seq_count
    slot_total = seq_count * slot_depth
    position = jnp.arange(item_count)
    same_before = (owner_dev[:, None] == owner_dev[None, :]) & (
        position[None, :] < position[:, None]
    )
    earlier = jnp.sum(same_before.astype(jnp.int32), axis=1)
    target = owner_dev * slot_depth + earlier
    item_span = position // NBR
    score_scale = HEAD ** (-0.5)

    match = target[None, :] == jnp.arange(slot_total)[:, None]
    slot_valid = jnp.any(match, axis=1)
    slot_item = jnp.sum(jnp.where(match, position[None, :], 0), axis=1)
    slot_span = item_span[slot_item]

    pair_send = gather_pairs(slot_span, queries, out_grad)
    row_send = jnp.where(slot_valid, local_row[slot_item], -1)
    pair_recv = lax.all_to_all(pair_send, "seq", split_axis=0, concat_axis=0, tiled=True)
    row_recv = lax.all_to_all(row_send, "seq", split_axis=0, concat_axis=0, tiled=True)

    row_index = jnp.clip(row_recv, 0, rows_here - 1)
    query_heads = pair_recv[:, 0]
    grad_heads = pair_recv[:, 1]
    key_heads = jnp.swapaxes(split_heads(row_keys), 1, 2)[row_index]
    value_heads = jnp.swapaxes(split_heads(row_values), 1, 2)[row_index]

    scores = (
        jnp.einsum("bhid,bhjd->bhij", query_heads, key_heads, preferred_element_type=jnp.float32)
        * score_scale
    )
    grad_p = jnp.einsum(
        "bhid,bhjd->bhij", grad_heads, value_heads, preferred_element_type=jnp.float32
    )
    highest = jnp.max(scores, axis=3)
    expons = jnp.exp(scores - highest[..., None])
    part = jnp.stack(
        [highest, jnp.sum(expons, axis=3), jnp.sum(expons * grad_p, axis=3)], axis=1
    ).reshape(slot_total, 3, heads_here * SPAN)
    back = lax.all_to_all(part, "seq", split_axis=0, concat_axis=0, tiled=True)

    item_part = back[target].reshape(span_count, NBR, 3, heads_here * SPAN)
    item_max = item_part[:, :, 0]
    item_sum = item_part[:, :, 1]
    item_cross = item_part[:, :, 2]
    span_max = jnp.max(item_max, axis=1, keepdims=True)
    factor = jnp.exp(item_max - span_max)
    span_sum = jnp.sum(item_sum * factor, axis=1)
    log_total = span_max[:, 0] + jnp.log(span_sum)
    row_delta = jnp.sum(item_cross * factor, axis=1) / span_sum
    span_stats = jnp.stack([log_total, row_delta], axis=1)
    stats_recv = lax.all_to_all(
        span_stats[slot_span], "seq", split_axis=0, concat_axis=0, tiled=True
    )

    norm_here = stats_recv[:, 0].reshape(slot_total, heads_here, SPAN)
    delta_here = stats_recv[:, 1].reshape(slot_total, heads_here, SPAN)
    softmax_p = jnp.exp(scores - norm_here[..., None])
    grad_s = (softmax_p * (grad_p - delta_here[..., None]) * score_scale).astype(jnp.bfloat16)
    probs_low = softmax_p.astype(jnp.bfloat16)
    query_part = jnp.einsum(
        "bhij,bhjd->bhid", grad_s, key_heads, preferred_element_type=jnp.float32
    ).astype(jnp.bfloat16)
    query_back = lax.all_to_all(query_part, "seq", split_axis=0, concat_axis=0, tiled=True)

    key_grad, value_grad = kv_grads(row_recv, probs_low, grad_s, pair_recv, rows_here)

    query_grad = sum_parts(target, query_back)
    return (query_grad, key_grad, value_grad)


def solution(mesh):
    in_specs = (
        P("seq", None, "mp"),
        P("seq", None, "mp"),
        P("seq", None, "mp"),
        P("seq", None, "mp"),
        P(("seq", "mp"), None),
    )
    out_specs = (P("seq", None, "mp"), P("seq", None, "mp"), P("seq", None, "mp"))
    return jax.shard_map(
        per_device, mesh=mesh, in_specs=in_specs, out_specs=out_specs, check_vma=False
    )
```

```python
import jax
import jax.numpy as jnp
from jax import lax
from jax.experimental import pallas as pl
from jax.experimental.pallas import tpu as pltpu
from jax.sharding import PartitionSpec as P

HEAD = 128
SPAN = 64
NLEN = 128
NBR = 2

TRANS_A = (((0,), (0,)), ((), ()))


def split_heads(tensor):
    return tensor.reshape(tensor.shape[:-1] + (tensor.shape[-1] // HEAD, HEAD))


def kv_kernel(rows_ref, probs_ref, grads_ref, pair_ref, key_out, value_out, key_acc, value_acc):
    slot = pl.program_id(0)
    heads = probs_ref.shape[1]

    @pl.when(slot == 0)
    def _():
        key_acc[...] = jnp.zeros_like(key_acc)
        value_acc[...] = jnp.zeros_like(value_acc)

    row = rows_ref[slot]

    @pl.when(row >= 0)
    def _():
        here = jnp.maximum(row, 0)
        for h in range(heads):
            cols = pl.ds(h * HEAD, HEAD)
            value_part = lax.dot_general(
                probs_ref[0, h], pair_ref[0, 1, h], TRANS_A,
                preferred_element_type=jnp.float32,
            )
            key_part = lax.dot_general(
                grads_ref[0, h], pair_ref[0, 0, h], TRANS_A,
                preferred_element_type=jnp.float32,
            )
            value_acc[here, :, cols] += value_part
            key_acc[here, :, cols] += key_part

    @pl.when(slot == pl.num_programs(0) - 1)
    def _():
        key_out[...] = key_acc[...].astype(key_out.dtype)
        value_out[...] = value_acc[...].astype(value_out.dtype)


def kv_grads(row_recv, probs_low, grad_s, pair_recv, rows_here):
    slot_total, heads, span_len, nlen = probs_low.shape
    width = heads * HEAD
    out_shape = jax.ShapeDtypeStruct((rows_here, nlen, width), jnp.bfloat16)
    grid_spec = pltpu.PrefetchScalarGridSpec(
        num_scalar_prefetch=1,
        grid=(slot_total,),
        in_specs=[
            pl.BlockSpec((1, heads, span_len, nlen), lambda t, rows: (t, 0, 0, 0)),
            pl.BlockSpec((1, heads, span_len, nlen), lambda t, rows: (t, 0, 0, 0)),
            pl.BlockSpec((1, 2, heads, span_len, HEAD), lambda t, rows: (t, 0, 0, 0, 0)),
        ],
        out_specs=[
            pl.BlockSpec((rows_here, nlen, width), lambda t, rows: (0, 0, 0)),
            pl.BlockSpec((rows_here, nlen, width), lambda t, rows: (0, 0, 0)),
        ],
        scratch_shapes=[
            pltpu.VMEM((rows_here, nlen, width), jnp.float32),
            pltpu.VMEM((rows_here, nlen, width), jnp.float32),
        ],
    )
    return pl.pallas_call(
        kv_kernel,
        grid_spec=grid_spec,
        out_shape=[out_shape, out_shape],
        compiler_params=pltpu.CompilerParams(
            dimension_semantics=("arbitrary",), vmem_limit_bytes=48 * 1024 * 1024
        ),
    )(row_recv, probs_low, grad_s, pair_recv)


def pair_kernel(span_ref, query_ref, grad_ref, pair_out):
    heads = pair_out.shape[2]

    def body(t, carry):
        source = span_ref[t]
        for h in range(heads):
            cols = pl.ds(h * HEAD, HEAD)
            pair_out[t, 0, h] = query_ref[source, :, cols]
            pair_out[t, 1, h] = grad_ref[source, :, cols]
        return carry

    lax.fori_loop(0, pair_out.shape[0], body, 0)


def gather_pairs(slot_span, queries, out_grad):
    span_count, span_len, width = queries.shape
    slot_total = slot_span.shape[0]
    heads = width // HEAD
    pair_shape = (slot_total, 2, heads, span_len, HEAD)
    grid_spec = pltpu.PrefetchScalarGridSpec(
        num_scalar_prefetch=1,
        grid=(1,),
        in_specs=[
            pl.BlockSpec((span_count, span_len, width), lambda i, spans: (0, 0, 0)),
            pl.BlockSpec((span_count, span_len, width), lambda i, spans: (0, 0, 0)),
        ],
        out_specs=pl.BlockSpec(pair_shape, lambda i, spans: (0, 0, 0, 0, 0)),
    )
    return pl.pallas_call(
        pair_kernel,
        grid_spec=grid_spec,
        out_shape=jax.ShapeDtypeStruct(pair_shape, queries.dtype),
        compiler_params=pltpu.CompilerParams(vmem_limit_bytes=48 * 1024 * 1024),
    )(jnp.clip(slot_span, 0, span_count - 1), queries, out_grad)


def sum_kernel(target_ref, back_ref, query_out):
    heads = back_ref.shape[1]

    def body(c, carry):
        first_slot = target_ref[c * NBR]
        second_slot = target_ref[c * NBR + 1]
        for h in range(heads):
            first = back_ref[first_slot, h].astype(jnp.float32)
            second = back_ref[second_slot, h].astype(jnp.float32)
            query_out[c, :, pl.ds(h * HEAD, HEAD)] = (first + second).astype(query_out.dtype)
        return carry

    lax.fori_loop(0, query_out.shape[0], body, 0)


def sum_parts(target, query_back):
    slot_total, heads, span_len, _ = query_back.shape
    width = heads * HEAD
    span_count = target.shape[0] // NBR
    grid_spec = pltpu.PrefetchScalarGridSpec(
        num_scalar_prefetch=1,
        grid=(1,),
        in_specs=[pl.BlockSpec(query_back.shape, lambda i, tgt: (0, 0, 0, 0))],
        out_specs=pl.BlockSpec((span_count, span_len, width), lambda i, tgt: (0, 0, 0)),
    )
    return pl.pallas_call(
        sum_kernel,
        grid_spec=grid_spec,
        out_shape=jax.ShapeDtypeStruct((span_count, span_len, width), query_back.dtype),
        compiler_params=pltpu.CompilerParams(vmem_limit_bytes=48 * 1024 * 1024),
    )(jnp.clip(target, 0, slot_total - 1), query_back)


def seq_exchange(blocks, seq_count):
    me = lax.axis_index("seq")
    result = jnp.zeros_like(blocks)
    result = lax.dynamic_update_index_in_dim(
        result, lax.dynamic_index_in_dim(blocks, me, keepdims=False), me, axis=0
    )
    for shift in range(1, seq_count):
        sent = lax.ppermute(
            lax.dynamic_index_in_dim(blocks, (me + shift) % seq_count, keepdims=False),
            "seq",
            perm=[(i, (i + shift) % seq_count) for i in range(seq_count)],
        )
        result = lax.dynamic_update_index_in_dim(
            result, sent, (me - shift) % seq_count, axis=0
        )
    return result


def per_device(queries, out_grad, row_keys, row_values, neighbours):
    seq_count = lax.axis_size("seq")
    own_lists = lax.all_gather(neighbours, "mp", axis=0, tiled=True)
    span_count = queries.shape[0]
    rows_here = row_keys.shape[0]
    width_here = queries.shape[2]
    heads_here = width_here // HEAD
    flat_rows = own_lists.reshape(-1)
    item_count = flat_rows.shape[0]
    owner_dev = flat_rows // rows_here
    local_row = flat_rows % rows_here
    slot_depth = (item_count + seq_count - 1) // seq_count
    slot_total = seq_count * slot_depth
    position = jnp.arange(item_count)
    same_before = (owner_dev[:, None] == owner_dev[None, :]) & (
        position[None, :] < position[:, None]
    )
    earlier = jnp.sum(same_before.astype(jnp.int32), axis=1)
    target = owner_dev * slot_depth + earlier
    item_span = position // NBR
    score_scale = HEAD ** (-0.5)

    match = target[None, :] == jnp.arange(slot_total)[:, None]
    slot_valid = jnp.any(match, axis=1)
    slot_item = jnp.sum(jnp.where(match, position[None, :], 0), axis=1)
    slot_span = item_span[slot_item]

    pair_send = gather_pairs(slot_span, queries, out_grad)
    row_send = jnp.where(slot_valid, local_row[slot_item], -1)
    pair_recv = lax.all_to_all(pair_send, "seq", split_axis=0, concat_axis=0, tiled=True)
    row_recv = lax.all_to_all(row_send, "seq", split_axis=0, concat_axis=0, tiled=True)

    row_index = jnp.clip(row_recv, 0, rows_here - 1)
    query_heads = pair_recv[:, 0]
    grad_heads = pair_recv[:, 1]
    key_heads = jnp.swapaxes(split_heads(row_keys), 1, 2)[row_index]
    value_heads = jnp.swapaxes(split_heads(row_values), 1, 2)[row_index]

    scores = (
        jnp.einsum("bhid,bhjd->bhij", query_heads, key_heads, preferred_element_type=jnp.float32)
        * score_scale
    )
    grad_p = jnp.einsum(
        "bhid,bhjd->bhij", grad_heads, value_heads, preferred_element_type=jnp.float32
    )
    highest = jnp.max(scores, axis=3)
    expons = jnp.exp(scores - highest[..., None])
    part = jnp.stack(
        [highest, jnp.sum(expons, axis=3), jnp.sum(expons * grad_p, axis=3)], axis=1
    ).reshape(slot_total, 3, heads_here * SPAN)
    back = lax.all_to_all(part, "seq", split_axis=0, concat_axis=0, tiled=True)

    item_part = back[target].reshape(span_count, NBR, 3, heads_here * SPAN)
    item_max = item_part[:, :, 0]
    item_sum = item_part[:, :, 1]
    item_cross = item_part[:, :, 2]
    span_max = jnp.max(item_max, axis=1, keepdims=True)
    factor = jnp.exp(item_max - span_max)
    span_sum = jnp.sum(item_sum * factor, axis=1)
    log_total = span_max[:, 0] + jnp.log(span_sum)
    row_delta = jnp.sum(item_cross * factor, axis=1) / span_sum
    span_stats = jnp.stack([log_total, row_delta], axis=1)
    stats_recv = lax.all_to_all(
        span_stats[slot_span], "seq", split_axis=0, concat_axis=0, tiled=True
    )

    norm_here = stats_recv[:, 0].reshape(slot_total, heads_here, SPAN)
    delta_here = stats_recv[:, 1].reshape(slot_total, heads_here, SPAN)
    softmax_p = jnp.exp(scores - norm_here[..., None])
    grad_s = (softmax_p * (grad_p - delta_here[..., None]) * score_scale).astype(jnp.bfloat16)
    probs_low = softmax_p.astype(jnp.bfloat16)
    query_part = jnp.einsum(
        "bhij,bhjd->bhid", grad_s, key_heads, preferred_element_type=jnp.float32
    ).astype(jnp.bfloat16)
    if seq_count <= 8:
        query_back = seq_exchange(
            query_part.reshape((seq_count, slot_depth) + query_part.shape[1:]), seq_count
        ).reshape(query_part.shape)
    else:
        query_back = lax.all_to_all(query_part, "seq", split_axis=0, concat_axis=0, tiled=True)

    key_grad, value_grad = kv_grads(row_recv, probs_low, grad_s, pair_recv, rows_here)

    query_grad = sum_parts(target, query_back)
    return (query_grad, key_grad, value_grad)


def solution(mesh):
    in_specs = (
        P("seq", None, "mp"),
        P("seq", None, "mp"),
        P("seq", None, "mp"),
        P("seq", None, "mp"),
        P(("seq", "mp"), None),
    )
    out_specs = (P("seq", None, "mp"), P("seq", None, "mp"), P("seq", None, "mp"))
    return jax.shard_map(
        per_device, mesh=mesh, in_specs=in_specs, out_specs=out_specs, check_vma=False
    )
```

```python
import jax
import jax.numpy as jnp
from jax import lax
from jax.experimental import pallas as pl
from jax.experimental.pallas import tpu as pltpu
from jax.sharding import PartitionSpec as P

HEAD = 128
SPAN = 64
NLEN = 128
NBR = 2

TRANS_A = (((0,), (0,)), ((), ()))


def split_heads(tensor):
    return tensor.reshape(tensor.shape[:-1] + (tensor.shape[-1] // HEAD, HEAD))


def kv_kernel(rows_ref, probs_ref, grads_ref, pair_ref, key_out, value_out, key_acc, value_acc):
    slot = pl.program_id(0)
    heads = probs_ref.shape[1]

    @pl.when(slot == 0)
    def _():
        key_acc[...] = jnp.zeros_like(key_acc)
        value_acc[...] = jnp.zeros_like(value_acc)

    row = rows_ref[slot]

    @pl.when(row >= 0)
    def _():
        here = jnp.maximum(row, 0)
        for h in range(heads):
            cols = pl.ds(h * HEAD, HEAD)
            value_part = lax.dot_general(
                probs_ref[0, h], pair_ref[0, 1, h], TRANS_A,
                preferred_element_type=jnp.float32,
            )
            key_part = lax.dot_general(
                grads_ref[0, h], pair_ref[0, 0, h], TRANS_A,
                preferred_element_type=jnp.float32,
            )
            value_acc[here, :, cols] += value_part
            key_acc[here, :, cols] += key_part

    @pl.when(slot == pl.num_programs(0) - 1)
    def _():
        key_out[...] = key_acc[...].astype(key_out.dtype)
        value_out[...] = value_acc[...].astype(value_out.dtype)


def kv_grads(row_recv, probs_low, grad_s, pair_recv, rows_here):
    slot_total, heads, span_len, nlen = probs_low.shape
    width = heads * HEAD
    out_shape = jax.ShapeDtypeStruct((rows_here, nlen, width), jnp.bfloat16)
    grid_spec = pltpu.PrefetchScalarGridSpec(
        num_scalar_prefetch=1,
        grid=(slot_total,),
        in_specs=[
            pl.BlockSpec((1, heads, span_len, nlen), lambda t, rows: (t, 0, 0, 0)),
            pl.BlockSpec((1, heads, span_len, nlen), lambda t, rows: (t, 0, 0, 0)),
            pl.BlockSpec((1, 2, heads, span_len, HEAD), lambda t, rows: (t, 0, 0, 0, 0)),
        ],
        out_specs=[
            pl.BlockSpec((rows_here, nlen, width), lambda t, rows: (0, 0, 0)),
            pl.BlockSpec((rows_here, nlen, width), lambda t, rows: (0, 0, 0)),
        ],
        scratch_shapes=[
            pltpu.VMEM((rows_here, nlen, width), jnp.float32),
            pltpu.VMEM((rows_here, nlen, width), jnp.float32),
        ],
    )
    return pl.pallas_call(
        kv_kernel,
        grid_spec=grid_spec,
        out_shape=[out_shape, out_shape],
        compiler_params=pltpu.CompilerParams(
            dimension_semantics=("arbitrary",), vmem_limit_bytes=48 * 1024 * 1024
        ),
    )(row_recv, probs_low, grad_s, pair_recv)


def pair_kernel(span_ref, query_ref, grad_ref, pair_out):
    heads = pair_out.shape[2]

    def body(t, carry):
        source = span_ref[t]
        for h in range(heads):
            cols = pl.ds(h * HEAD, HEAD)
            pair_out[t, 0, h] = query_ref[source, :, cols]
            pair_out[t, 1, h] = grad_ref[source, :, cols]
        return carry

    lax.fori_loop(0, pair_out.shape[0], body, 0)


def gather_pairs(slot_span, queries, out_grad):
    span_count, span_len, width = queries.shape
    slot_total = slot_span.shape[0]
    heads = width // HEAD
    pair_shape = (slot_total, 2, heads, span_len, HEAD)
    grid_spec = pltpu.PrefetchScalarGridSpec(
        num_scalar_prefetch=1,
        grid=(1,),
        in_specs=[
            pl.BlockSpec((span_count, span_len, width), lambda i, spans: (0, 0, 0)),
            pl.BlockSpec((span_count, span_len, width), lambda i, spans: (0, 0, 0)),
        ],
        out_specs=pl.BlockSpec(pair_shape, lambda i, spans: (0, 0, 0, 0, 0)),
    )
    return pl.pallas_call(
        pair_kernel,
        grid_spec=grid_spec,
        out_shape=jax.ShapeDtypeStruct(pair_shape, queries.dtype),
        compiler_params=pltpu.CompilerParams(vmem_limit_bytes=48 * 1024 * 1024),
    )(jnp.clip(slot_span, 0, span_count - 1), queries, out_grad)


def sum_kernel(target_ref, back_ref, query_out):
    heads = back_ref.shape[1]

    def body(c, carry):
        first_slot = target_ref[c * NBR]
        second_slot = target_ref[c * NBR + 1]
        for h in range(heads):
            first = back_ref[first_slot, h].astype(jnp.float32)
            second = back_ref[second_slot, h].astype(jnp.float32)
            query_out[c, :, pl.ds(h * HEAD, HEAD)] = (first + second).astype(query_out.dtype)
        return carry

    lax.fori_loop(0, query_out.shape[0], body, 0)


def sum_parts(target, query_back):
    slot_total, heads, span_len, _ = query_back.shape
    width = heads * HEAD
    span_count = target.shape[0] // NBR
    grid_spec = pltpu.PrefetchScalarGridSpec(
        num_scalar_prefetch=1,
        grid=(1,),
        in_specs=[pl.BlockSpec(query_back.shape, lambda i, tgt: (0, 0, 0, 0))],
        out_specs=pl.BlockSpec((span_count, span_len, width), lambda i, tgt: (0, 0, 0)),
    )
    return pl.pallas_call(
        sum_kernel,
        grid_spec=grid_spec,
        out_shape=jax.ShapeDtypeStruct((span_count, span_len, width), query_back.dtype),
        compiler_params=pltpu.CompilerParams(vmem_limit_bytes=48 * 1024 * 1024),
    )(jnp.clip(target, 0, slot_total - 1), query_back)


def seq_exchange(blocks, seq_count):
    me = lax.axis_index("seq")
    result = jnp.zeros_like(blocks)
    result = lax.dynamic_update_index_in_dim(
        result, lax.dynamic_index_in_dim(blocks, me, keepdims=False), me, axis=0
    )
    for shift in range(1, seq_count):
        sent = lax.ppermute(
            lax.dynamic_index_in_dim(blocks, (me + shift) % seq_count, keepdims=False),
            "seq",
            perm=[(i, (i + shift) % seq_count) for i in range(seq_count)],
        )
        result = lax.dynamic_update_index_in_dim(
            result, sent, (me - shift) % seq_count, axis=0
        )
    return result


def per_device(queries, out_grad, row_keys, row_values, neighbours):
    seq_count = lax.axis_size("seq")
    own_lists = lax.all_gather(neighbours, "mp", axis=0, tiled=True)
    span_count = queries.shape[0]
    rows_here = row_keys.shape[0]
    width_here = queries.shape[2]
    heads_here = width_here // HEAD
    flat_rows = own_lists.reshape(-1)
    item_count = flat_rows.shape[0]
    owner_dev = flat_rows // rows_here
    local_row = flat_rows % rows_here
    slot_depth = (item_count + seq_count - 1) // seq_count
    slot_total = seq_count * slot_depth
    position = jnp.arange(item_count)
    same_before = (owner_dev[:, None] == owner_dev[None, :]) & (
        position[None, :] < position[:, None]
    )
    earlier = jnp.sum(same_before.astype(jnp.int32), axis=1)
    target = owner_dev * slot_depth + earlier
    item_span = position // NBR
    score_scale = HEAD ** (-0.5)

    match = target[None, :] == jnp.arange(slot_total)[:, None]
    slot_valid = jnp.any(match, axis=1)
    slot_item = jnp.sum(jnp.where(match, position[None, :], 0), axis=1)
    slot_span = item_span[slot_item]

    pair_send = gather_pairs(slot_span, queries, out_grad)
    row_send = jnp.where(slot_valid, local_row[slot_item], -1)
    if seq_count <= 8:
        pair_recv = seq_exchange(
            pair_send.reshape((seq_count, slot_depth) + pair_send.shape[1:]), seq_count
        ).reshape(pair_send.shape)
    else:
        pair_recv = lax.all_to_all(pair_send, "seq", split_axis=0, concat_axis=0, tiled=True)
    row_recv = lax.all_to_all(row_send, "seq", split_axis=0, concat_axis=0, tiled=True)

    row_index = jnp.clip(row_recv, 0, rows_here - 1)
    query_heads = pair_recv[:, 0]
    grad_heads = pair_recv[:, 1]
    key_heads = jnp.swapaxes(split_heads(row_keys), 1, 2)[row_index]
    value_heads = jnp.swapaxes(split_heads(row_values), 1, 2)[row_index]

    scores = (
        jnp.einsum("bhid,bhjd->bhij", query_heads, key_heads, preferred_element_type=jnp.float32)
        * score_scale
    )
    grad_p = jnp.einsum(
        "bhid,bhjd->bhij", grad_heads, value_heads, preferred_element_type=jnp.float32
    )
    highest = jnp.max(scores, axis=3)
    expons = jnp.exp(scores - highest[..., None])
    part = jnp.stack(
        [highest, jnp.sum(expons, axis=3), jnp.sum(expons * grad_p, axis=3)], axis=1
    ).reshape(slot_total, 3, heads_here * SPAN)
    back = lax.all_to_all(part, "seq", split_axis=0, concat_axis=0, tiled=True)

    item_part = back[target].reshape(span_count, NBR, 3, heads_here * SPAN)
    item_max = item_part[:, :, 0]
    item_sum = item_part[:, :, 1]
    item_cross = item_part[:, :, 2]
    span_max = jnp.max(item_max, axis=1, keepdims=True)
    factor = jnp.exp(item_max - span_max)
    span_sum = jnp.sum(item_sum * factor, axis=1)
    log_total = span_max[:, 0] + jnp.log(span_sum)
    row_delta = jnp.sum(item_cross * factor, axis=1) / span_sum
    span_stats = jnp.stack([log_total, row_delta], axis=1)
    stats_recv = lax.all_to_all(
        span_stats[slot_span], "seq", split_axis=0, concat_axis=0, tiled=True
    )

    norm_here = stats_recv[:, 0].reshape(slot_total, heads_here, SPAN)
    delta_here = stats_recv[:, 1].reshape(slot_total, heads_here, SPAN)
    softmax_p = jnp.exp(scores - norm_here[..., None])
    grad_s = (softmax_p * (grad_p - delta_here[..., None]) * score_scale).astype(jnp.bfloat16)
    probs_low = softmax_p.astype(jnp.bfloat16)
    query_part = jnp.einsum(
        "bhij,bhjd->bhid", grad_s, key_heads, preferred_element_type=jnp.float32
    ).astype(jnp.bfloat16)
    if seq_count <= 8:
        query_back = seq_exchange(
            query_part.reshape((seq_count, slot_depth) + query_part.shape[1:]), seq_count
        ).reshape(query_part.shape)
    else:
        query_back = lax.all_to_all(query_part, "seq", split_axis=0, concat_axis=0, tiled=True)

    key_grad, value_grad = kv_grads(row_recv, probs_low, grad_s, pair_recv, rows_here)

    query_grad = sum_parts(target, query_back)
    return (query_grad, key_grad, value_grad)


def solution(mesh):
    in_specs = (
        P("seq", None, "mp"),
        P("seq", None, "mp"),
        P("seq", None, "mp"),
        P("seq", None, "mp"),
        P(("seq", "mp"), None),
    )
    out_specs = (P("seq", None, "mp"), P("seq", None, "mp"), P("seq", None, "mp"))
    return jax.shard_map(
        per_device, mesh=mesh, in_specs=in_specs, out_specs=out_specs, check_vma=False
    )
```

```python
import jax
import jax.numpy as jnp
from jax import lax
from jax.experimental import pallas as pl
from jax.experimental.pallas import tpu as pltpu
from jax.sharding import PartitionSpec as P

HEAD = 128
SPAN = 64
NLEN = 128
NBR = 2

TRANS_A = (((0,), (0,)), ((), ()))


def split_heads(tensor):
    return tensor.reshape(tensor.shape[:-1] + (tensor.shape[-1] // HEAD, HEAD))


def kv_kernel(rows_ref, probs_ref, grads_ref, pair_ref, key_out, value_out, key_acc, value_acc):
    slot = pl.program_id(0)
    heads = probs_ref.shape[1]

    @pl.when(slot == 0)
    def _():
        key_acc[...] = jnp.zeros_like(key_acc)
        value_acc[...] = jnp.zeros_like(value_acc)

    row = rows_ref[slot]

    @pl.when(row >= 0)
    def _():
        here = jnp.maximum(row, 0)
        for h in range(heads):
            cols = pl.ds(h * HEAD, HEAD)
            value_part = lax.dot_general(
                probs_ref[0, h], pair_ref[0, 1, h], TRANS_A,
                preferred_element_type=jnp.float32,
            )
            key_part = lax.dot_general(
                grads_ref[0, h], pair_ref[0, 0, h], TRANS_A,
                preferred_element_type=jnp.float32,
            )
            value_acc[here, :, cols] += value_part
            key_acc[here, :, cols] += key_part

    @pl.when(slot == pl.num_programs(0) - 1)
    def _():
        key_out[...] = key_acc[...].astype(key_out.dtype)
        value_out[...] = value_acc[...].astype(value_out.dtype)


def kv_grads(row_recv, probs_low, grad_s, pair_recv, rows_here):
    slot_total, heads, span_len, nlen = probs_low.shape
    width = heads * HEAD
    out_shape = jax.ShapeDtypeStruct((rows_here, nlen, width), jnp.bfloat16)
    grid_spec = pltpu.PrefetchScalarGridSpec(
        num_scalar_prefetch=1,
        grid=(slot_total,),
        in_specs=[
            pl.BlockSpec((1, heads, span_len, nlen), lambda t, rows: (t, 0, 0, 0)),
            pl.BlockSpec((1, heads, span_len, nlen), lambda t, rows: (t, 0, 0, 0)),
            pl.BlockSpec((1, 2, heads, span_len, HEAD), lambda t, rows: (t, 0, 0, 0, 0)),
        ],
        out_specs=[
            pl.BlockSpec((rows_here, nlen, width), lambda t, rows: (0, 0, 0)),
            pl.BlockSpec((rows_here, nlen, width), lambda t, rows: (0, 0, 0)),
        ],
        scratch_shapes=[
            pltpu.VMEM((rows_here, nlen, width), jnp.float32),
            pltpu.VMEM((rows_here, nlen, width), jnp.float32),
        ],
    )
    return pl.pallas_call(
        kv_kernel,
        grid_spec=grid_spec,
        out_shape=[out_shape, out_shape],
        compiler_params=pltpu.CompilerParams(
            dimension_semantics=("arbitrary",), vmem_limit_bytes=48 * 1024 * 1024
        ),
    )(row_recv, probs_low, grad_s, pair_recv)


def pair_kernel(span_ref, query_ref, grad_ref, pair_out):
    heads = pair_out.shape[2]

    def body(t, carry):
        source = span_ref[t]
        for h in range(heads):
            cols = pl.ds(h * HEAD, HEAD)
            pair_out[t, 0, h] = query_ref[source, :, cols]
            pair_out[t, 1, h] = grad_ref[source, :, cols]
        return carry

    lax.fori_loop(0, pair_out.shape[0], body, 0)


def gather_pairs(slot_span, queries, out_grad):
    span_count, span_len, width = queries.shape
    slot_total = slot_span.shape[0]
    heads = width // HEAD
    pair_shape = (slot_total, 2, heads, span_len, HEAD)
    grid_spec = pltpu.PrefetchScalarGridSpec(
        num_scalar_prefetch=1,
        grid=(1,),
        in_specs=[
            pl.BlockSpec((span_count, span_len, width), lambda i, spans: (0, 0, 0)),
            pl.BlockSpec((span_count, span_len, width), lambda i, spans: (0, 0, 0)),
        ],
        out_specs=pl.BlockSpec(pair_shape, lambda i, spans: (0, 0, 0, 0, 0)),
    )
    return pl.pallas_call(
        pair_kernel,
        grid_spec=grid_spec,
        out_shape=jax.ShapeDtypeStruct(pair_shape, queries.dtype),
        compiler_params=pltpu.CompilerParams(vmem_limit_bytes=48 * 1024 * 1024),
    )(jnp.clip(slot_span, 0, span_count - 1), queries, out_grad)


def sum_kernel(target_ref, back_ref, query_out):
    heads = back_ref.shape[1]

    def body(c, carry):
        first_slot = target_ref[c * NBR]
        second_slot = target_ref[c * NBR + 1]
        for h in range(heads):
            first = back_ref[first_slot, h].astype(jnp.float32)
            second = back_ref[second_slot, h].astype(jnp.float32)
            query_out[c, :, pl.ds(h * HEAD, HEAD)] = (first + second).astype(query_out.dtype)
        return carry

    lax.fori_loop(0, query_out.shape[0], body, 0)


def sum_parts(target, query_back):
    slot_total, heads, span_len, _ = query_back.shape
    width = heads * HEAD
    span_count = target.shape[0] // NBR
    grid_spec = pltpu.PrefetchScalarGridSpec(
        num_scalar_prefetch=1,
        grid=(1,),
        in_specs=[pl.BlockSpec(query_back.shape, lambda i, tgt: (0, 0, 0, 0))],
        out_specs=pl.BlockSpec((span_count, span_len, width), lambda i, tgt: (0, 0, 0)),
    )
    return pl.pallas_call(
        sum_kernel,
        grid_spec=grid_spec,
        out_shape=jax.ShapeDtypeStruct((span_count, span_len, width), query_back.dtype),
        compiler_params=pltpu.CompilerParams(vmem_limit_bytes=48 * 1024 * 1024),
    )(jnp.clip(target, 0, slot_total - 1), query_back)


def seq_exchange(blocks, seq_count):
    me = lax.axis_index("seq")
    result = jnp.zeros_like(blocks)
    result = lax.dynamic_update_index_in_dim(
        result, lax.dynamic_index_in_dim(blocks, me, keepdims=False), me, axis=0
    )
    shifts = []
    for low in range(1, seq_count // 2 + 1):
        for shift in (low, seq_count - low):
            if shift not in shifts and 0 < shift < seq_count:
                shifts.append(shift)
    for shift in shifts:
        sent = lax.ppermute(
            lax.dynamic_index_in_dim(blocks, (me + shift) % seq_count, keepdims=False),
            "seq",
            perm=[(i, (i + shift) % seq_count) for i in range(seq_count)],
        )
        result = lax.dynamic_update_index_in_dim(
            result, sent, (me - shift) % seq_count, axis=0
        )
    return result


def per_device(queries, out_grad, row_keys, row_values, neighbours):
    seq_count = lax.axis_size("seq")
    own_lists = lax.all_gather(neighbours, "mp", axis=0, tiled=True)
    span_count = queries.shape[0]
    rows_here = row_keys.shape[0]
    width_here = queries.shape[2]
    heads_here = width_here // HEAD
    flat_rows = own_lists.reshape(-1)
    item_count = flat_rows.shape[0]
    owner_dev = flat_rows // rows_here
    local_row = flat_rows % rows_here
    slot_depth = (item_count + seq_count - 1) // seq_count
    slot_total = seq_count * slot_depth
    position = jnp.arange(item_count)
    same_before = (owner_dev[:, None] == owner_dev[None, :]) & (
        position[None, :] < position[:, None]
    )
    earlier = jnp.sum(same_before.astype(jnp.int32), axis=1)
    target = owner_dev * slot_depth + earlier
    item_span = position // NBR
    score_scale = HEAD ** (-0.5)

    match = target[None, :] == jnp.arange(slot_total)[:, None]
    slot_valid = jnp.any(match, axis=1)
    slot_item = jnp.sum(jnp.where(match, position[None, :], 0), axis=1)
    slot_span = item_span[slot_item]

    pair_send = gather_pairs(slot_span, queries, out_grad)
    row_send = jnp.where(slot_valid, local_row[slot_item], -1)
    if seq_count <= 8:
        pair_recv = seq_exchange(
            pair_send.reshape((seq_count, slot_depth) + pair_send.shape[1:]), seq_count
        ).reshape(pair_send.shape)
    else:
        pair_recv = lax.all_to_all(pair_send, "seq", split_axis=0, concat_axis=0, tiled=True)
    row_recv = lax.all_to_all(row_send, "seq", split_axis=0, concat_axis=0, tiled=True)

    row_index = jnp.clip(row_recv, 0, rows_here - 1)
    query_heads = pair_recv[:, 0]
    grad_heads = pair_recv[:, 1]
    key_heads = jnp.swapaxes(split_heads(row_keys), 1, 2)[row_index]
    value_heads = jnp.swapaxes(split_heads(row_values), 1, 2)[row_index]

    scores = (
        jnp.einsum("bhid,bhjd->bhij", query_heads, key_heads, preferred_element_type=jnp.float32)
        * score_scale
    )
    grad_p = jnp.einsum(
        "bhid,bhjd->bhij", grad_heads, value_heads, preferred_element_type=jnp.float32
    )
    highest = jnp.max(scores, axis=3)
    expons = jnp.exp(scores - highest[..., None])
    part = jnp.stack(
        [highest, jnp.sum(expons, axis=3), jnp.sum(expons * grad_p, axis=3)], axis=1
    ).reshape(slot_total, 3, heads_here * SPAN)
    back = lax.all_to_all(part, "seq", split_axis=0, concat_axis=0, tiled=True)

    item_part = back[target].reshape(span_count, NBR, 3, heads_here * SPAN)
    item_max = item_part[:, :, 0]
    item_sum = item_part[:, :, 1]
    item_cross = item_part[:, :, 2]
    span_max = jnp.max(item_max, axis=1, keepdims=True)
    factor = jnp.exp(item_max - span_max)
    span_sum = jnp.sum(item_sum * factor, axis=1)
    log_total = span_max[:, 0] + jnp.log(span_sum)
    row_delta = jnp.sum(item_cross * factor, axis=1) / span_sum
    span_stats = jnp.stack([log_total, row_delta], axis=1)
    stats_recv = lax.all_to_all(
        span_stats[slot_span], "seq", split_axis=0, concat_axis=0, tiled=True
    )

    norm_here = stats_recv[:, 0].reshape(slot_total, heads_here, SPAN)
    delta_here = stats_recv[:, 1].reshape(slot_total, heads_here, SPAN)
    softmax_p = jnp.exp(scores - norm_here[..., None])
    grad_s = (softmax_p * (grad_p - delta_here[..., None]) * score_scale).astype(jnp.bfloat16)
    probs_low = softmax_p.astype(jnp.bfloat16)
    query_part = jnp.einsum(
        "bhij,bhjd->bhid", grad_s, key_heads, preferred_element_type=jnp.float32
    ).astype(jnp.bfloat16)
    if seq_count <= 8:
        query_back = seq_exchange(
            query_part.reshape((seq_count, slot_depth) + query_part.shape[1:]), seq_count
        ).reshape(query_part.shape)
    else:
        query_back = lax.all_to_all(query_part, "seq", split_axis=0, concat_axis=0, tiled=True)

    key_grad, value_grad = kv_grads(row_recv, probs_low, grad_s, pair_recv, rows_here)

    query_grad = sum_parts(target, query_back)
    return (query_grad, key_grad, value_grad)


def solution(mesh):
    in_specs = (
        P("seq", None, "mp"),
        P("seq", None, "mp"),
        P("seq", None, "mp"),
        P("seq", None, "mp"),
        P(("seq", "mp"), None),
    )
    out_specs = (P("seq", None, "mp"), P("seq", None, "mp"), P("seq", None, "mp"))
    return jax.shard_map(
        per_device, mesh=mesh, in_specs=in_specs, out_specs=out_specs, check_vma=False
    )
```

```python
import jax
import jax.numpy as jnp
from jax import lax
from jax.experimental import pallas as pl
from jax.experimental.pallas import tpu as pltpu
from jax.sharding import PartitionSpec as P

HEAD = 128
SPAN = 64
NLEN = 128
NBR = 2

TRANS_A = (((0,), (0,)), ((), ()))


def split_heads(tensor):
    return tensor.reshape(tensor.shape[:-1] + (tensor.shape[-1] // HEAD, HEAD))


def kv_kernel(rows_ref, probs_ref, grads_ref, pair_ref, key_out, value_out, key_acc, value_acc):
    slot = pl.program_id(0)
    heads = probs_ref.shape[1]

    @pl.when(slot == 0)
    def _():
        key_acc[...] = jnp.zeros_like(key_acc)
        value_acc[...] = jnp.zeros_like(value_acc)

    row = rows_ref[slot]

    @pl.when(row >= 0)
    def _():
        here = jnp.maximum(row, 0)
        for h in range(heads):
            cols = pl.ds(h * HEAD, HEAD)
            value_part = lax.dot_general(
                probs_ref[0, h], pair_ref[0, 1, h], TRANS_A,
                preferred_element_type=jnp.float32,
            )
            key_part = lax.dot_general(
                grads_ref[0, h], pair_ref[0, 0, h], TRANS_A,
                preferred_element_type=jnp.float32,
            )
            value_acc[here, :, cols] += value_part
            key_acc[here, :, cols] += key_part

    @pl.when(slot == pl.num_programs(0) - 1)
    def _():
        key_out[...] = key_acc[...].astype(key_out.dtype)
        value_out[...] = value_acc[...].astype(value_out.dtype)


def kv_grads(row_recv, probs_low, grad_s, pair_recv, rows_here):
    slot_total, heads, span_len, nlen = probs_low.shape
    width = heads * HEAD
    out_shape = jax.ShapeDtypeStruct((rows_here, nlen, width), jnp.bfloat16)
    grid_spec = pltpu.PrefetchScalarGridSpec(
        num_scalar_prefetch=1,
        grid=(slot_total,),
        in_specs=[
            pl.BlockSpec((1, heads, span_len, nlen), lambda t, rows: (t, 0, 0, 0)),
            pl.BlockSpec((1, heads, span_len, nlen), lambda t, rows: (t, 0, 0, 0)),
            pl.BlockSpec((1, 2, heads, span_len, HEAD), lambda t, rows: (t, 0, 0, 0, 0)),
        ],
        out_specs=[
            pl.BlockSpec((rows_here, nlen, width), lambda t, rows: (0, 0, 0)),
            pl.BlockSpec((rows_here, nlen, width), lambda t, rows: (0, 0, 0)),
        ],
        scratch_shapes=[
            pltpu.VMEM((rows_here, nlen, width), jnp.float32),
            pltpu.VMEM((rows_here, nlen, width), jnp.float32),
        ],
    )
    return pl.pallas_call(
        kv_kernel,
        grid_spec=grid_spec,
        out_shape=[out_shape, out_shape],
        compiler_params=pltpu.CompilerParams(
            dimension_semantics=("arbitrary",), vmem_limit_bytes=48 * 1024 * 1024
        ),
    )(row_recv, probs_low, grad_s, pair_recv)


def pair_kernel(span_ref, query_ref, grad_ref, pair_out):
    heads = pair_out.shape[2]

    def body(t, carry):
        source = span_ref[t]
        for h in range(heads):
            cols = pl.ds(h * HEAD, HEAD)
            pair_out[t, 0, h] = query_ref[source, :, cols]
            pair_out[t, 1, h] = grad_ref[source, :, cols]
        return carry

    lax.fori_loop(0, pair_out.shape[0], body, 0)


def gather_pairs(slot_span, queries, out_grad):
    span_count, span_len, width = queries.shape
    slot_total = slot_span.shape[0]
    heads = width // HEAD
    pair_shape = (slot_total, 2, heads, span_len, HEAD)
    grid_spec = pltpu.PrefetchScalarGridSpec(
        num_scalar_prefetch=1,
        grid=(1,),
        in_specs=[
            pl.BlockSpec((span_count, span_len, width), lambda i, spans: (0, 0, 0)),
            pl.BlockSpec((span_count, span_len, width), lambda i, spans: (0, 0, 0)),
        ],
        out_specs=pl.BlockSpec(pair_shape, lambda i, spans: (0, 0, 0, 0, 0)),
    )
    return pl.pallas_call(
        pair_kernel,
        grid_spec=grid_spec,
        out_shape=jax.ShapeDtypeStruct(pair_shape, queries.dtype),
        compiler_params=pltpu.CompilerParams(vmem_limit_bytes=48 * 1024 * 1024),
    )(jnp.clip(slot_span, 0, span_count - 1), queries, out_grad)


def sum_kernel(target_ref, back_ref, query_out):
    heads = back_ref.shape[1]

    def body(c, carry):
        first_slot = target_ref[c * NBR]
        second_slot = target_ref[c * NBR + 1]
        for h in range(heads):
            first = back_ref[first_slot, h].astype(jnp.float32)
            second = back_ref[second_slot, h].astype(jnp.float32)
            query_out[c, :, pl.ds(h * HEAD, HEAD)] = (first + second).astype(query_out.dtype)
        return carry

    lax.fori_loop(0, query_out.shape[0], body, 0)


def sum_parts(target, query_back):
    slot_total, heads, span_len, _ = query_back.shape
    width = heads * HEAD
    span_count = target.shape[0] // NBR
    grid_spec = pltpu.PrefetchScalarGridSpec(
        num_scalar_prefetch=1,
        grid=(1,),
        in_specs=[pl.BlockSpec(query_back.shape, lambda i, tgt: (0, 0, 0, 0))],
        out_specs=pl.BlockSpec((span_count, span_len, width), lambda i, tgt: (0, 0, 0)),
    )
    return pl.pallas_call(
        sum_kernel,
        grid_spec=grid_spec,
        out_shape=jax.ShapeDtypeStruct((span_count, span_len, width), query_back.dtype),
        compiler_params=pltpu.CompilerParams(vmem_limit_bytes=48 * 1024 * 1024),
    )(jnp.clip(target, 0, slot_total - 1), query_back)


def gather_over(block, axis_name, axis_count):
    me = lax.axis_index(axis_name)
    result = jnp.zeros((axis_count,) + block.shape, block.dtype)
    result = lax.dynamic_update_index_in_dim(result, block, me, axis=0)
    for shift in range(1, axis_count):
        sent = lax.ppermute(
            block, axis_name, perm=[(i, (i + shift) % axis_count) for i in range(axis_count)]
        )
        result = lax.dynamic_update_index_in_dim(result, sent, (me - shift) % axis_count, axis=0)
    return result


def seq_exchange(blocks, seq_count):
    me = lax.axis_index("seq")
    result = jnp.zeros_like(blocks)
    result = lax.dynamic_update_index_in_dim(
        result, lax.dynamic_index_in_dim(blocks, me, keepdims=False), me, axis=0
    )
    for shift in range(1, seq_count):
        sent = lax.ppermute(
            lax.dynamic_index_in_dim(blocks, (me + shift) % seq_count, keepdims=False),
            "seq",
            perm=[(i, (i + shift) % seq_count) for i in range(seq_count)],
        )
        result = lax.dynamic_update_index_in_dim(
            result, sent, (me - shift) % seq_count, axis=0
        )
    return result


def per_device(queries, out_grad, row_keys, row_values, neighbours):
    seq_count = lax.axis_size("seq")
    own_lists = gather_over(neighbours, "mp", lax.axis_size("mp")).reshape(
        (-1,) + neighbours.shape[1:]
    )
    span_count = queries.shape[0]
    rows_here = row_keys.shape[0]
    width_here = queries.shape[2]
    heads_here = width_here // HEAD
    flat_rows = own_lists.reshape(-1)
    item_count = flat_rows.shape[0]
    owner_dev = flat_rows // rows_here
    local_row = flat_rows % rows_here
    slot_depth = (item_count + seq_count - 1) // seq_count
    slot_total = seq_count * slot_depth
    position = jnp.arange(item_count)
    same_before = (owner_dev[:, None] == owner_dev[None, :]) & (
        position[None, :] < position[:, None]
    )
    earlier = jnp.sum(same_before.astype(jnp.int32), axis=1)
    target = owner_dev * slot_depth + earlier
    item_span = position // NBR
    score_scale = HEAD ** (-0.5)

    match = target[None, :] == jnp.arange(slot_total)[:, None]
    slot_valid = jnp.any(match, axis=1)
    slot_item = jnp.sum(jnp.where(match, position[None, :], 0), axis=1)
    slot_span = item_span[slot_item]

    pair_send = gather_pairs(slot_span, queries, out_grad)
    row_send = jnp.where(slot_valid, local_row[slot_item], -1)
    pair_recv = lax.all_to_all(pair_send, "seq", split_axis=0, concat_axis=0, tiled=True)
    row_recv = lax.all_to_all(row_send, "seq", split_axis=0, concat_axis=0, tiled=True)

    row_index = jnp.clip(row_recv, 0, rows_here - 1)
    query_heads = pair_recv[:, 0]
    grad_heads = pair_recv[:, 1]
    key_heads = jnp.swapaxes(split_heads(row_keys), 1, 2)[row_index]
    value_heads = jnp.swapaxes(split_heads(row_values), 1, 2)[row_index]

    scores = (
        jnp.einsum("bhid,bhjd->bhij", query_heads, key_heads, preferred_element_type=jnp.float32)
        * score_scale
    )
    grad_p = jnp.einsum(
        "bhid,bhjd->bhij", grad_heads, value_heads, preferred_element_type=jnp.float32
    )
    highest = jnp.max(scores, axis=3)
    expons = jnp.exp(scores - highest[..., None])
    part = jnp.stack(
        [highest, jnp.sum(expons, axis=3), jnp.sum(expons * grad_p, axis=3)], axis=1
    ).reshape(slot_total, 3, heads_here * SPAN)
    back = lax.all_to_all(part, "seq", split_axis=0, concat_axis=0, tiled=True)

    item_part = back[target].reshape(span_count, NBR, 3, heads_here * SPAN)
    item_max = item_part[:, :, 0]
    item_sum = item_part[:, :, 1]
    item_cross = item_part[:, :, 2]
    span_max = jnp.max(item_max, axis=1, keepdims=True)
    factor = jnp.exp(item_max - span_max)
    span_sum = jnp.sum(item_sum * factor, axis=1)
    log_total = span_max[:, 0] + jnp.log(span_sum)
    row_delta = jnp.sum(item_cross * factor, axis=1) / span_sum
    span_stats = jnp.stack([log_total, row_delta], axis=1)
    stats_recv = lax.all_to_all(
        span_stats[slot_span], "seq", split_axis=0, concat_axis=0, tiled=True
    )

    norm_here = stats_recv[:, 0].reshape(slot_total, heads_here, SPAN)
    delta_here = stats_recv[:, 1].reshape(slot_total, heads_here, SPAN)
    softmax_p = jnp.exp(scores - norm_here[..., None])
    grad_s = (softmax_p * (grad_p - delta_here[..., None]) * score_scale).astype(jnp.bfloat16)
    probs_low = softmax_p.astype(jnp.bfloat16)
    query_part = jnp.einsum(
        "bhij,bhjd->bhid", grad_s, key_heads, preferred_element_type=jnp.float32
    ).astype(jnp.bfloat16)
    if seq_count <= 8:
        query_back = seq_exchange(
            query_part.reshape((seq_count, slot_depth) + query_part.shape[1:]), seq_count
        ).reshape(query_part.shape)
    else:
        query_back = lax.all_to_all(query_part, "seq", split_axis=0, concat_axis=0, tiled=True)

    key_grad, value_grad = kv_grads(row_recv, probs_low, grad_s, pair_recv, rows_here)

    query_grad = sum_parts(target, query_back)
    return (query_grad, key_grad, value_grad)


def solution(mesh):
    in_specs = (
        P("seq", None, "mp"),
        P("seq", None, "mp"),
        P("seq", None, "mp"),
        P("seq", None, "mp"),
        P(("seq", "mp"), None),
    )
    out_specs = (P("seq", None, "mp"), P("seq", None, "mp"), P("seq", None, "mp"))
    return jax.shard_map(
        per_device, mesh=mesh, in_specs=in_specs, out_specs=out_specs, check_vma=False
    )
```

```python
import jax
import jax.numpy as jnp
from jax import lax
from jax.experimental import pallas as pl
from jax.experimental.pallas import tpu as pltpu
from jax.sharding import PartitionSpec as P

HEAD = 128
SPAN = 64
NLEN = 128
NBR = 2

TRANS_A = (((0,), (0,)), ((), ()))


def split_heads(tensor):
    return tensor.reshape(tensor.shape[:-1] + (tensor.shape[-1] // HEAD, HEAD))


def kv_kernel(rows_ref, probs_ref, grads_ref, pair_ref, key_out, value_out, key_acc, value_acc):
    slot = pl.program_id(0)
    heads = probs_ref.shape[1]

    @pl.when(slot == 0)
    def _():
        key_acc[...] = jnp.zeros_like(key_acc)
        value_acc[...] = jnp.zeros_like(value_acc)

    row = rows_ref[slot]

    @pl.when(row >= 0)
    def _():
        here = jnp.maximum(row, 0)
        for h in range(heads):
            cols = pl.ds(h * HEAD, HEAD)
            value_part = lax.dot_general(
                probs_ref[0, h], pair_ref[0, 1, h], TRANS_A,
                preferred_element_type=jnp.float32,
            )
            key_part = lax.dot_general(
                grads_ref[0, h], pair_ref[0, 0, h], TRANS_A,
                preferred_element_type=jnp.float32,
            )
            value_acc[here, :, cols] += value_part
            key_acc[here, :, cols] += key_part

    @pl.when(slot == pl.num_programs(0) - 1)
    def _():
        key_out[...] = key_acc[...].astype(key_out.dtype)
        value_out[...] = value_acc[...].astype(value_out.dtype)


def kv_grads(row_recv, probs_low, grad_s, pair_recv, rows_here):
    slot_total, heads, span_len, nlen = probs_low.shape
    width = heads * HEAD
    out_shape = jax.ShapeDtypeStruct((rows_here, nlen, width), jnp.bfloat16)
    grid_spec = pltpu.PrefetchScalarGridSpec(
        num_scalar_prefetch=1,
        grid=(slot_total,),
        in_specs=[
            pl.BlockSpec((1, heads, span_len, nlen), lambda t, rows: (t, 0, 0, 0)),
            pl.BlockSpec((1, heads, span_len, nlen), lambda t, rows: (t, 0, 0, 0)),
            pl.BlockSpec((1, 2, heads, span_len, HEAD), lambda t, rows: (t, 0, 0, 0, 0)),
        ],
        out_specs=[
            pl.BlockSpec((rows_here, nlen, width), lambda t, rows: (0, 0, 0)),
            pl.BlockSpec((rows_here, nlen, width), lambda t, rows: (0, 0, 0)),
        ],
        scratch_shapes=[
            pltpu.VMEM((rows_here, nlen, width), jnp.float32),
            pltpu.VMEM((rows_here, nlen, width), jnp.float32),
        ],
    )
    return pl.pallas_call(
        kv_kernel,
        grid_spec=grid_spec,
        out_shape=[out_shape, out_shape],
        compiler_params=pltpu.CompilerParams(
            dimension_semantics=("arbitrary",), vmem_limit_bytes=48 * 1024 * 1024
        ),
    )(row_recv, probs_low, grad_s, pair_recv)


def pair_kernel(span_ref, query_ref, grad_ref, pair_out):
    heads = pair_out.shape[2]

    def body(t, carry):
        source = span_ref[t]
        for h in range(heads):
            cols = pl.ds(h * HEAD, HEAD)
            pair_out[t, 0, h] = query_ref[source, :, cols]
            pair_out[t, 1, h] = grad_ref[source, :, cols]
        return carry

    lax.fori_loop(0, pair_out.shape[0], body, 0)


def gather_pairs(slot_span, queries, out_grad):
    span_count, span_len, width = queries.shape
    slot_total = slot_span.shape[0]
    heads = width // HEAD
    pair_shape = (slot_total, 2, heads, span_len, HEAD)
    grid_spec = pltpu.PrefetchScalarGridSpec(
        num_scalar_prefetch=1,
        grid=(1,),
        in_specs=[
            pl.BlockSpec((span_count, span_len, width), lambda i, spans: (0, 0, 0)),
            pl.BlockSpec((span_count, span_len, width), lambda i, spans: (0, 0, 0)),
        ],
        out_specs=pl.BlockSpec(pair_shape, lambda i, spans: (0, 0, 0, 0, 0)),
    )
    return pl.pallas_call(
        pair_kernel,
        grid_spec=grid_spec,
        out_shape=jax.ShapeDtypeStruct(pair_shape, queries.dtype),
        compiler_params=pltpu.CompilerParams(vmem_limit_bytes=48 * 1024 * 1024),
    )(jnp.clip(slot_span, 0, span_count - 1), queries, out_grad)


def sum_kernel(target_ref, back_ref, query_out):
    heads = back_ref.shape[1]

    def body(c, carry):
        first_slot = target_ref[c * NBR]
        second_slot = target_ref[c * NBR + 1]
        for h in range(heads):
            first = back_ref[first_slot, h].astype(jnp.float32)
            second = back_ref[second_slot, h].astype(jnp.float32)
            query_out[c, :, pl.ds(h * HEAD, HEAD)] = (first + second).astype(query_out.dtype)
        return carry

    lax.fori_loop(0, query_out.shape[0], body, 0)


def sum_parts(target, query_back):
    slot_total, heads, span_len, _ = query_back.shape
    width = heads * HEAD
    span_count = target.shape[0] // NBR
    grid_spec = pltpu.PrefetchScalarGridSpec(
        num_scalar_prefetch=1,
        grid=(1,),
        in_specs=[pl.BlockSpec(query_back.shape, lambda i, tgt: (0, 0, 0, 0))],
        out_specs=pl.BlockSpec((span_count, span_len, width), lambda i, tgt: (0, 0, 0)),
    )
    return pl.pallas_call(
        sum_kernel,
        grid_spec=grid_spec,
        out_shape=jax.ShapeDtypeStruct((span_count, span_len, width), query_back.dtype),
        compiler_params=pltpu.CompilerParams(vmem_limit_bytes=48 * 1024 * 1024),
    )(jnp.clip(target, 0, slot_total - 1), query_back)


def gather_over(block, axis_name, axis_count):
    me = lax.axis_index(axis_name)
    result = jnp.zeros((axis_count,) + block.shape, block.dtype)
    result = lax.dynamic_update_index_in_dim(result, block, me, axis=0)
    for shift in range(1, axis_count):
        sent = lax.ppermute(
            block, axis_name, perm=[(i, (i + shift) % axis_count) for i in range(axis_count)]
        )
        result = lax.dynamic_update_index_in_dim(result, sent, (me - shift) % axis_count, axis=0)
    return result


def seq_exchange(blocks, seq_count):
    me = lax.axis_index("seq")
    result = jnp.zeros_like(blocks)
    result = lax.dynamic_update_index_in_dim(
        result, lax.dynamic_index_in_dim(blocks, me, keepdims=False), me, axis=0
    )
    for shift in range(1, seq_count):
        sent = lax.ppermute(
            lax.dynamic_index_in_dim(blocks, (me + shift) % seq_count, keepdims=False),
            "seq",
            perm=[(i, (i + shift) % seq_count) for i in range(seq_count)],
        )
        result = lax.dynamic_update_index_in_dim(
            result, sent, (me - shift) % seq_count, axis=0
        )
    return result


def seq_move(tensor, seq_count, slot_depth):
    if seq_count > 8:
        return lax.all_to_all(tensor, "seq", split_axis=0, concat_axis=0, tiled=True)
    blocks = tensor.reshape((seq_count, slot_depth) + tensor.shape[1:])
    return seq_exchange(blocks, seq_count).reshape(tensor.shape)


def per_device(queries, out_grad, row_keys, row_values, neighbours):
    seq_count = lax.axis_size("seq")
    own_lists = gather_over(neighbours, "mp", lax.axis_size("mp")).reshape(
        (-1,) + neighbours.shape[1:]
    )
    span_count = queries.shape[0]
    rows_here = row_keys.shape[0]
    width_here = queries.shape[2]
    heads_here = width_here // HEAD
    flat_rows = own_lists.reshape(-1)
    item_count = flat_rows.shape[0]
    owner_dev = flat_rows // rows_here
    local_row = flat_rows % rows_here
    slot_depth = (item_count + seq_count - 1) // seq_count
    slot_total = seq_count * slot_depth
    position = jnp.arange(item_count)
    same_before = (owner_dev[:, None] == owner_dev[None, :]) & (
        position[None, :] < position[:, None]
    )
    earlier = jnp.sum(same_before.astype(jnp.int32), axis=1)
    target = owner_dev * slot_depth + earlier
    item_span = position // NBR
    score_scale = HEAD ** (-0.5)

    match = target[None, :] == jnp.arange(slot_total)[:, None]
    slot_valid = jnp.any(match, axis=1)
    slot_item = jnp.sum(jnp.where(match, position[None, :], 0), axis=1)
    slot_span = item_span[slot_item]

    pair_send = gather_pairs(slot_span, queries, out_grad)
    row_send = jnp.where(slot_valid, local_row[slot_item], -1)
    pair_recv = lax.all_to_all(pair_send, "seq", split_axis=0, concat_axis=0, tiled=True)
    row_recv = lax.all_to_all(row_send, "seq", split_axis=0, concat_axis=0, tiled=True)

    row_index = jnp.clip(row_recv, 0, rows_here - 1)
    query_heads = pair_recv[:, 0]
    grad_heads = pair_recv[:, 1]
    key_heads = jnp.swapaxes(split_heads(row_keys), 1, 2)[row_index]
    value_heads = jnp.swapaxes(split_heads(row_values), 1, 2)[row_index]

    scores = (
        jnp.einsum("bhid,bhjd->bhij", query_heads, key_heads, preferred_element_type=jnp.float32)
        * score_scale
    )
    grad_p = jnp.einsum(
        "bhid,bhjd->bhij", grad_heads, value_heads, preferred_element_type=jnp.float32
    )
    highest = jnp.max(scores, axis=3)
    expons = jnp.exp(scores - highest[..., None])
    part = jnp.stack(
        [highest, jnp.sum(expons, axis=3), jnp.sum(expons * grad_p, axis=3)], axis=1
    ).reshape(slot_total, 3, heads_here * SPAN)
    back = seq_move(part, seq_count, slot_depth)

    item_part = back[target].reshape(span_count, NBR, 3, heads_here * SPAN)
    item_max = item_part[:, :, 0]
    item_sum = item_part[:, :, 1]
    item_cross = item_part[:, :, 2]
    span_max = jnp.max(item_max, axis=1, keepdims=True)
    factor = jnp.exp(item_max - span_max)
    span_sum = jnp.sum(item_sum * factor, axis=1)
    log_total = span_max[:, 0] + jnp.log(span_sum)
    row_delta = jnp.sum(item_cross * factor, axis=1) / span_sum
    span_stats = jnp.stack([log_total, row_delta], axis=1)
    stats_recv = seq_move(span_stats[slot_span], seq_count, slot_depth)

    norm_here = stats_recv[:, 0].reshape(slot_total, heads_here, SPAN)
    delta_here = stats_recv[:, 1].reshape(slot_total, heads_here, SPAN)
    softmax_p = jnp.exp(scores - norm_here[..., None])
    grad_s = (softmax_p * (grad_p - delta_here[..., None]) * score_scale).astype(jnp.bfloat16)
    probs_low = softmax_p.astype(jnp.bfloat16)
    query_part = jnp.einsum(
        "bhij,bhjd->bhid", grad_s, key_heads, preferred_element_type=jnp.float32
    ).astype(jnp.bfloat16)
    if seq_count <= 8:
        query_back = seq_exchange(
            query_part.reshape((seq_count, slot_depth) + query_part.shape[1:]), seq_count
        ).reshape(query_part.shape)
    else:
        query_back = lax.all_to_all(query_part, "seq", split_axis=0, concat_axis=0, tiled=True)

    key_grad, value_grad = kv_grads(row_recv, probs_low, grad_s, pair_recv, rows_here)

    query_grad = sum_parts(target, query_back)
    return (query_grad, key_grad, value_grad)


def solution(mesh):
    in_specs = (
        P("seq", None, "mp"),
        P("seq", None, "mp"),
        P("seq", None, "mp"),
        P("seq", None, "mp"),
        P(("seq", "mp"), None),
    )
    out_specs = (P("seq", None, "mp"), P("seq", None, "mp"), P("seq", None, "mp"))
    return jax.shard_map(
        per_device, mesh=mesh, in_specs=in_specs, out_specs=out_specs, check_vma=False
    )
```

```python
import jax
import jax.numpy as jnp
from jax import lax
from jax.experimental import pallas as pl
from jax.experimental.pallas import tpu as pltpu
from jax.sharding import PartitionSpec as P

HEAD = 128
SPAN = 64
NLEN = 128
NBR = 2

TRANS_A = (((0,), (0,)), ((), ()))


def split_heads(tensor):
    return tensor.reshape(tensor.shape[:-1] + (tensor.shape[-1] // HEAD, HEAD))


def kv_kernel(rows_ref, probs_ref, grads_ref, pair_ref, key_out, value_out, key_acc, value_acc):
    slot = pl.program_id(0)
    heads = probs_ref.shape[1]

    @pl.when(slot == 0)
    def _():
        key_acc[...] = jnp.zeros_like(key_acc)
        value_acc[...] = jnp.zeros_like(value_acc)

    row = rows_ref[slot]

    @pl.when(row >= 0)
    def _():
        here = jnp.maximum(row, 0)
        for h in range(heads):
            cols = pl.ds(h * HEAD, HEAD)
            value_part = lax.dot_general(
                probs_ref[0, h], pair_ref[0, 1, h], TRANS_A,
                preferred_element_type=jnp.float32,
            )
            key_part = lax.dot_general(
                grads_ref[0, h], pair_ref[0, 0, h], TRANS_A,
                preferred_element_type=jnp.float32,
            )
            value_acc[here, :, cols] += value_part
            key_acc[here, :, cols] += key_part

    @pl.when(slot == pl.num_programs(0) - 1)
    def _():
        key_out[...] = key_acc[...].astype(key_out.dtype)
        value_out[...] = value_acc[...].astype(value_out.dtype)


def kv_grads(row_recv, probs_low, grad_s, pair_recv, rows_here):
    slot_total, heads, span_len, nlen = probs_low.shape
    width = heads * HEAD
    out_shape = jax.ShapeDtypeStruct((rows_here, nlen, width), jnp.bfloat16)
    grid_spec = pltpu.PrefetchScalarGridSpec(
        num_scalar_prefetch=1,
        grid=(slot_total,),
        in_specs=[
            pl.BlockSpec((1, heads, span_len, nlen), lambda t, rows: (t, 0, 0, 0)),
            pl.BlockSpec((1, heads, span_len, nlen), lambda t, rows: (t, 0, 0, 0)),
            pl.BlockSpec((1, 2, heads, span_len, HEAD), lambda t, rows: (t, 0, 0, 0, 0)),
        ],
        out_specs=[
            pl.BlockSpec((rows_here, nlen, width), lambda t, rows: (0, 0, 0)),
            pl.BlockSpec((rows_here, nlen, width), lambda t, rows: (0, 0, 0)),
        ],
        scratch_shapes=[
            pltpu.VMEM((rows_here, nlen, width), jnp.float32),
            pltpu.VMEM((rows_here, nlen, width), jnp.float32),
        ],
    )
    return pl.pallas_call(
        kv_kernel,
        grid_spec=grid_spec,
        out_shape=[out_shape, out_shape],
        compiler_params=pltpu.CompilerParams(
            dimension_semantics=("arbitrary",), vmem_limit_bytes=48 * 1024 * 1024
        ),
    )(row_recv, probs_low, grad_s, pair_recv)


def pair_kernel(span_ref, query_hbm, grad_hbm, pair_hbm, done):
    heads = pair_hbm.shape[2]

    def body(t, carry):
        source = span_ref[t]
        for h in range(heads):
            cols = pl.ds(h * HEAD, HEAD)
            pltpu.make_async_copy(query_hbm.at[source, :, cols], pair_hbm.at[t, 0, h], done).start()
            pltpu.make_async_copy(grad_hbm.at[source, :, cols], pair_hbm.at[t, 1, h], done).start()
        return carry

    lax.fori_loop(0, pair_hbm.shape[0], body, 0)
    pltpu.make_async_copy(pair_hbm, pair_hbm, done).wait()


def gather_pairs(slot_span, queries, out_grad):
    span_count, span_len, width = queries.shape
    slot_total = slot_span.shape[0]
    heads = width // HEAD
    pair_shape = (slot_total, 2, heads, span_len, HEAD)
    grid_spec = pltpu.PrefetchScalarGridSpec(
        num_scalar_prefetch=1,
        grid=(1,),
        in_specs=[pl.BlockSpec(memory_space=pl.ANY), pl.BlockSpec(memory_space=pl.ANY)],
        out_specs=pl.BlockSpec(memory_space=pl.ANY),
        scratch_shapes=[pltpu.SemaphoreType.DMA(())],
    )
    return pl.pallas_call(
        pair_kernel,
        grid_spec=grid_spec,
        out_shape=jax.ShapeDtypeStruct(pair_shape, queries.dtype),
    )(jnp.clip(slot_span, 0, span_count - 1), queries, out_grad)


def sum_kernel(target_ref, back_ref, query_out):
    heads = back_ref.shape[1]

    def body(c, carry):
        first_slot = target_ref[c * NBR]
        second_slot = target_ref[c * NBR + 1]
        for h in range(heads):
            first = back_ref[first_slot, h].astype(jnp.float32)
            second = back_ref[second_slot, h].astype(jnp.float32)
            query_out[c, :, pl.ds(h * HEAD, HEAD)] = (first + second).astype(query_out.dtype)
        return carry

    lax.fori_loop(0, query_out.shape[0], body, 0)


def sum_parts(target, query_back):
    slot_total, heads, span_len, _ = query_back.shape
    width = heads * HEAD
    span_count = target.shape[0] // NBR
    grid_spec = pltpu.PrefetchScalarGridSpec(
        num_scalar_prefetch=1,
        grid=(1,),
        in_specs=[pl.BlockSpec(query_back.shape, lambda i, tgt: (0, 0, 0, 0))],
        out_specs=pl.BlockSpec((span_count, span_len, width), lambda i, tgt: (0, 0, 0)),
    )
    return pl.pallas_call(
        sum_kernel,
        grid_spec=grid_spec,
        out_shape=jax.ShapeDtypeStruct((span_count, span_len, width), query_back.dtype),
        compiler_params=pltpu.CompilerParams(vmem_limit_bytes=48 * 1024 * 1024),
    )(jnp.clip(target, 0, slot_total - 1), query_back)


def gather_over(block, axis_name, axis_count):
    me = lax.axis_index(axis_name)
    result = jnp.zeros((axis_count,) + block.shape, block.dtype)
    result = lax.dynamic_update_index_in_dim(result, block, me, axis=0)
    for shift in range(1, axis_count):
        sent = lax.ppermute(
            block, axis_name, perm=[(i, (i + shift) % axis_count) for i in range(axis_count)]
        )
        result = lax.dynamic_update_index_in_dim(result, sent, (me - shift) % axis_count, axis=0)
    return result


def seq_exchange(blocks, seq_count):
    me = lax.axis_index("seq")
    result = jnp.zeros_like(blocks)
    result = lax.dynamic_update_index_in_dim(
        result, lax.dynamic_index_in_dim(blocks, me, keepdims=False), me, axis=0
    )
    for shift in range(1, seq_count):
        sent = lax.ppermute(
            lax.dynamic_index_in_dim(blocks, (me + shift) % seq_count, keepdims=False),
            "seq",
            perm=[(i, (i + shift) % seq_count) for i in range(seq_count)],
        )
        result = lax.dynamic_update_index_in_dim(
            result, sent, (me - shift) % seq_count, axis=0
        )
    return result


def per_device(queries, out_grad, row_keys, row_values, neighbours):
    seq_count = lax.axis_size("seq")
    own_lists = gather_over(neighbours, "mp", lax.axis_size("mp")).reshape(
        (-1,) + neighbours.shape[1:]
    )
    span_count = queries.shape[0]
    rows_here = row_keys.shape[0]
    width_here = queries.shape[2]
    heads_here = width_here // HEAD
    flat_rows = own_lists.reshape(-1)
    item_count = flat_rows.shape[0]
    owner_dev = flat_rows // rows_here
    local_row = flat_rows % rows_here
    slot_depth = (item_count + seq_count - 1) // seq_count
    slot_total = seq_count * slot_depth
    position = jnp.arange(item_count)
    same_before = (owner_dev[:, None] == owner_dev[None, :]) & (
        position[None, :] < position[:, None]
    )
    earlier = jnp.sum(same_before.astype(jnp.int32), axis=1)
    target = owner_dev * slot_depth + earlier
    item_span = position // NBR
    score_scale = HEAD ** (-0.5)

    match = target[None, :] == jnp.arange(slot_total)[:, None]
    slot_valid = jnp.any(match, axis=1)
    slot_item = jnp.sum(jnp.where(match, position[None, :], 0), axis=1)
    slot_span = item_span[slot_item]

    pair_send = gather_pairs(slot_span, queries, out_grad)
    row_send = jnp.where(slot_valid, local_row[slot_item], -1)
    pair_recv = lax.all_to_all(pair_send, "seq", split_axis=0, concat_axis=0, tiled=True)
    row_recv = lax.all_to_all(row_send, "seq", split_axis=0, concat_axis=0, tiled=True)

    row_index = jnp.clip(row_recv, 0, rows_here - 1)
    query_heads = pair_recv[:, 0]
    grad_heads = pair_recv[:, 1]
    key_heads = jnp.swapaxes(split_heads(row_keys), 1, 2)[row_index]
    value_heads = jnp.swapaxes(split_heads(row_values), 1, 2)[row_index]

    scores = (
        jnp.einsum("bhid,bhjd->bhij", query_heads, key_heads, preferred_element_type=jnp.float32)
        * score_scale
    )
    grad_p = jnp.einsum(
        "bhid,bhjd->bhij", grad_heads, value_heads, preferred_element_type=jnp.float32
    )
    highest = jnp.max(scores, axis=3)
    expons = jnp.exp(scores - highest[..., None])
    part = jnp.stack(
        [highest, jnp.sum(expons, axis=3), jnp.sum(expons * grad_p, axis=3)], axis=1
    ).reshape(slot_total, 3, heads_here * SPAN)
    back = lax.all_to_all(part, "seq", split_axis=0, concat_axis=0, tiled=True)

    item_part = back[target].reshape(span_count, NBR, 3, heads_here * SPAN)
    item_max = item_part[:, :, 0]
    item_sum = item_part[:, :, 1]
    item_cross = item_part[:, :, 2]
    span_max = jnp.max(item_max, axis=1, keepdims=True)
    factor = jnp.exp(item_max - span_max)
    span_sum = jnp.sum(item_sum * factor, axis=1)
    log_total = span_max[:, 0] + jnp.log(span_sum)
    row_delta = jnp.sum(item_cross * factor, axis=1) / span_sum
    span_stats = jnp.stack([log_total, row_delta], axis=1)
    stats_recv = lax.all_to_all(
        span_stats[slot_span], "seq", split_axis=0, concat_axis=0, tiled=True
    )

    norm_here = stats_recv[:, 0].reshape(slot_total, heads_here, SPAN)
    delta_here = stats_recv[:, 1].reshape(slot_total, heads_here, SPAN)
    softmax_p = jnp.exp(scores - norm_here[..., None])
    grad_s = (softmax_p * (grad_p - delta_here[..., None]) * score_scale).astype(jnp.bfloat16)
    probs_low = softmax_p.astype(jnp.bfloat16)
    query_part = jnp.einsum(
        "bhij,bhjd->bhid", grad_s, key_heads, preferred_element_type=jnp.float32
    ).astype(jnp.bfloat16)
    if seq_count <= 8:
        query_back = seq_exchange(
            query_part.reshape((seq_count, slot_depth) + query_part.shape[1:]), seq_count
        ).reshape(query_part.shape)
    else:
        query_back = lax.all_to_all(query_part, "seq", split_axis=0, concat_axis=0, tiled=True)

    key_grad, value_grad = kv_grads(row_recv, probs_low, grad_s, pair_recv, rows_here)

    query_grad = sum_parts(target, query_back)
    return (query_grad, key_grad, value_grad)


def solution(mesh):
    in_specs = (
        P("seq", None, "mp"),
        P("seq", None, "mp"),
        P("seq", None, "mp"),
        P("seq", None, "mp"),
        P(("seq", "mp"), None),
    )
    out_specs = (P("seq", None, "mp"), P("seq", None, "mp"), P("seq", None, "mp"))
    return jax.shard_map(
        per_device, mesh=mesh, in_specs=in_specs, out_specs=out_specs, check_vma=False
    )
```

```python
import jax
import jax.numpy as jnp
from jax import lax
from jax.experimental import pallas as pl
from jax.experimental.pallas import tpu as pltpu
from jax.sharding import PartitionSpec as P

HEAD = 128
SPAN = 64
NLEN = 128
NBR = 2

TRANS_A = (((0,), (0,)), ((), ()))


def split_heads(tensor):
    return tensor.reshape(tensor.shape[:-1] + (tensor.shape[-1] // HEAD, HEAD))


def kv_kernel(rows_ref, probs_ref, grads_ref, pair_ref, key_out, value_out, key_acc, value_acc):
    slot = pl.program_id(0)
    heads = probs_ref.shape[1]

    @pl.when(slot == 0)
    def _():
        key_acc[...] = jnp.zeros_like(key_acc)
        value_acc[...] = jnp.zeros_like(value_acc)

    row = rows_ref[slot]

    @pl.when(row >= 0)
    def _():
        here = jnp.maximum(row, 0)
        for h in range(heads):
            cols = pl.ds(h * HEAD, HEAD)
            value_part = lax.dot_general(
                probs_ref[0, h], pair_ref[0, 1, h], TRANS_A,
                preferred_element_type=jnp.float32,
            )
            key_part = lax.dot_general(
                grads_ref[0, h], pair_ref[0, 0, h], TRANS_A,
                preferred_element_type=jnp.float32,
            )
            value_acc[here, :, cols] += value_part
            key_acc[here, :, cols] += key_part

    @pl.when(slot == pl.num_programs(0) - 1)
    def _():
        key_out[...] = key_acc[...].astype(key_out.dtype)
        value_out[...] = value_acc[...].astype(value_out.dtype)


def kv_grads(row_recv, probs_low, grad_s, pair_recv, rows_here):
    slot_total, heads, span_len, nlen = probs_low.shape
    width = heads * HEAD
    out_shape = jax.ShapeDtypeStruct((rows_here, nlen, width), jnp.bfloat16)
    grid_spec = pltpu.PrefetchScalarGridSpec(
        num_scalar_prefetch=1,
        grid=(slot_total,),
        in_specs=[
            pl.BlockSpec((1, heads, span_len, nlen), lambda t, rows: (t, 0, 0, 0)),
            pl.BlockSpec((1, heads, span_len, nlen), lambda t, rows: (t, 0, 0, 0)),
            pl.BlockSpec((1, 2, heads, span_len, HEAD), lambda t, rows: (t, 0, 0, 0, 0)),
        ],
        out_specs=[
            pl.BlockSpec((rows_here, nlen, width), lambda t, rows: (0, 0, 0)),
            pl.BlockSpec((rows_here, nlen, width), lambda t, rows: (0, 0, 0)),
        ],
        scratch_shapes=[
            pltpu.VMEM((rows_here, nlen, width), jnp.float32),
            pltpu.VMEM((rows_here, nlen, width), jnp.float32),
        ],
    )
    return pl.pallas_call(
        kv_kernel,
        grid_spec=grid_spec,
        out_shape=[out_shape, out_shape],
        compiler_params=pltpu.CompilerParams(
            dimension_semantics=("arbitrary",), vmem_limit_bytes=48 * 1024 * 1024
        ),
    )(row_recv, probs_low, grad_s, pair_recv)


def pair_kernel(span_ref, query_ref, grad_ref, pair_out):
    heads = pair_out.shape[2]

    def body(t, carry):
        source = span_ref[t]
        for h in range(heads):
            cols = pl.ds(h * HEAD, HEAD)
            pair_out[t, 0, h] = query_ref[source, :, cols]
            pair_out[t, 1, h] = grad_ref[source, :, cols]
        return carry

    lax.fori_loop(0, pair_out.shape[0], body, 0)


def gather_pairs(slot_span, queries, out_grad):
    span_count, span_len, width = queries.shape
    slot_total = slot_span.shape[0]
    heads = width // HEAD
    pair_shape = (slot_total, 2, heads, span_len, HEAD)
    grid_spec = pltpu.PrefetchScalarGridSpec(
        num_scalar_prefetch=1,
        grid=(1,),
        in_specs=[
            pl.BlockSpec((span_count, span_len, width), lambda i, spans: (0, 0, 0)),
            pl.BlockSpec((span_count, span_len, width), lambda i, spans: (0, 0, 0)),
        ],
        out_specs=pl.BlockSpec(pair_shape, lambda i, spans: (0, 0, 0, 0, 0)),
    )
    return pl.pallas_call(
        pair_kernel,
        grid_spec=grid_spec,
        out_shape=jax.ShapeDtypeStruct(pair_shape, queries.dtype),
        compiler_params=pltpu.CompilerParams(vmem_limit_bytes=48 * 1024 * 1024),
    )(jnp.clip(slot_span, 0, span_count - 1), queries, out_grad)


def sum_kernel(target_ref, back_ref, query_out):
    heads = back_ref.shape[1]

    def body(c, carry):
        first_slot = target_ref[c * NBR]
        second_slot = target_ref[c * NBR + 1]
        for h in range(heads):
            first = back_ref[first_slot, h].astype(jnp.float32)
            second = back_ref[second_slot, h].astype(jnp.float32)
            query_out[c, :, pl.ds(h * HEAD, HEAD)] = (first + second).astype(query_out.dtype)
        return carry

    lax.fori_loop(0, query_out.shape[0], body, 0)


def sum_parts(target, query_back):
    slot_total, heads, span_len, _ = query_back.shape
    width = heads * HEAD
    span_count = target.shape[0] // NBR
    grid_spec = pltpu.PrefetchScalarGridSpec(
        num_scalar_prefetch=1,
        grid=(1,),
        in_specs=[pl.BlockSpec(query_back.shape, lambda i, tgt: (0, 0, 0, 0))],
        out_specs=pl.BlockSpec((span_count, span_len, width), lambda i, tgt: (0, 0, 0)),
    )
    return pl.pallas_call(
        sum_kernel,
        grid_spec=grid_spec,
        out_shape=jax.ShapeDtypeStruct((span_count, span_len, width), query_back.dtype),
        compiler_params=pltpu.CompilerParams(vmem_limit_bytes=48 * 1024 * 1024),
    )(jnp.clip(target, 0, slot_total - 1), query_back)


def gather_over(block, axis_name, axis_count):
    me = lax.axis_index(axis_name)
    result = jnp.zeros((axis_count,) + block.shape, block.dtype)
    result = lax.dynamic_update_index_in_dim(result, block, me, axis=0)
    for shift in range(1, axis_count):
        sent = lax.ppermute(
            block, axis_name, perm=[(i, (i + shift) % axis_count) for i in range(axis_count)]
        )
        result = lax.dynamic_update_index_in_dim(result, sent, (me - shift) % axis_count, axis=0)
    return result


def seq_exchange(blocks, seq_count):
    me = lax.axis_index("seq")
    result = jnp.zeros_like(blocks)
    result = lax.dynamic_update_index_in_dim(
        result, lax.dynamic_index_in_dim(blocks, me, keepdims=False), me, axis=0
    )
    for shift in range(1, seq_count):
        sent = lax.ppermute(
            lax.dynamic_index_in_dim(blocks, (me + shift) % seq_count, keepdims=False),
            "seq",
            perm=[(i, (i + shift) % seq_count) for i in range(seq_count)],
        )
        result = lax.dynamic_update_index_in_dim(
            result, sent, (me - shift) % seq_count, axis=0
        )
    return result


def per_device(queries, out_grad, row_keys, row_values, neighbours):
    seq_count = lax.axis_size("seq")
    own_lists = gather_over(neighbours, "mp", lax.axis_size("mp")).reshape(
        (-1,) + neighbours.shape[1:]
    )
    span_count = queries.shape[0]
    rows_here = row_keys.shape[0]
    width_here = queries.shape[2]
    heads_here = width_here // HEAD
    flat_rows = own_lists.reshape(-1)
    item_count = flat_rows.shape[0]
    owner_dev = flat_rows // rows_here
    local_row = flat_rows % rows_here
    slot_depth = (item_count + seq_count - 1) // seq_count
    slot_total = seq_count * slot_depth
    position = jnp.arange(item_count)
    same_before = (owner_dev[:, None] == owner_dev[None, :]) & (
        position[None, :] < position[:, None]
    )
    earlier = jnp.sum(same_before.astype(jnp.int32), axis=1)
    target = owner_dev * slot_depth + earlier
    item_span = position // NBR
    score_scale = HEAD ** (-0.5)

    match = target[None, :] == jnp.arange(slot_total)[:, None]
    slot_valid = jnp.any(match, axis=1)
    slot_item = jnp.sum(jnp.where(match, position[None, :], 0), axis=1)
    slot_span = item_span[slot_item]

    pair_send = gather_pairs(slot_span, queries, out_grad)
    row_send = jnp.where(slot_valid, local_row[slot_item], -1)
    pair_recv = lax.all_to_all(pair_send, "seq", split_axis=0, concat_axis=0, tiled=True)
    row_recv = lax.all_to_all(row_send, "seq", split_axis=0, concat_axis=0, tiled=True)

    row_index = jnp.clip(row_recv, 0, rows_here - 1)
    query_heads = pair_recv[:, 0]
    grad_heads = pair_recv[:, 1]
    key_heads = jnp.swapaxes(split_heads(row_keys), 1, 2)[row_index]
    value_heads = jnp.swapaxes(split_heads(row_values), 1, 2)[row_index]

    scores = (
        jnp.einsum("bhid,bhjd->bhij", query_heads, key_heads, preferred_element_type=jnp.float32)
        * score_scale
    )
    grad_p = jnp.einsum(
        "bhid,bhjd->bhij", grad_heads, value_heads, preferred_element_type=jnp.float32
    )
    highest = jnp.max(scores, axis=3)
    expons = jnp.exp(scores - highest[..., None])
    part = jnp.stack(
        [highest, jnp.sum(expons, axis=3), jnp.sum(expons * grad_p, axis=3)], axis=1
    ).reshape(slot_total, 3, heads_here * SPAN)
    back = lax.all_to_all(part, "seq", split_axis=0, concat_axis=0, tiled=True)

    item_part = back[target].reshape(span_count, NBR, 3, heads_here * SPAN)
    item_max = item_part[:, :, 0]
    item_sum = item_part[:, :, 1]
    item_cross = item_part[:, :, 2]
    span_max = jnp.max(item_max, axis=1, keepdims=True)
    factor = jnp.exp(item_max - span_max)
    span_sum = jnp.sum(item_sum * factor, axis=1)
    log_total = span_max[:, 0] + jnp.log(span_sum)
    row_delta = jnp.sum(item_cross * factor, axis=1) / span_sum
    span_stats = jnp.stack([log_total, row_delta], axis=1)
    stats_recv = lax.all_to_all(
        span_stats[slot_span], "seq", split_axis=0, concat_axis=0, tiled=True
    )

    norm_here = stats_recv[:, 0].reshape(slot_total, heads_here, SPAN)
    delta_here = stats_recv[:, 1].reshape(slot_total, heads_here, SPAN)
    softmax_p = jnp.exp(scores - norm_here[..., None])
    grad_s = (softmax_p * (grad_p - delta_here[..., None]) * score_scale).astype(jnp.bfloat16)
    query_part = jnp.einsum(
        "bhij,bhjd->bhid", grad_s, key_heads, preferred_element_type=jnp.float32
    ).astype(jnp.bfloat16)
    if seq_count <= 8:
        query_back = seq_exchange(
            query_part.reshape((seq_count, slot_depth) + query_part.shape[1:]), seq_count
        ).reshape(query_part.shape)
    else:
        query_back = lax.all_to_all(query_part, "seq", split_axis=0, concat_axis=0, tiled=True)

    held_scores, _ = lax.optimization_barrier((scores, query_part))
    probs_low = jnp.exp(held_scores - norm_here[..., None]).astype(jnp.bfloat16)
    key_grad, value_grad = kv_grads(row_recv, probs_low, grad_s, pair_recv, rows_here)

    query_grad = sum_parts(target, query_back)
    return (query_grad, key_grad, value_grad)


def solution(mesh):
    in_specs = (
        P("seq", None, "mp"),
        P("seq", None, "mp"),
        P("seq", None, "mp"),
        P("seq", None, "mp"),
        P(("seq", "mp"), None),
    )
    out_specs = (P("seq", None, "mp"), P("seq", None, "mp"), P("seq", None, "mp"))
    return jax.shard_map(
        per_device, mesh=mesh, in_specs=in_specs, out_specs=out_specs, check_vma=False
    )
```

```python
import jax
import jax.numpy as jnp
from jax import lax
from jax.experimental import pallas as pl
from jax.experimental.pallas import tpu as pltpu
from jax.sharding import PartitionSpec as P

HEAD = 128
SPAN = 64
NLEN = 128
NBR = 2

TRANS_A = (((0,), (0,)), ((), ()))


def split_heads(tensor):
    return tensor.reshape(tensor.shape[:-1] + (tensor.shape[-1] // HEAD, HEAD))


def kv_kernel(rows_ref, probs_ref, grads_ref, pair_ref, key_out, value_out, key_acc, value_acc):
    slot = pl.program_id(0)
    heads = probs_ref.shape[1]

    @pl.when(slot == 0)
    def _():
        key_acc[...] = jnp.zeros_like(key_acc)
        value_acc[...] = jnp.zeros_like(value_acc)

    row = rows_ref[slot]

    @pl.when(row >= 0)
    def _():
        here = jnp.maximum(row, 0)
        for h in range(heads):
            cols = pl.ds(h * HEAD, HEAD)
            value_part = lax.dot_general(
                probs_ref[0, h], pair_ref[0, 1, h], TRANS_A,
                preferred_element_type=jnp.float32,
            )
            key_part = lax.dot_general(
                grads_ref[0, h], pair_ref[0, 0, h], TRANS_A,
                preferred_element_type=jnp.float32,
            )
            value_acc[here, :, cols] += value_part
            key_acc[here, :, cols] += key_part

    @pl.when(slot == pl.num_programs(0) - 1)
    def _():
        key_out[...] = key_acc[...].astype(key_out.dtype)
        value_out[...] = value_acc[...].astype(value_out.dtype)


def kv_grads(row_recv, probs_low, grad_s, pair_recv, rows_here):
    slot_total, heads, span_len, nlen = probs_low.shape
    width = heads * HEAD
    out_shape = jax.ShapeDtypeStruct((rows_here, nlen, width), jnp.bfloat16)
    grid_spec = pltpu.PrefetchScalarGridSpec(
        num_scalar_prefetch=1,
        grid=(slot_total,),
        in_specs=[
            pl.BlockSpec((1, heads, span_len, nlen), lambda t, rows: (t, 0, 0, 0)),
            pl.BlockSpec((1, heads, span_len, nlen), lambda t, rows: (t, 0, 0, 0)),
            pl.BlockSpec((1, 2, heads, span_len, HEAD), lambda t, rows: (t, 0, 0, 0, 0)),
        ],
        out_specs=[
            pl.BlockSpec((rows_here, nlen, width), lambda t, rows: (0, 0, 0)),
            pl.BlockSpec((rows_here, nlen, width), lambda t, rows: (0, 0, 0)),
        ],
        scratch_shapes=[
            pltpu.VMEM((rows_here, nlen, width), jnp.float32),
            pltpu.VMEM((rows_here, nlen, width), jnp.float32),
        ],
    )
    return pl.pallas_call(
        kv_kernel,
        grid_spec=grid_spec,
        out_shape=[out_shape, out_shape],
        compiler_params=pltpu.CompilerParams(
            dimension_semantics=("arbitrary",), vmem_limit_bytes=48 * 1024 * 1024
        ),
    )(row_recv, probs_low, grad_s, pair_recv)


def pair_kernel(span_ref, query_ref, grad_ref, pair_out):
    heads = pair_out.shape[2]

    def body(t, carry):
        source = span_ref[t]
        for h in range(heads):
            cols = pl.ds(h * HEAD, HEAD)
            pair_out[t, 0, h] = query_ref[source, :, cols]
            pair_out[t, 1, h] = grad_ref[source, :, cols]
        return carry

    lax.fori_loop(0, pair_out.shape[0], body, 0)


def gather_pairs(slot_span, queries, out_grad):
    span_count, span_len, width = queries.shape
    slot_total = slot_span.shape[0]
    heads = width // HEAD
    pair_shape = (slot_total, 2, heads, span_len, HEAD)
    grid_spec = pltpu.PrefetchScalarGridSpec(
        num_scalar_prefetch=1,
        grid=(1,),
        in_specs=[
            pl.BlockSpec((span_count, span_len, width), lambda i, spans: (0, 0, 0)),
            pl.BlockSpec((span_count, span_len, width), lambda i, spans: (0, 0, 0)),
        ],
        out_specs=pl.BlockSpec(pair_shape, lambda i, spans: (0, 0, 0, 0, 0)),
    )
    return pl.pallas_call(
        pair_kernel,
        grid_spec=grid_spec,
        out_shape=jax.ShapeDtypeStruct(pair_shape, queries.dtype),
        compiler_params=pltpu.CompilerParams(vmem_limit_bytes=48 * 1024 * 1024),
    )(jnp.clip(slot_span, 0, span_count - 1), queries, out_grad)


def sum_kernel(target_ref, back_ref, query_out):
    heads = back_ref.shape[1]

    def body(c, carry):
        first_slot = target_ref[c * NBR]
        second_slot = target_ref[c * NBR + 1]
        for h in range(heads):
            first = back_ref[first_slot, h].astype(jnp.float32)
            second = back_ref[second_slot, h].astype(jnp.float32)
            query_out[c, :, pl.ds(h * HEAD, HEAD)] = (first + second).astype(query_out.dtype)
        return carry

    lax.fori_loop(0, query_out.shape[0], body, 0)


def sum_parts(target, query_back):
    slot_total, heads, span_len, _ = query_back.shape
    width = heads * HEAD
    span_count = target.shape[0] // NBR
    grid_spec = pltpu.PrefetchScalarGridSpec(
        num_scalar_prefetch=1,
        grid=(1,),
        in_specs=[pl.BlockSpec(query_back.shape, lambda i, tgt: (0, 0, 0, 0))],
        out_specs=pl.BlockSpec((span_count, span_len, width), lambda i, tgt: (0, 0, 0)),
    )
    return pl.pallas_call(
        sum_kernel,
        grid_spec=grid_spec,
        out_shape=jax.ShapeDtypeStruct((span_count, span_len, width), query_back.dtype),
        compiler_params=pltpu.CompilerParams(vmem_limit_bytes=48 * 1024 * 1024),
    )(jnp.clip(target, 0, slot_total - 1), query_back)


def gather_over(block, axis_name, axis_count):
    me = lax.axis_index(axis_name)
    result = jnp.zeros((axis_count,) + block.shape, block.dtype)
    result = lax.dynamic_update_index_in_dim(result, block, me, axis=0)
    for shift in range(1, axis_count):
        sent = lax.ppermute(
            block, axis_name, perm=[(i, (i + shift) % axis_count) for i in range(axis_count)]
        )
        result = lax.dynamic_update_index_in_dim(result, sent, (me - shift) % axis_count, axis=0)
    return result


def seq_exchange(blocks, seq_count):
    me = lax.axis_index("seq")
    result = jnp.zeros_like(blocks)
    result = lax.dynamic_update_index_in_dim(
        result, lax.dynamic_index_in_dim(blocks, me, keepdims=False), me, axis=0
    )
    for shift in range(1, seq_count):
        sent = lax.ppermute(
            lax.dynamic_index_in_dim(blocks, (me + shift) % seq_count, keepdims=False),
            "seq",
            perm=[(i, (i + shift) % seq_count) for i in range(seq_count)],
        )
        result = lax.dynamic_update_index_in_dim(
            result, sent, (me - shift) % seq_count, axis=0
        )
    return result


def per_device(queries, out_grad, row_keys, row_values, neighbours):
    seq_count = lax.axis_size("seq")
    own_lists = gather_over(neighbours, "mp", lax.axis_size("mp")).reshape(
        (-1,) + neighbours.shape[1:]
    )
    span_count = queries.shape[0]
    rows_here = row_keys.shape[0]
    width_here = queries.shape[2]
    heads_here = width_here // HEAD
    flat_rows = own_lists.reshape(-1)
    item_count = flat_rows.shape[0]
    owner_dev = flat_rows // rows_here
    local_row = flat_rows % rows_here
    slot_depth = (item_count + seq_count - 1) // seq_count
    slot_total = seq_count * slot_depth
    position = jnp.arange(item_count)
    same_before = (owner_dev[:, None] == owner_dev[None, :]) & (
        position[None, :] < position[:, None]
    )
    earlier = jnp.sum(same_before.astype(jnp.int32), axis=1)
    target = owner_dev * slot_depth + earlier
    item_span = position // NBR
    score_scale = HEAD ** (-0.5)

    match = target[None, :] == jnp.arange(slot_total)[:, None]
    slot_valid = jnp.any(match, axis=1)
    slot_item = jnp.sum(jnp.where(match, position[None, :], 0), axis=1)
    slot_span = item_span[slot_item]

    pair_send = gather_pairs(slot_span, queries, out_grad)
    row_send = jnp.where(slot_valid, local_row[slot_item], -1)
    pair_recv = lax.all_to_all(pair_send, "seq", split_axis=0, concat_axis=0, tiled=True)
    row_recv = lax.all_to_all(row_send, "seq", split_axis=0, concat_axis=0, tiled=True)

    row_index = jnp.clip(row_recv, 0, rows_here - 1)
    query_heads = pair_recv[:, 0]
    grad_heads = pair_recv[:, 1]
    key_heads = jnp.swapaxes(split_heads(row_keys), 1, 2)[row_index]
    value_heads = jnp.swapaxes(split_heads(row_values), 1, 2)[row_index]

    scores = (
        jnp.einsum("bhid,bhjd->bhij", query_heads, key_heads, preferred_element_type=jnp.float32)
        * score_scale
    )
    grad_p = jnp.einsum(
        "bhid,bhjd->bhij", grad_heads, value_heads, preferred_element_type=jnp.float32
    )
    highest = jnp.max(scores, axis=3)
    expons = jnp.exp(scores - highest[..., None])
    part = jnp.stack(
        [highest, jnp.sum(expons, axis=3), jnp.sum(expons * grad_p, axis=3)], axis=1
    ).reshape(slot_total, 3, heads_here * SPAN)
    back = lax.all_to_all(part, "seq", split_axis=0, concat_axis=0, tiled=True)
    query_heads, grad_heads, key_heads, value_heads, _ = lax.optimization_barrier(
        (query_heads, grad_heads, key_heads, value_heads, part)
    )
    scores = (
        jnp.einsum("bhid,bhjd->bhij", query_heads, key_heads, preferred_element_type=jnp.float32)
        * score_scale
    )
    grad_p = jnp.einsum(
        "bhid,bhjd->bhij", grad_heads, value_heads, preferred_element_type=jnp.float32
    )

    item_part = back[target].reshape(span_count, NBR, 3, heads_here * SPAN)
    item_max = item_part[:, :, 0]
    item_sum = item_part[:, :, 1]
    item_cross = item_part[:, :, 2]
    span_max = jnp.max(item_max, axis=1, keepdims=True)
    factor = jnp.exp(item_max - span_max)
    span_sum = jnp.sum(item_sum * factor, axis=1)
    log_total = span_max[:, 0] + jnp.log(span_sum)
    row_delta = jnp.sum(item_cross * factor, axis=1) / span_sum
    span_stats = jnp.stack([log_total, row_delta], axis=1)
    stats_recv = lax.all_to_all(
        span_stats[slot_span], "seq", split_axis=0, concat_axis=0, tiled=True
    )

    norm_here = stats_recv[:, 0].reshape(slot_total, heads_here, SPAN)
    delta_here = stats_recv[:, 1].reshape(slot_total, heads_here, SPAN)
    softmax_p = jnp.exp(scores - norm_here[..., None])
    grad_s = (softmax_p * (grad_p - delta_here[..., None]) * score_scale).astype(jnp.bfloat16)
    query_part = jnp.einsum(
        "bhij,bhjd->bhid", grad_s, key_heads, preferred_element_type=jnp.float32
    ).astype(jnp.bfloat16)
    if seq_count <= 8:
        query_back = seq_exchange(
            query_part.reshape((seq_count, slot_depth) + query_part.shape[1:]), seq_count
        ).reshape(query_part.shape)
    else:
        query_back = lax.all_to_all(query_part, "seq", split_axis=0, concat_axis=0, tiled=True)

    held_scores, _ = lax.optimization_barrier((scores, query_part))
    probs_low = jnp.exp(held_scores - norm_here[..., None]).astype(jnp.bfloat16)
    key_grad, value_grad = kv_grads(row_recv, probs_low, grad_s, pair_recv, rows_here)

    query_grad = sum_parts(target, query_back)
    return (query_grad, key_grad, value_grad)


def solution(mesh):
    in_specs = (
        P("seq", None, "mp"),
        P("seq", None, "mp"),
        P("seq", None, "mp"),
        P("seq", None, "mp"),
        P(("seq", "mp"), None),
    )
    out_specs = (P("seq", None, "mp"), P("seq", None, "mp"), P("seq", None, "mp"))
    return jax.shard_map(
        per_device, mesh=mesh, in_specs=in_specs, out_specs=out_specs, check_vma=False
    )
```

```python
import jax
import jax.numpy as jnp
from jax import lax
from jax.experimental import pallas as pl
from jax.experimental.pallas import tpu as pltpu
from jax.sharding import PartitionSpec as P

HEAD = 128
SPAN = 64
NLEN = 128
NBR = 2

TRANS_A = (((0,), (0,)), ((), ()))


def split_heads(tensor):
    return tensor.reshape(tensor.shape[:-1] + (tensor.shape[-1] // HEAD, HEAD))


def kv_kernel(rows_ref, probs_ref, grads_ref, pair_ref, key_out, value_out, key_acc, value_acc):
    slot = pl.program_id(0)
    heads = probs_ref.shape[1]

    @pl.when(slot == 0)
    def _():
        key_acc[...] = jnp.zeros_like(key_acc)
        value_acc[...] = jnp.zeros_like(value_acc)

    row = rows_ref[slot]

    @pl.when(row >= 0)
    def _():
        here = jnp.maximum(row, 0)
        for h in range(heads):
            cols = pl.ds(h * HEAD, HEAD)
            value_part = lax.dot_general(
                probs_ref[0, h], pair_ref[0, 1, h], TRANS_A,
                preferred_element_type=jnp.float32,
            )
            key_part = lax.dot_general(
                grads_ref[0, h], pair_ref[0, 0, h], TRANS_A,
                preferred_element_type=jnp.float32,
            )
            value_acc[here, :, cols] += value_part
            key_acc[here, :, cols] += key_part

    @pl.when(slot == pl.num_programs(0) - 1)
    def _():
        key_out[...] = key_acc[...].astype(key_out.dtype)
        value_out[...] = value_acc[...].astype(value_out.dtype)


def kv_grads(row_recv, probs_low, grad_s, pair_recv, rows_here):
    slot_total, heads, span_len, nlen = probs_low.shape
    width = heads * HEAD
    out_shape = jax.ShapeDtypeStruct((rows_here, nlen, width), jnp.bfloat16)
    grid_spec = pltpu.PrefetchScalarGridSpec(
        num_scalar_prefetch=1,
        grid=(slot_total,),
        in_specs=[
            pl.BlockSpec((1, heads, span_len, nlen), lambda t, rows: (t, 0, 0, 0)),
            pl.BlockSpec((1, heads, span_len, nlen), lambda t, rows: (t, 0, 0, 0)),
            pl.BlockSpec((1, 2, heads, span_len, HEAD), lambda t, rows: (t, 0, 0, 0, 0)),
        ],
        out_specs=[
            pl.BlockSpec((rows_here, nlen, width), lambda t, rows: (0, 0, 0)),
            pl.BlockSpec((rows_here, nlen, width), lambda t, rows: (0, 0, 0)),
        ],
        scratch_shapes=[
            pltpu.VMEM((rows_here, nlen, width), jnp.float32),
            pltpu.VMEM((rows_here, nlen, width), jnp.float32),
        ],
    )
    return pl.pallas_call(
        kv_kernel,
        grid_spec=grid_spec,
        out_shape=[out_shape, out_shape],
        compiler_params=pltpu.CompilerParams(
            dimension_semantics=("arbitrary",), vmem_limit_bytes=48 * 1024 * 1024
        ),
    )(row_recv, probs_low, grad_s, pair_recv)


def pair_kernel(span_ref, query_ref, grad_ref, pair_out):
    heads = pair_out.shape[2]

    def body(t, carry):
        source = span_ref[t]
        for h in range(heads):
            cols = pl.ds(h * HEAD, HEAD)
            pair_out[t, 0, h] = query_ref[source, :, cols]
            pair_out[t, 1, h] = grad_ref[source, :, cols]
        return carry

    lax.fori_loop(0, pair_out.shape[0], body, 0)


def gather_pairs(slot_span, queries, out_grad):
    span_count, span_len, width = queries.shape
    slot_total = slot_span.shape[0]
    heads = width // HEAD
    pair_shape = (slot_total, 2, heads, span_len, HEAD)
    grid_spec = pltpu.PrefetchScalarGridSpec(
        num_scalar_prefetch=1,
        grid=(1,),
        in_specs=[
            pl.BlockSpec((span_count, span_len, width), lambda i, spans: (0, 0, 0)),
            pl.BlockSpec((span_count, span_len, width), lambda i, spans: (0, 0, 0)),
        ],
        out_specs=pl.BlockSpec(pair_shape, lambda i, spans: (0, 0, 0, 0, 0)),
    )
    return pl.pallas_call(
        pair_kernel,
        grid_spec=grid_spec,
        out_shape=jax.ShapeDtypeStruct(pair_shape, queries.dtype),
        compiler_params=pltpu.CompilerParams(vmem_limit_bytes=48 * 1024 * 1024),
    )(jnp.clip(slot_span, 0, span_count - 1), queries, out_grad)


def sum_kernel(target_ref, back_ref, query_out):
    heads = back_ref.shape[1]

    def body(c, carry):
        first_slot = target_ref[c * NBR]
        second_slot = target_ref[c * NBR + 1]
        for h in range(heads):
            first = back_ref[first_slot, h].astype(jnp.float32)
            second = back_ref[second_slot, h].astype(jnp.float32)
            query_out[c, :, pl.ds(h * HEAD, HEAD)] = (first + second).astype(query_out.dtype)
        return carry

    lax.fori_loop(0, query_out.shape[0], body, 0)


def sum_parts(target, query_back):
    slot_total, heads, span_len, _ = query_back.shape
    width = heads * HEAD
    span_count = target.shape[0] // NBR
    grid_spec = pltpu.PrefetchScalarGridSpec(
        num_scalar_prefetch=1,
        grid=(1,),
        in_specs=[pl.BlockSpec(query_back.shape, lambda i, tgt: (0, 0, 0, 0))],
        out_specs=pl.BlockSpec((span_count, span_len, width), lambda i, tgt: (0, 0, 0)),
    )
    return pl.pallas_call(
        sum_kernel,
        grid_spec=grid_spec,
        out_shape=jax.ShapeDtypeStruct((span_count, span_len, width), query_back.dtype),
        compiler_params=pltpu.CompilerParams(vmem_limit_bytes=48 * 1024 * 1024),
    )(jnp.clip(target, 0, slot_total - 1), query_back)


def gather_over(block, axis_name, axis_count):
    me = lax.axis_index(axis_name)
    result = jnp.zeros((axis_count,) + block.shape, block.dtype)
    result = lax.dynamic_update_index_in_dim(result, block, me, axis=0)
    for shift in range(1, axis_count):
        sent = lax.ppermute(
            block, axis_name, perm=[(i, (i + shift) % axis_count) for i in range(axis_count)]
        )
        result = lax.dynamic_update_index_in_dim(result, sent, (me - shift) % axis_count, axis=0)
    return result


def seq_exchange(blocks, seq_count):
    me = lax.axis_index("seq")
    result = jnp.zeros_like(blocks)
    result = lax.dynamic_update_index_in_dim(
        result, lax.dynamic_index_in_dim(blocks, me, keepdims=False), me, axis=0
    )
    for shift in range(1, seq_count):
        sent = lax.ppermute(
            lax.dynamic_index_in_dim(blocks, (me + shift) % seq_count, keepdims=False),
            "seq",
            perm=[(i, (i + shift) % seq_count) for i in range(seq_count)],
        )
        result = lax.dynamic_update_index_in_dim(
            result, sent, (me - shift) % seq_count, axis=0
        )
    return result


def per_device(queries, out_grad, row_keys, row_values, neighbours):
    seq_count = lax.axis_size("seq")
    own_lists = gather_over(neighbours, "mp", lax.axis_size("mp")).reshape(
        (-1,) + neighbours.shape[1:]
    )
    span_count = queries.shape[0]
    rows_here = row_keys.shape[0]
    width_here = queries.shape[2]
    heads_here = width_here // HEAD
    flat_rows = own_lists.reshape(-1)
    item_count = flat_rows.shape[0]
    owner_dev = flat_rows // rows_here
    local_row = flat_rows % rows_here
    slot_depth = (item_count + seq_count - 1) // seq_count
    slot_total = seq_count * slot_depth
    position = jnp.arange(item_count)
    same_before = (owner_dev[:, None] == owner_dev[None, :]) & (
        position[None, :] < position[:, None]
    )
    earlier = jnp.sum(same_before.astype(jnp.int32), axis=1)
    target = owner_dev * slot_depth + earlier
    item_span = position // NBR
    score_scale = HEAD ** (-0.5)

    match = target[None, :] == jnp.arange(slot_total)[:, None]
    slot_valid = jnp.any(match, axis=1)
    slot_item = jnp.sum(jnp.where(match, position[None, :], 0), axis=1)
    slot_span = item_span[slot_item]

    pair_send = gather_pairs(slot_span, queries, out_grad)
    row_send = jnp.where(slot_valid, local_row[slot_item], -1)
    if seq_count <= 8:
        pair_recv = seq_exchange(
            pair_send.reshape((seq_count, slot_depth) + pair_send.shape[1:]), seq_count
        ).reshape(pair_send.shape)
    else:
        pair_recv = lax.all_to_all(pair_send, "seq", split_axis=0, concat_axis=0, tiled=True)
    row_recv = lax.all_to_all(row_send, "seq", split_axis=0, concat_axis=0, tiled=True)

    row_index = jnp.clip(row_recv, 0, rows_here - 1)
    query_heads = pair_recv[:, 0]
    grad_heads = pair_recv[:, 1]
    key_heads = jnp.swapaxes(split_heads(row_keys), 1, 2)[row_index]
    value_heads = jnp.swapaxes(split_heads(row_values), 1, 2)[row_index]

    scores = (
        jnp.einsum("bhid,bhjd->bhij", query_heads, key_heads, preferred_element_type=jnp.float32)
        * score_scale
    )
    grad_p = jnp.einsum(
        "bhid,bhjd->bhij", grad_heads, value_heads, preferred_element_type=jnp.float32
    )
    highest = jnp.max(scores, axis=3)
    expons = jnp.exp(scores - highest[..., None])
    part = jnp.stack(
        [highest, jnp.sum(expons, axis=3), jnp.sum(expons * grad_p, axis=3)], axis=1
    ).reshape(slot_total, 3, heads_here * SPAN)
    back = lax.all_to_all(part, "seq", split_axis=0, concat_axis=0, tiled=True)

    item_part = back[target].reshape(span_count, NBR, 3, heads_here * SPAN)
    item_max = item_part[:, :, 0]
    item_sum = item_part[:, :, 1]
    item_cross = item_part[:, :, 2]
    span_max = jnp.max(item_max, axis=1, keepdims=True)
    factor = jnp.exp(item_max - span_max)
    span_sum = jnp.sum(item_sum * factor, axis=1)
    log_total = span_max[:, 0] + jnp.log(span_sum)
    row_delta = jnp.sum(item_cross * factor, axis=1) / span_sum
    span_stats = jnp.stack([log_total, row_delta], axis=1)
    stats_recv = lax.all_to_all(
        span_stats[slot_span], "seq", split_axis=0, concat_axis=0, tiled=True
    )

    norm_here = stats_recv[:, 0].reshape(slot_total, heads_here, SPAN)
    delta_here = stats_recv[:, 1].reshape(slot_total, heads_here, SPAN)
    softmax_p = jnp.exp(scores - norm_here[..., None])
    grad_s = (softmax_p * (grad_p - delta_here[..., None]) * score_scale).astype(jnp.bfloat16)
    query_part = jnp.einsum(
        "bhij,bhjd->bhid", grad_s, key_heads, preferred_element_type=jnp.float32
    ).astype(jnp.bfloat16)
    if seq_count <= 8:
        query_back = seq_exchange(
            query_part.reshape((seq_count, slot_depth) + query_part.shape[1:]), seq_count
        ).reshape(query_part.shape)
    else:
        query_back = lax.all_to_all(query_part, "seq", split_axis=0, concat_axis=0, tiled=True)

    held_scores, _ = lax.optimization_barrier((scores, query_part))
    probs_low = jnp.exp(held_scores - norm_here[..., None]).astype(jnp.bfloat16)
    key_grad, value_grad = kv_grads(row_recv, probs_low, grad_s, pair_recv, rows_here)

    query_grad = sum_parts(target, query_back)
    return (query_grad, key_grad, value_grad)


def solution(mesh):
    in_specs = (
        P("seq", None, "mp"),
        P("seq", None, "mp"),
        P("seq", None, "mp"),
        P("seq", None, "mp"),
        P(("seq", "mp"), None),
    )
    out_specs = (P("seq", None, "mp"), P("seq", None, "mp"), P("seq", None, "mp"))
    return jax.shard_map(
        per_device, mesh=mesh, in_specs=in_specs, out_specs=out_specs, check_vma=False
    )
```
